32 devices in a mesh: days: 2 (over y), chan: 4 (over z), win: 4 (over x, core).
Axes of the slice: x: 2, y: 2, z: 4, core: 2. Of those that a mesh axis runs over, the one named last changes fastest.
Arguments:
- spectra: bfloat16 [2560, 32, 1024], P(('days', 'chan'), 'win'), parts along dimension 0, may hold values from -17 to 17
- pair_anchor: int32 [2048], P('chan'), may hold values from 0 to 319
- pair_offset: int32 [2048], P('chan'), may hold values from 0 to 2
- pair_partner: int32 [2048], P('chan'), may hold values from 0 to 319
- pair_count: int32 [4], P('chan'), may hold values from 1 to 512, as said below
- window_bins: int32 [64], P(('days', 'win')), parts along dimension 0, may hold values from 0 to 7
- bin_gain: float32 [8], replicated, may hold values from 0.2 to 5
Outputs:
- ref_stack: float32 [4096, 128], P(('days', 'chan')), parts along dimension 0
- restack: float32 [4096, 128], P(('days', 'chan')), parts along dimension 0
The draws below stay inside these ranges and needn't reach their ends.
There are 2 independent parts, one for each index of `days`. The reference program is written for one: setup_inputs(seed, part) draws one part's arguments, and reference() takes and returns one part's arrays. A program takes and returns all parts, laid end to end along the dimension named above; an argument that names none is the same for every part. Nothing has to cross between parts.
Inputs may be any that keep to these rules, and one draw needn't show every extreme that they name: `pair_count`: each block holds from 1 to 512 live pair slots, the first ones of its slots; some block holds 512 in every draw.
All inputs are finite; a program needn't handle non-finite values.
Results may differ from the reference program's by a relative error of at most 0.0062.
Values may be sent and summed in bfloat16 or wider, within the bound.
No kernel may reach another device: no remote copies, remote signals or barrier semaphores. Data moves between devices by JAX's collectives and lax.ppermute only.
A program may use at most 128 MiB of HBM per device.

```python
import math
import jax
import jax.numpy as jnp
from jax import lax

C = 320
P_SIZE = 512
F = 512
LAG = 128
NBIN = 8
BLOCKS = 4
NCH = 1280
NWIN = 32
NPAIRS = 2048


def draw_spectra(key, part):
    key_base, key_level = jax.random.split(key, 2)
    base_draw = jnp.clip(jax.random.normal(key_base, (NCH, NWIN, 2 * F), jnp.float32), -5.0, 5.0)
    log_spread = 1.2
    row_level = jnp.exp(jax.random.uniform(key_level, (NCH, NWIN, 1), jnp.float32, -log_spread, log_spread))
    return (base_draw * row_level).astype(jnp.bfloat16)


def draw_pair_count(key, part):
    key_first, key_second, key_busy = jax.random.split(key, 3)
    first_draw = jax.random.randint(key_first, (BLOCKS,), 0, P_SIZE + 1)
    second_draw = jax.random.randint(key_second, (BLOCKS,), 0, P_SIZE + 1)
    block_counts = jnp.maximum(first_draw * second_draw // P_SIZE, 1)
    busiest = jax.random.randint(key_busy, (), 0, BLOCKS)
    return jnp.where(jnp.arange(BLOCKS) == busiest, P_SIZE, block_counts).astype(jnp.int32)


def touch_ends(values, rng, smallest, largest):
    longest = values.shape.index(max(values.shape))
    spots = []
    for shift in (0, 1):
        where = [jax.random.randint(jax.random.fold_in(rng, axis), (), 0, length) for axis, length in enumerate(values.shape)]
        where[longest] = (where[longest] + shift) % values.shape[longest]
        spots.append(tuple(where))
    return values.at[spots[0]].set(smallest).at[spots[1]].set(largest)


def setup_inputs(seed: int = 0, part: int = 0) -> dict:
    arg_keys = jax.random.split(jax.random.key(seed), 8)
    part_keys = jax.random.split(jax.random.fold_in(arg_keys[7], part), 8)
    spectra = draw_spectra(jax.random.fold_in(jax.random.fold_in(arg_keys[7], part), 71), part)
    pair_anchor = touch_ends(jax.random.randint(arg_keys[1], (NPAIRS,), 0, C), jax.random.fold_in(arg_keys[1], 1), 0, C - 1).astype(jnp.int32)
    pair_offset = touch_ends(jax.random.randint(arg_keys[2], (NPAIRS,), 0, 3), jax.random.fold_in(arg_keys[2], 1), 0, 2).astype(jnp.int32)
    pair_partner = touch_ends(jax.random.randint(arg_keys[3], (NPAIRS,), 0, C), jax.random.fold_in(arg_keys[3], 1), 0, C - 1).astype(jnp.int32)
    pair_count = draw_pair_count(jax.random.fold_in(arg_keys[7], 71), part)
    window_bins = touch_ends(jax.random.randint(part_keys[5], (NWIN,), 0, NBIN), jax.random.fold_in(part_keys[5], 1), 0, NBIN - 1).astype(jnp.int32)
    bin_gain = jnp.clip(jnp.exp(jax.random.uniform(arg_keys[6], (NBIN,), jnp.float32, math.log(0.2), math.log(5.0))), 0.2, 5.0)
    return dict(spectra=spectra, pair_anchor=pair_anchor, pair_offset=pair_offset, pair_partner=pair_partner, pair_count=pair_count, window_bins=window_bins, bin_gain=bin_gain)


EPS_POWER = 1e-05
EPS_LAG = 1e-06

def whiten(spectra):
    spectra_f = spectra.astype(jnp.float32)
    power_mean = lax.optimization_barrier(jnp.mean(spectra_f * spectra_f, axis=-1, keepdims=True))
    return (spectra_f * lax.rsqrt(power_mean + EPS_POWER)).astype(jnp.bfloat16)

def lag_table(freq_count, lag_count):
    freq_ids = lax.broadcasted_iota(jnp.float32, (freq_count, lag_count), 0)
    lag_ids = lax.broadcasted_iota(jnp.float32, (freq_count, lag_count), 1) - lag_count // 2
    angles = 2.0 * jnp.pi / (2 * freq_count) * freq_ids * lag_ids
    norm_scale = 1.0 / jnp.sqrt(jnp.float32(freq_count))
    return jnp.concatenate([jnp.cos(angles) * norm_scale, -jnp.sin(angles) * norm_scale], axis=0).astype(jnp.bfloat16)

def cross_spectra(anchors, partners):
    half_width = anchors.shape[-1] // 2
    anchor_f = anchors.astype(jnp.float32)
    partner_f = partners.astype(jnp.float32)
    anchor_re = anchor_f[..., :half_width]
    anchor_im = anchor_f[..., half_width:]
    partner_re = partner_f[..., :half_width]
    partner_im = partner_f[..., half_width:]
    cross_re = anchor_re * partner_re + anchor_im * partner_im
    cross_im = anchor_im * partner_re - anchor_re * partner_im
    return jnp.concatenate([cross_re, cross_im], axis=-1).astype(jnp.bfloat16)

def window_gains(bins, gains):
    levels = lax.broadcasted_iota(jnp.int32, (bins.shape[0], gains.shape[0]), 1)
    return lax.optimization_barrier(jnp.sum(jnp.where(bins[:, None] == levels, gains[None, :], jnp.float32(0.0)), axis=1))

def window_weights(lag_corr, ref_sum, window_gain):
    corr_f = lag_corr.astype(jnp.float32)
    inner_prod = lax.optimization_barrier(jnp.mean(corr_f * ref_sum[:, None, :], axis=-1))
    corr_rms = jnp.sqrt(lax.optimization_barrier(jnp.mean(corr_f * corr_f, axis=-1)) + EPS_LAG)
    ref_rms = jnp.sqrt(lax.optimization_barrier(jnp.mean(ref_sum * ref_sum, axis=-1)) + EPS_LAG)
    coherence = inner_prod / (corr_rms * ref_rms[:, None])
    weights = window_gain[None, :] * jnp.exp(2.0 * coherence)
    numerator = lax.optimization_barrier(jnp.sum(weights[:, :, None] * corr_f, axis=1))
    denominator = lax.optimization_barrier(jnp.sum(weights, axis=1))
    return (numerator, denominator)

def reference(spectra, pair_anchor, pair_offset, pair_partner, pair_count, window_bins, bin_gain):
    white = whiten(spectra)
    transform = lag_table(F, LAG).astype(jnp.float32)
    window_gain = window_gains(window_bins, bin_gain)
    norm_scale = jnp.sqrt(jnp.float32(NWIN))

    def per_block(block_id):
        first_slot = (block_id * P_SIZE).astype(jnp.int32)
        anchor_rows = lax.dynamic_slice_in_dim(pair_anchor, first_slot, P_SIZE) + block_id * C
        offsets = lax.dynamic_slice_in_dim(pair_offset, first_slot, P_SIZE)
        partner_chan = lax.dynamic_slice_in_dim(pair_partner, first_slot, P_SIZE)
        partner_rows = (block_id + offsets - 1) % BLOCKS * C + partner_chan
        cross_spec = cross_spectra(jnp.take(white, anchor_rows, axis=0), jnp.take(white, partner_rows, axis=0))
        corr_full = jnp.dot(cross_spec.reshape(P_SIZE * NWIN, 2 * F).astype(jnp.float32), transform, precision=lax.Precision.HIGHEST).reshape(P_SIZE, NWIN, LAG)
        ref_sum = lax.optimization_barrier(jnp.sum(corr_full, axis=1))
        lag_corr = corr_full.astype(jnp.bfloat16)
        slot_ids = jnp.arange(P_SIZE, dtype=jnp.int32)
        live_mask = (slot_ids < pair_count[block_id]).astype(jnp.float32)
        numerator, denominator = window_weights(lag_corr, ref_sum, window_gain)
        ref_out = ref_sum * live_mask[:, None] / norm_scale
        restack_out = norm_scale * numerator / denominator[:, None] * live_mask[:, None]
        return (ref_out, restack_out)
    ref_all, restack_all = lax.map(per_block, jnp.arange(BLOCKS, dtype=jnp.int32))
    return (ref_all.reshape(NPAIRS, LAG), restack_all.reshape(NPAIRS, LAG))
```

```python
import jax
import jax.numpy as jnp
from jax import lax
from jax.sharding import PartitionSpec as P

LAG = 128


EPS_POWER = 1e-05
EPS_LAG = 1e-06


def ring_neighbours(shard, axis):
    peers = lax.axis_size(axis)
    up = [(i, (i + 1) % peers) for i in range(peers)]
    down = [(j, i) for i, j in up]
    before = lax.ppermute(shard, axis, up)
    after = lax.ppermute(shard, axis, down)
    return before, after


def whiten(spectra):
    spectra_f = spectra.astype(jnp.float32)
    power_mean = jnp.mean(spectra_f * spectra_f, axis=-1, keepdims=True)
    return (spectra_f * lax.rsqrt(power_mean + EPS_POWER)).astype(jnp.bfloat16)


def lag_table(freq_count, lag_count):
    freq_ids = lax.broadcasted_iota(jnp.float32, (freq_count, lag_count), 0)
    lag_ids = lax.broadcasted_iota(jnp.float32, (freq_count, lag_count), 1) - lag_count // 2
    angles = 2.0 * jnp.pi / (2 * freq_count) * freq_ids * lag_ids
    norm_scale = 1.0 / jnp.sqrt(jnp.float32(freq_count))
    return jnp.concatenate(
        [jnp.cos(angles) * norm_scale, -jnp.sin(angles) * norm_scale], axis=0
    ).astype(jnp.bfloat16)


def cross_spectra(anchors, partners):
    half_width = anchors.shape[-1] // 2
    anchor_f = anchors.astype(jnp.float32)
    partner_f = partners.astype(jnp.float32)
    anchor_re = anchor_f[..., :half_width]
    anchor_im = anchor_f[..., half_width:]
    partner_re = partner_f[..., :half_width]
    partner_im = partner_f[..., half_width:]
    cross_re = anchor_re * partner_re + anchor_im * partner_im
    cross_im = anchor_im * partner_re - anchor_re * partner_im
    return jnp.concatenate([cross_re, cross_im], axis=-1).astype(jnp.bfloat16)


def window_gains(bins, gains):
    levels = lax.broadcasted_iota(jnp.int32, (bins.shape[0], gains.shape[0]), 1)
    return jnp.sum(jnp.where(bins[:, None] == levels, gains[None, :], jnp.float32(0.0)), axis=1)


def window_weights(lag_corr, ref_sum, window_gain):
    corr_f = lag_corr.astype(jnp.float32)
    inner_prod = jnp.mean(corr_f * ref_sum[:, None, :], axis=-1)
    corr_rms = jnp.sqrt(jnp.mean(corr_f * corr_f, axis=-1) + EPS_LAG)
    ref_rms = jnp.sqrt(jnp.mean(ref_sum * ref_sum, axis=-1) + EPS_LAG)
    coherence = inner_prod / (corr_rms * ref_rms[:, None])
    weights = window_gain[None, :] * jnp.exp(2.0 * coherence)
    numerator = jnp.sum(weights[:, :, None] * corr_f, axis=1)
    denominator = jnp.sum(weights, axis=1)
    return (numerator, denominator)


def select_rows(selector, rows):
    return jnp.einsum("sc,cwf->swf", selector, rows, preferred_element_type=jnp.float32)


def local(spectra, pair_anchor, pair_offset, pair_partner, pair_count, window_bins, bin_gain):
    block_chans, local_wins, spec_width = spectra.shape
    pair_slots = pair_anchor.shape[0]
    white = whiten(spectra)
    before, after = ring_neighbours(white, "chan")
    transform = lag_table(spec_width // 2, LAG)
    lag_count = transform.shape[1]
    live_count = pair_count[0]

    chan_ids = lax.broadcasted_iota(jnp.int32, (pair_slots, block_chans), 1)
    pick_anchor = (pair_anchor[:, None] == chan_ids).astype(jnp.bfloat16)
    pick_partner = pair_partner[:, None] == chan_ids
    offsets = pair_offset[:, None]
    anchors = select_rows(pick_anchor, white).astype(jnp.bfloat16)
    partners = (
        select_rows((pick_partner & (offsets == 1)).astype(jnp.bfloat16), white)
        + select_rows((pick_partner & (offsets == 0)).astype(jnp.bfloat16), before)
        + select_rows((pick_partner & (offsets == 2)).astype(jnp.bfloat16), after)
    ).astype(jnp.bfloat16)
    cross_spec = cross_spectra(anchors, partners)
    corr_full = jnp.dot(
        cross_spec.reshape(pair_slots * local_wins, spec_width),
        transform,
        preferred_element_type=jnp.float32,
    ).reshape(pair_slots, local_wins, lag_count)
    corr_all = corr_full.astype(jnp.bfloat16)
    running = jnp.sum(corr_full, axis=1)

    ref_sum = lax.psum(running, "win")
    norm_scale = jnp.sqrt(jnp.float32(local_wins * lax.axis_size("win")))
    slot_ids = lax.broadcasted_iota(jnp.int32, (pair_slots,), 0)
    live = slot_ids < live_count
    ref_stack = jnp.where(live[:, None], ref_sum / norm_scale, 0.0)
    window_gain = window_gains(window_bins, bin_gain)
    numerator, denominator = window_weights(corr_all, ref_sum, window_gain)
    numerator, denominator = lax.psum((numerator, denominator), "win")
    restack = jnp.where(live[:, None], norm_scale * numerator / denominator[:, None], 0.0)
    return (ref_stack, restack)


def solution(mesh):
    in_specs = (
        P(("days", "chan"), "win", None),
        P("chan"),
        P("chan"),
        P("chan"),
        P("chan"),
        P(("days", "win")),
        P(),
    )
    out_specs = (P(("days", "chan"), None), P(("days", "chan"), None))
    return jax.shard_map(local, mesh=mesh, in_specs=in_specs, out_specs=out_specs, check_vma=False)
```

```python
import jax
import jax.numpy as jnp
from jax import lax
from jax.sharding import PartitionSpec as P

LAG = 128


EPS_POWER = 1e-05
EPS_LAG = 1e-06


def whiten(spectra):
    spectra_f = spectra.astype(jnp.float32)
    power_mean = jnp.mean(spectra_f * spectra_f, axis=-1, keepdims=True)
    return (spectra_f * lax.rsqrt(power_mean + EPS_POWER)).astype(jnp.bfloat16)


def lag_table(freq_count, lag_count):
    freq_ids = lax.broadcasted_iota(jnp.float32, (freq_count, lag_count), 0)
    lag_ids = lax.broadcasted_iota(jnp.float32, (freq_count, lag_count), 1) - lag_count // 2
    angles = 2.0 * jnp.pi / (2 * freq_count) * freq_ids * lag_ids
    norm_scale = 1.0 / jnp.sqrt(jnp.float32(freq_count))
    return jnp.concatenate(
        [jnp.cos(angles) * norm_scale, -jnp.sin(angles) * norm_scale], axis=0
    ).astype(jnp.bfloat16)


def cross_spectra(anchors, partners):
    half_width = anchors.shape[-1] // 2
    anchor_f = anchors.astype(jnp.float32)
    partner_f = partners.astype(jnp.float32)
    anchor_re = anchor_f[..., :half_width]
    anchor_im = anchor_f[..., half_width:]
    partner_re = partner_f[..., :half_width]
    partner_im = partner_f[..., half_width:]
    cross_re = anchor_re * partner_re + anchor_im * partner_im
    cross_im = anchor_im * partner_re - anchor_re * partner_im
    return jnp.concatenate([cross_re, cross_im], axis=-1).astype(jnp.bfloat16)


def window_gains(bins, gains):
    levels = lax.broadcasted_iota(jnp.int32, (bins.shape[0], gains.shape[0]), 1)
    return jnp.sum(jnp.where(bins[:, None] == levels, gains[None, :], jnp.float32(0.0)), axis=1)


def window_weights(lag_corr, ref_sum, window_gain):
    corr_f = lag_corr.astype(jnp.float32)
    inner_prod = jnp.mean(corr_f * ref_sum[:, None, :], axis=-1)
    corr_rms = jnp.sqrt(jnp.mean(corr_f * corr_f, axis=-1) + EPS_LAG)
    ref_rms = jnp.sqrt(jnp.mean(ref_sum * ref_sum, axis=-1) + EPS_LAG)
    coherence = inner_prod / (corr_rms * ref_rms[:, None])
    weights = window_gain[None, :] * jnp.exp(2.0 * coherence)
    numerator = jnp.sum(weights[:, :, None] * corr_f, axis=1)
    denominator = jnp.sum(weights, axis=1)
    return (numerator, denominator)


def select_rows(selector, rows):
    return jnp.einsum("sc,cwf->swf", selector, rows, preferred_element_type=jnp.float32)


def ring_exchange(up_rows, down_rows, axis):
    peers = lax.axis_size(axis)
    up = [(i, (i + 1) % peers) for i in range(peers)]
    down = [(j, i) for i, j in up]
    return lax.ppermute(up_rows, axis, up), lax.ppermute(down_rows, axis, down)


def onehot(index, size, mask):
    return (index[:, None] == lax.broadcasted_iota(jnp.int32, (index.shape[0], size), 1)) & mask[:, None]


def local(spectra, pair_anchor, pair_offset, pair_partner, pair_count, window_bins, bin_gain):
    block_chans, local_wins, spec_width = spectra.shape
    pair_slots = pair_anchor.shape[0]
    blocks = lax.axis_size("chan")
    block = lax.axis_index("chan")
    fast_rows = (block_chans // 2 + 15) // 16 * 16
    spill_rows = block_chans - fast_rows

    table = jnp.concatenate([pair_offset, pair_partner, pair_count])
    tables = lax.all_gather(table, "chan")
    offs = tables[:, :pair_slots]
    parts = tables[:, pair_slots:2 * pair_slots]
    counts = tables[:, 2 * pair_slots]
    live_all = lax.broadcasted_iota(jnp.int32, offs.shape, 1) < counts[:, None]
    hit = parts[:, :, None] == lax.broadcasted_iota(jnp.int32, (1, 1, block_chans), 2)
    need_minus = jnp.any(hit & (live_all & (offs == 0))[:, :, None], axis=1)
    need_plus = jnp.any(hit & (live_all & (offs == 2))[:, :, None], axis=1)
    need_most = jnp.maximum(
        jnp.max(jnp.sum(need_minus, axis=1, dtype=jnp.int32)),
        jnp.max(jnp.sum(need_plus, axis=1, dtype=jnp.int32)),
    )
    pos_minus = jnp.cumsum(need_minus, axis=1, dtype=jnp.int32) - 1
    pos_plus = jnp.cumsum(need_plus, axis=1, dtype=jnp.int32) - 1

    white = whiten(spectra)
    chan_ids = lax.broadcasted_iota(jnp.int32, (block_chans,), 0)

    def send_selector(need, pos, first, rows):
        return onehot(pos - first, rows, need).T.astype(jnp.bfloat16)

    up_block = (block + 1) % blocks
    down_block = (block + blocks - 1) % blocks
    up_need, up_pos = need_minus[up_block], pos_minus[up_block]
    down_need, down_pos = need_plus[down_block], pos_plus[down_block]

    def gather_rows(first, rows):
        up_rows = select_rows(send_selector(up_need, up_pos, first, rows), white).astype(jnp.bfloat16)
        down_rows = select_rows(send_selector(down_need, down_pos, first, rows), white).astype(jnp.bfloat16)
        return ring_exchange(up_rows, down_rows, "chan")

    before_fast, after_fast = gather_rows(0, fast_rows)

    def spill(_):
        return gather_rows(fast_rows, spill_rows)

    def no_spill(_):
        empty = jnp.zeros((spill_rows, local_wins, spec_width), jnp.bfloat16)
        return empty, empty

    before_spill, after_spill = lax.cond(need_most > fast_rows, spill, no_spill, 0)

    transform = lag_table(spec_width // 2, LAG)
    lag_count = transform.shape[1]
    live_count = pair_count[0]
    slot_ids = lax.broadcasted_iota(jnp.int32, (pair_slots,), 0)
    live = slot_ids < live_count

    anchors = select_rows(onehot(pair_anchor, block_chans, live).astype(jnp.bfloat16), white).astype(jnp.bfloat16)
    before_row = jnp.take(pos_minus[block], pair_partner)
    after_row = jnp.take(pos_plus[block], pair_partner)
    use_before = live & (pair_offset == 0)
    use_after = live & (pair_offset == 2)
    partners = (
        select_rows(onehot(pair_partner, block_chans, live & (pair_offset == 1)).astype(jnp.bfloat16), white)
        + select_rows(onehot(before_row, fast_rows, use_before).astype(jnp.bfloat16), before_fast)
        + select_rows(onehot(after_row, fast_rows, use_after).astype(jnp.bfloat16), after_fast)
        + select_rows(onehot(before_row - fast_rows, spill_rows, use_before).astype(jnp.bfloat16), before_spill)
        + select_rows(onehot(after_row - fast_rows, spill_rows, use_after).astype(jnp.bfloat16), after_spill)
    ).astype(jnp.bfloat16)
    cross_spec = cross_spectra(anchors, partners)
    corr_full = jnp.dot(
        cross_spec.reshape(pair_slots * local_wins, spec_width),
        transform,
        preferred_element_type=jnp.float32,
    ).reshape(pair_slots, local_wins, lag_count)
    corr_all = corr_full.astype(jnp.bfloat16)
    running = jnp.sum(corr_full, axis=1)

    ref_sum = lax.psum(running, "win")
    norm_scale = jnp.sqrt(jnp.float32(local_wins * lax.axis_size("win")))
    ref_stack = jnp.where(live[:, None], ref_sum / norm_scale, 0.0)
    window_gain = window_gains(window_bins, bin_gain)
    numerator, denominator = window_weights(corr_all, ref_sum, window_gain)
    numerator, denominator = lax.psum((numerator, denominator), "win")
    restack = jnp.where(live[:, None], norm_scale * numerator / denominator[:, None], 0.0)
    return (ref_stack, restack)


def solution(mesh):
    in_specs = (
        P(("days", "chan"), "win", None),
        P("chan"),
        P("chan"),
        P("chan"),
        P("chan"),
        P(("days", "win")),
        P(),
    )
    out_specs = (P(("days", "chan"), None), P(("days", "chan"), None))
    return jax.shard_map(local, mesh=mesh, in_specs=in_specs, out_specs=out_specs, check_vma=False)
```

```python
import jax
import jax.numpy as jnp
from jax import lax
from jax.sharding import PartitionSpec as P

LAG = 128


EPS_POWER = 1e-05
EPS_LAG = 1e-06


def whiten(spectra):
    spectra_f = spectra.astype(jnp.float32)
    power_mean = jnp.mean(spectra_f * spectra_f, axis=-1, keepdims=True)
    return (spectra_f * lax.rsqrt(power_mean + EPS_POWER)).astype(jnp.bfloat16)


def lag_table(freq_count, lag_count):
    freq_ids = lax.broadcasted_iota(jnp.float32, (freq_count, lag_count), 0)
    lag_ids = lax.broadcasted_iota(jnp.float32, (freq_count, lag_count), 1) - lag_count // 2
    angles = 2.0 * jnp.pi / (2 * freq_count) * freq_ids * lag_ids
    norm_scale = 1.0 / jnp.sqrt(jnp.float32(freq_count))
    return jnp.concatenate(
        [jnp.cos(angles) * norm_scale, -jnp.sin(angles) * norm_scale], axis=0
    ).astype(jnp.bfloat16)


def cross_spectra(anchors, partners):
    half_width = anchors.shape[-1] // 2
    anchor_f = anchors.astype(jnp.float32)
    partner_f = partners.astype(jnp.float32)
    anchor_re = anchor_f[..., :half_width]
    anchor_im = anchor_f[..., half_width:]
    partner_re = partner_f[..., :half_width]
    partner_im = partner_f[..., half_width:]
    cross_re = anchor_re * partner_re + anchor_im * partner_im
    cross_im = anchor_im * partner_re - anchor_re * partner_im
    return jnp.concatenate([cross_re, cross_im], axis=-1).astype(jnp.bfloat16)


def window_gains(bins, gains):
    levels = lax.broadcasted_iota(jnp.int32, (bins.shape[0], gains.shape[0]), 1)
    return jnp.sum(jnp.where(bins[:, None] == levels, gains[None, :], jnp.float32(0.0)), axis=1)


def window_weights(lag_corr, ref_sum, window_gain):
    corr_f = lag_corr.astype(jnp.float32)
    inner_prod = jnp.mean(corr_f * ref_sum[:, None, :], axis=-1)
    corr_rms = jnp.sqrt(jnp.mean(corr_f * corr_f, axis=-1) + EPS_LAG)
    ref_rms = jnp.sqrt(jnp.mean(ref_sum * ref_sum, axis=-1) + EPS_LAG)
    coherence = inner_prod / (corr_rms * ref_rms[:, None])
    weights = window_gain[None, :] * jnp.exp(2.0 * coherence)
    numerator = jnp.sum(weights[:, :, None] * corr_f, axis=1)
    denominator = jnp.sum(weights, axis=1)
    return (numerator, denominator)


def select_rows(selector, rows):
    return jnp.einsum("sc,cwf->swf", selector, rows, preferred_element_type=jnp.bfloat16)


def butterfly_sum(value, axis):
    peers = lax.axis_size(axis)
    if peers & (peers - 1):
        return lax.psum(value, axis)
    step = 1
    while step < peers:
        pairs = [(i, i ^ step) for i in range(peers)]
        value = jax.tree.map(jnp.add, value, lax.ppermute(value, axis, pairs))
        step *= 2
    return value


def ring_exchange(up_rows, down_rows, axis):
    peers = lax.axis_size(axis)
    up = [(i, (i + 1) % peers) for i in range(peers)]
    down = [(j, i) for i, j in up]
    return lax.ppermute(up_rows, axis, up), lax.ppermute(down_rows, axis, down)


def onehot(index, size, mask):
    return (index[:, None] == lax.broadcasted_iota(jnp.int32, (index.shape[0], size), 1)) & mask[:, None]


def local(spectra, pair_anchor, pair_offset, pair_partner, pair_count, window_bins, bin_gain):
    block_chans, local_wins, spec_width = spectra.shape
    pair_slots = pair_anchor.shape[0]
    blocks = lax.axis_size("chan")
    block = lax.axis_index("chan")
    fast_rows = (block_chans // 2 + 15) // 16 * 16
    spill_rows = block_chans - fast_rows

    table = jnp.concatenate([pair_offset, pair_partner, pair_count])
    tables = lax.all_gather(table.astype(jnp.float32), "chan").astype(jnp.int32)
    offs = tables[:, :pair_slots]
    parts = tables[:, pair_slots:2 * pair_slots]
    counts = tables[:, 2 * pair_slots]
    live_all = lax.broadcasted_iota(jnp.int32, offs.shape, 1) < counts[:, None]
    hit = parts[:, :, None] == lax.broadcasted_iota(jnp.int32, (1, 1, block_chans), 2)
    need_minus = jnp.any(hit & (live_all & (offs == 0))[:, :, None], axis=1)
    need_plus = jnp.any(hit & (live_all & (offs == 2))[:, :, None], axis=1)
    need_most = jnp.maximum(
        jnp.max(jnp.sum(need_minus, axis=1, dtype=jnp.int32)),
        jnp.max(jnp.sum(need_plus, axis=1, dtype=jnp.int32)),
    )
    pos_minus = jnp.cumsum(need_minus, axis=1, dtype=jnp.int32) - 1
    pos_plus = jnp.cumsum(need_plus, axis=1, dtype=jnp.int32) - 1

    white = whiten(spectra)
    chan_ids = lax.broadcasted_iota(jnp.int32, (block_chans,), 0)

    def send_selector(need, pos, first, rows):
        return onehot(pos - first, rows, need).T.astype(jnp.bfloat16)

    up_block = (block + 1) % blocks
    down_block = (block + blocks - 1) % blocks
    up_need, up_pos = need_minus[up_block], pos_minus[up_block]
    down_need, down_pos = need_plus[down_block], pos_plus[down_block]

    def gather_rows(first, rows):
        up_rows = select_rows(send_selector(up_need, up_pos, first, rows), white).astype(jnp.bfloat16)
        down_rows = select_rows(send_selector(down_need, down_pos, first, rows), white).astype(jnp.bfloat16)
        return ring_exchange(up_rows, down_rows, "chan")

    before_fast, after_fast = gather_rows(0, fast_rows)

    def spill(_):
        return gather_rows(fast_rows, spill_rows)

    def no_spill(_):
        empty = jnp.zeros((spill_rows, local_wins, spec_width), jnp.bfloat16)
        return empty, empty

    before_spill, after_spill = lax.cond(need_most > fast_rows, spill, no_spill, 0)

    transform = lag_table(spec_width // 2, LAG)
    lag_count = transform.shape[1]
    live_count = pair_count[0]
    slot_ids = lax.broadcasted_iota(jnp.int32, (pair_slots,), 0)
    live = slot_ids < live_count

    anchors = select_rows(onehot(pair_anchor, block_chans, live).astype(jnp.bfloat16), white).astype(jnp.bfloat16)
    own_hit = onehot(pair_partner, block_chans, live)
    before_row = jnp.sum(jnp.where(own_hit, pos_minus[block][None, :], 0), axis=1)
    after_row = jnp.sum(jnp.where(own_hit, pos_plus[block][None, :], 0), axis=1)
    use_before = live & (pair_offset == 0)
    use_after = live & (pair_offset == 2)
    partners = (
        select_rows(onehot(pair_partner, block_chans, live & (pair_offset == 1)).astype(jnp.bfloat16), white)
        + select_rows(onehot(before_row, fast_rows, use_before).astype(jnp.bfloat16), before_fast)
        + select_rows(onehot(after_row, fast_rows, use_after).astype(jnp.bfloat16), after_fast)
        + select_rows(onehot(before_row - fast_rows, spill_rows, use_before).astype(jnp.bfloat16), before_spill)
        + select_rows(onehot(after_row - fast_rows, spill_rows, use_after).astype(jnp.bfloat16), after_spill)
    ).astype(jnp.bfloat16)
    cross_spec = cross_spectra(anchors, partners)
    corr_full = jnp.dot(
        cross_spec.reshape(pair_slots * local_wins, spec_width),
        transform,
        preferred_element_type=jnp.float32,
    ).reshape(pair_slots, local_wins, lag_count)
    corr_all = corr_full.astype(jnp.bfloat16)
    running = jnp.sum(corr_full, axis=1)

    ref_sum = butterfly_sum(running, "win")
    norm_scale = jnp.sqrt(jnp.float32(local_wins * lax.axis_size("win")))
    ref_stack = jnp.where(live[:, None], ref_sum / norm_scale, 0.0)
    window_gain = window_gains(window_bins, bin_gain)
    numerator, denominator = window_weights(corr_all, ref_sum, window_gain)
    numerator, denominator = butterfly_sum((numerator, denominator), "win")
    restack = jnp.where(live[:, None], norm_scale * numerator / denominator[:, None], 0.0)
    return (ref_stack, restack)


def solution(mesh):
    in_specs = (
        P(("days", "chan"), "win", None),
        P("chan"),
        P("chan"),
        P("chan"),
        P("chan"),
        P(("days", "win")),
        P(),
    )
    out_specs = (P(("days", "chan"), None), P(("days", "chan"), None))
    return jax.shard_map(local, mesh=mesh, in_specs=in_specs, out_specs=out_specs, check_vma=False)
```

```python
import jax
import jax.numpy as jnp
from jax import lax
from jax.experimental import pallas as pl
from jax.experimental.pallas import tpu as pltpu
from jax.sharding import PartitionSpec as P

LAG = 128


EPS_POWER = 1e-05
EPS_LAG = 1e-06


def whiten(spectra):
    spectra_f = spectra.astype(jnp.float32)
    power_mean = jnp.mean(spectra_f * spectra_f, axis=-1, keepdims=True)
    return (spectra_f * lax.rsqrt(power_mean + EPS_POWER)).astype(jnp.bfloat16)


def lag_table(freq_count, lag_count):
    freq_ids = lax.broadcasted_iota(jnp.float32, (freq_count, lag_count), 0)
    lag_ids = lax.broadcasted_iota(jnp.float32, (freq_count, lag_count), 1) - lag_count // 2
    angles = 2.0 * jnp.pi / (2 * freq_count) * freq_ids * lag_ids
    norm_scale = 1.0 / jnp.sqrt(jnp.float32(freq_count))
    return jnp.concatenate(
        [jnp.cos(angles) * norm_scale, -jnp.sin(angles) * norm_scale], axis=0
    ).astype(jnp.bfloat16)


def cross_spectra(anchors, partners):
    half_width = anchors.shape[-1] // 2
    anchor_f = anchors.astype(jnp.float32)
    partner_f = partners.astype(jnp.float32)
    anchor_re = anchor_f[..., :half_width]
    anchor_im = anchor_f[..., half_width:]
    partner_re = partner_f[..., :half_width]
    partner_im = partner_f[..., half_width:]
    cross_re = anchor_re * partner_re + anchor_im * partner_im
    cross_im = anchor_im * partner_re - anchor_re * partner_im
    return jnp.concatenate([cross_re, cross_im], axis=-1).astype(jnp.bfloat16)


def window_gains(bins, gains):
    levels = lax.broadcasted_iota(jnp.int32, (bins.shape[0], gains.shape[0]), 1)
    return jnp.sum(jnp.where(bins[:, None] == levels, gains[None, :], jnp.float32(0.0)), axis=1)


def window_weights(lag_corr, ref_sum, window_gain):
    corr_f = lag_corr.astype(jnp.float32)
    inner_prod = jnp.mean(corr_f * ref_sum[:, None, :], axis=-1)
    corr_rms = jnp.sqrt(jnp.mean(corr_f * corr_f, axis=-1) + EPS_LAG)
    ref_rms = jnp.sqrt(jnp.mean(ref_sum * ref_sum, axis=-1) + EPS_LAG)
    coherence = inner_prod / (corr_rms * ref_rms[:, None])
    weights = window_gain[None, :] * jnp.exp(2.0 * coherence)
    numerator = jnp.sum(weights[:, :, None] * corr_f, axis=1)
    denominator = jnp.sum(weights, axis=1)
    return (numerator, denominator)


def select_rows(selector, rows):
    return jnp.einsum("sc,cwf->swf", selector, rows, preferred_element_type=jnp.bfloat16)


def butterfly_sum(value, axis):
    peers = lax.axis_size(axis)
    if peers & (peers - 1):
        return lax.psum(value, axis)
    step = 1
    while step < peers:
        pairs = [(i, i ^ step) for i in range(peers)]
        value = jax.tree.map(jnp.add, value, lax.ppermute(value, axis, pairs))
        step *= 2
    return value


def ring_exchange(up_rows, down_rows, axis):
    peers = lax.axis_size(axis)
    up = [(i, (i + 1) % peers) for i in range(peers)]
    down = [(j, i) for i, j in up]
    return lax.ppermute(up_rows, axis, up), lax.ppermute(down_rows, axis, down)


def onehot(index, size, mask):
    return (index[:, None] == lax.broadcasted_iota(jnp.int32, (index.shape[0], size), 1)) & mask[:, None]


def window_weights_wm(corr_f, ref_sum, window_gain):
    inner_prod = jnp.mean(corr_f * ref_sum[None, :, :], axis=-1)
    corr_rms = jnp.sqrt(jnp.mean(corr_f * corr_f, axis=-1) + EPS_LAG)
    ref_rms = jnp.sqrt(jnp.mean(ref_sum * ref_sum, axis=-1) + EPS_LAG)
    coherence = inner_prod / (corr_rms * ref_rms[None, :])
    weights = window_gain[:, None] * jnp.exp(2.0 * coherence)
    numerator = jnp.sum(weights[:, :, None] * corr_f, axis=0)
    denominator = jnp.sum(weights, axis=0)
    return (numerator, denominator)


def block_needs(offs, parts, count, block_chans):
    live = lax.broadcasted_iota(jnp.int32, offs.shape, 0) < count
    hit = parts[:, None] == lax.broadcasted_iota(jnp.int32, (1, block_chans), 1)
    need_minus = jnp.any(hit & (live & (offs == 0))[:, None], axis=0)
    need_plus = jnp.any(hit & (live & (offs == 2))[:, None], axis=0)
    pos_minus = jnp.cumsum(need_minus, dtype=jnp.int32) - 1
    pos_plus = jnp.cumsum(need_plus, dtype=jnp.int32) - 1
    return need_minus, need_plus, pos_minus, pos_plus


def cross_kernel(spill_ref, anchor_ref, own_ref, sbf_ref, saf_ref, sbs_ref, sas_ref,
                 bf_ref, af_ref, bs_ref, as_ref, t_ref, corr_ref):
    wins = anchor_ref.shape[0]
    half = anchor_ref.shape[2] // 2
    t_re = t_ref[:half, :]
    t_im = t_ref[half:, :]
    sbf, saf = sbf_ref[...], saf_ref[...]
    for w in range(wins):
        part = (
            own_ref[w].astype(jnp.float32)
            + jnp.dot(sbf, bf_ref[w], preferred_element_type=jnp.float32)
            + jnp.dot(saf, af_ref[w], preferred_element_type=jnp.float32)
        )

        def add_spill(p):
            return (
                p
                + jnp.dot(sbs_ref[...], bs_ref[w], preferred_element_type=jnp.float32)
                + jnp.dot(sas_ref[...], as_ref[w], preferred_element_type=jnp.float32)
            )

        part = lax.cond(spill_ref[0] != 0, add_spill, lambda p: p, part)
        anc = anchor_ref[w].astype(jnp.float32)
        a_re, a_im = anc[:, :half], anc[:, half:]
        p_re, p_im = part[:, :half], part[:, half:]
        c_re = (a_re * p_re + a_im * p_im).astype(jnp.bfloat16)
        c_im = (a_im * p_re - a_re * p_im).astype(jnp.bfloat16)
        corr_ref[w] = jnp.dot(c_re, t_re, preferred_element_type=jnp.float32) + jnp.dot(
            c_im, t_im, preferred_element_type=jnp.float32
        )


def halo_cross(spill, anchors, own, sels, bufs, transform):
    wins, slots, width = anchors.shape
    lag_count = transform.shape[1]
    group = min(128, slots)
    row_spec = pl.BlockSpec((wins, group, width), lambda i, s: (0, i, 0))
    sel_specs = [pl.BlockSpec((group, sel.shape[1]), lambda i, s: (i, 0)) for sel in sels]
    buf_specs = [pl.BlockSpec(buf.shape, lambda i, s: (0, 0, 0)) for buf in bufs]
    grid_spec = pltpu.PrefetchScalarGridSpec(
        num_scalar_prefetch=1,
        grid=(slots // group,),
        in_specs=[row_spec, row_spec] + sel_specs + buf_specs
        + [pl.BlockSpec(transform.shape, lambda i, s: (0, 0))],
        out_specs=pl.BlockSpec((wins, group, lag_count), lambda i, s: (0, i, 0)),
    )
    return pl.pallas_call(
        cross_kernel,
        grid_spec=grid_spec,
        out_shape=jax.ShapeDtypeStruct((wins, slots, lag_count), jnp.float32),
        compiler_params=pltpu.CompilerParams(vmem_limit_bytes=56 * 1024 * 1024),
    )(spill, anchors, own, *sels, *bufs, transform)


def local(spectra, pair_anchor, pair_offset, pair_partner, pair_count, window_bins, bin_gain):
    block_chans, local_wins, spec_width = spectra.shape
    pair_slots = pair_anchor.shape[0]
    fast_rows = (block_chans // 2 + 15) // 16 * 16
    spill_rows = block_chans - fast_rows

    table = jnp.concatenate([pair_offset, pair_partner, pair_count])
    table_before, table_after = ring_exchange(table, table, "chan")

    def needs_of(tab):
        return block_needs(tab[:pair_slots], tab[pair_slots:2 * pair_slots], tab[2 * pair_slots], block_chans)

    own_minus, own_plus, own_pos_minus, own_pos_plus = needs_of(table)
    up_need, _, up_pos, _ = needs_of(table_after)
    _, down_need, _, down_pos = needs_of(table_before)
    own_most = jnp.maximum(jnp.sum(own_minus, dtype=jnp.int32), jnp.sum(own_plus, dtype=jnp.int32))
    need_most = lax.pmax(own_most.astype(jnp.float32), "chan")

    white = whiten(spectra)

    def send_selector(need, pos, first, rows):
        return onehot(pos - first, rows, need).T.astype(jnp.bfloat16)

    def gather_rows(first, rows):
        up_rows = jnp.einsum("jc,cwf->wjf", send_selector(up_need, up_pos, first, rows), white,
                             preferred_element_type=jnp.bfloat16)
        down_rows = jnp.einsum("jc,cwf->wjf", send_selector(down_need, down_pos, first, rows), white,
                               preferred_element_type=jnp.bfloat16)
        return ring_exchange(up_rows, down_rows, "chan")

    before_fast, after_fast = gather_rows(0, fast_rows)
    spill = need_most > fast_rows

    def do_spill(_):
        return gather_rows(fast_rows, spill_rows)

    def no_spill(_):
        empty = jnp.zeros((local_wins, spill_rows, spec_width), jnp.bfloat16)
        return empty, empty

    before_spill, after_spill = lax.cond(spill, do_spill, no_spill, 0)

    transform = lag_table(spec_width // 2, LAG)
    lag_count = transform.shape[1]
    live_count = pair_count[0]
    slot_ids = lax.broadcasted_iota(jnp.int32, (pair_slots,), 0)
    live = slot_ids < live_count

    def pick(selector, rows):
        return jnp.einsum("sc,cwf->wsf", selector.astype(jnp.bfloat16), rows, preferred_element_type=jnp.bfloat16)

    anchors = pick(onehot(pair_anchor, block_chans, live), white)
    own = pick(onehot(pair_partner, block_chans, live & (pair_offset == 1)), white)
    own_hit = onehot(pair_partner, block_chans, live)
    before_row = jnp.sum(jnp.where(own_hit, own_pos_minus[None, :], 0), axis=1)
    after_row = jnp.sum(jnp.where(own_hit, own_pos_plus[None, :], 0), axis=1)
    use_before = live & (pair_offset == 0)
    use_after = live & (pair_offset == 2)
    sels = [
        onehot(before_row, fast_rows, use_before).astype(jnp.bfloat16),
        onehot(after_row, fast_rows, use_after).astype(jnp.bfloat16),
        onehot(before_row - fast_rows, spill_rows, use_before).astype(jnp.bfloat16),
        onehot(after_row - fast_rows, spill_rows, use_after).astype(jnp.bfloat16),
    ]
    corr_full = halo_cross(
        spill.astype(jnp.int32).reshape(1), anchors, own, sels,
        [before_fast, after_fast, before_spill, after_spill], transform,
    )
    corr_all = corr_full.astype(jnp.bfloat16).astype(jnp.float32)
    running = jnp.sum(corr_full, axis=0)

    ref_sum = butterfly_sum(running, "win")
    norm_scale = jnp.sqrt(jnp.float32(local_wins * lax.axis_size("win")))
    ref_stack = jnp.where(live[:, None], ref_sum / norm_scale, 0.0)
    window_gain = window_gains(window_bins, bin_gain)
    numerator, denominator = window_weights_wm(corr_all, ref_sum, window_gain)
    numerator, denominator = butterfly_sum((numerator, denominator), "win")
    restack = jnp.where(live[:, None], norm_scale * numerator / denominator[:, None], 0.0)
    return (ref_stack, restack)


def solution(mesh):
    in_specs = (
        P(("days", "chan"), "win", None),
        P("chan"),
        P("chan"),
        P("chan"),
        P("chan"),
        P(("days", "win")),
        P(),
    )
    out_specs = (P(("days", "chan"), None), P(("days", "chan"), None))
    return jax.shard_map(local, mesh=mesh, in_specs=in_specs, out_specs=out_specs, check_vma=False)
```

```python
import jax
import jax.numpy as jnp
from jax import lax
from jax.experimental import pallas as pl
from jax.experimental.pallas import tpu as pltpu
from jax.sharding import PartitionSpec as P

LAG = 128


EPS_POWER = 1e-05
EPS_LAG = 1e-06


def whiten(spectra):
    spectra_f = spectra.astype(jnp.float32)
    power_mean = jnp.mean(spectra_f * spectra_f, axis=-1, keepdims=True)
    return (spectra_f * lax.rsqrt(power_mean + EPS_POWER)).astype(jnp.bfloat16)


def lag_table(freq_count, lag_count):
    freq_ids = lax.broadcasted_iota(jnp.float32, (freq_count, lag_count), 0)
    lag_ids = lax.broadcasted_iota(jnp.float32, (freq_count, lag_count), 1) - lag_count // 2
    angles = 2.0 * jnp.pi / (2 * freq_count) * freq_ids * lag_ids
    norm_scale = 1.0 / jnp.sqrt(jnp.float32(freq_count))
    return jnp.concatenate(
        [jnp.cos(angles) * norm_scale, -jnp.sin(angles) * norm_scale], axis=0
    ).astype(jnp.bfloat16)


def cross_spectra(anchors, partners):
    half_width = anchors.shape[-1] // 2
    anchor_f = anchors.astype(jnp.float32)
    partner_f = partners.astype(jnp.float32)
    anchor_re = anchor_f[..., :half_width]
    anchor_im = anchor_f[..., half_width:]
    partner_re = partner_f[..., :half_width]
    partner_im = partner_f[..., half_width:]
    cross_re = anchor_re * partner_re + anchor_im * partner_im
    cross_im = anchor_im * partner_re - anchor_re * partner_im
    return jnp.concatenate([cross_re, cross_im], axis=-1).astype(jnp.bfloat16)


def window_gains(bins, gains):
    levels = lax.broadcasted_iota(jnp.int32, (bins.shape[0], gains.shape[0]), 1)
    return jnp.sum(jnp.where(bins[:, None] == levels, gains[None, :], jnp.float32(0.0)), axis=1)


def window_weights(lag_corr, ref_sum, window_gain):
    corr_f = lag_corr.astype(jnp.float32)
    inner_prod = jnp.mean(corr_f * ref_sum[:, None, :], axis=-1)
    corr_rms = jnp.sqrt(jnp.mean(corr_f * corr_f, axis=-1) + EPS_LAG)
    ref_rms = jnp.sqrt(jnp.mean(ref_sum * ref_sum, axis=-1) + EPS_LAG)
    coherence = inner_prod / (corr_rms * ref_rms[:, None])
    weights = window_gain[None, :] * jnp.exp(2.0 * coherence)
    numerator = jnp.sum(weights[:, :, None] * corr_f, axis=1)
    denominator = jnp.sum(weights, axis=1)
    return (numerator, denominator)


def select_rows(selector, rows):
    return jnp.einsum("sc,cwf->swf", selector, rows, preferred_element_type=jnp.bfloat16)


def butterfly_sum(value, axis):
    peers = lax.axis_size(axis)
    if peers & (peers - 1):
        return lax.psum(value, axis)
    step = 1
    while step < peers:
        pairs = [(i, i ^ step) for i in range(peers)]
        value = jax.tree.map(jnp.add, value, lax.ppermute(value, axis, pairs))
        step *= 2
    return value


def ring_exchange(up_rows, down_rows, axis):
    peers = lax.axis_size(axis)
    up = [(i, (i + 1) % peers) for i in range(peers)]
    down = [(j, i) for i, j in up]
    return lax.ppermute(up_rows, axis, up), lax.ppermute(down_rows, axis, down)


def gather_blocks(row, axis):
    peers = lax.axis_size(axis)
    if peers & (peers - 1):
        return lax.all_gather(row, axis)
    me = lax.axis_index(axis)
    acc = row[None]
    step = 1
    while step < peers:
        pairs = [(i, i ^ step) for i in range(peers)]
        got = lax.ppermute(acc, axis, pairs)
        acc = jnp.where((me & step) == 0, jnp.concatenate([acc, got]), jnp.concatenate([got, acc]))
        step *= 2
    return acc


def onehot(index, size, mask):
    return (index[:, None] == lax.broadcasted_iota(jnp.int32, (index.shape[0], size), 1)) & mask[:, None]


def window_weights_wm(corr_f, ref_sum, window_gain):
    inner_prod = jnp.mean(corr_f * ref_sum[None, :, :], axis=-1)
    corr_rms = jnp.sqrt(jnp.mean(corr_f * corr_f, axis=-1) + EPS_LAG)
    ref_rms = jnp.sqrt(jnp.mean(ref_sum * ref_sum, axis=-1) + EPS_LAG)
    coherence = inner_prod / (corr_rms * ref_rms[None, :])
    weights = window_gain[:, None] * jnp.exp(2.0 * coherence)
    numerator = jnp.sum(weights[:, :, None] * corr_f, axis=0)
    denominator = jnp.sum(weights, axis=0)
    return (numerator, denominator)


def block_needs(offs, parts, count, block_chans):
    live = lax.broadcasted_iota(jnp.int32, offs.shape, 0) < count
    hit = parts[:, None] == lax.broadcasted_iota(jnp.int32, (1, block_chans), 1)
    need_minus = jnp.any(hit & (live & (offs == 0))[:, None], axis=0)
    need_plus = jnp.any(hit & (live & (offs == 2))[:, None], axis=0)
    pos_minus = jnp.cumsum(need_minus, dtype=jnp.int32) - 1
    pos_plus = jnp.cumsum(need_plus, dtype=jnp.int32) - 1
    return need_minus, need_plus, pos_minus, pos_plus


def cross_kernel(spill_ref, anchor_ref, own_ref, sbf_ref, saf_ref, sbs_ref, sas_ref,
                 bf_ref, af_ref, bs_ref, as_ref, t_ref, corr_ref):
    wins = anchor_ref.shape[0]
    half = anchor_ref.shape[2] // 2
    t_re = t_ref[:half, :]
    t_im = t_ref[half:, :]
    sbf, saf = sbf_ref[...], saf_ref[...]
    for w in range(wins):
        part = (
            own_ref[w].astype(jnp.float32)
            + jnp.dot(sbf, bf_ref[w], preferred_element_type=jnp.float32)
            + jnp.dot(saf, af_ref[w], preferred_element_type=jnp.float32)
        )

        def add_spill(p):
            return (
                p
                + jnp.dot(sbs_ref[...], bs_ref[w], preferred_element_type=jnp.float32)
                + jnp.dot(sas_ref[...], as_ref[w], preferred_element_type=jnp.float32)
            )

        part = lax.cond(spill_ref[0] != 0, add_spill, lambda p: p, part)
        anc = anchor_ref[w].astype(jnp.float32)
        a_re, a_im = anc[:, :half], anc[:, half:]
        p_re, p_im = part[:, :half], part[:, half:]
        c_re = (a_re * p_re + a_im * p_im).astype(jnp.bfloat16)
        c_im = (a_im * p_re - a_re * p_im).astype(jnp.bfloat16)
        corr_ref[w] = jnp.dot(c_re, t_re, preferred_element_type=jnp.float32) + jnp.dot(
            c_im, t_im, preferred_element_type=jnp.float32
        )


def halo_cross(spill, chunk, wins, anchors, own, sels, bufs, transform):
    _, slots, width = anchors.shape
    lag_count = transform.shape[1]
    group = min(128, slots)
    row_spec = pl.BlockSpec((wins, group, width), lambda i, s: (chunk, i, 0))
    sel_specs = [pl.BlockSpec((group, sel.shape[1]), lambda i, s: (i, 0)) for sel in sels]
    buf_specs = [
        pl.BlockSpec((wins,) + buf.shape[1:], lambda i, s, c=(chunk if buf.shape[0] > wins else 0): (c, 0, 0)) for buf in bufs
    ]
    grid_spec = pltpu.PrefetchScalarGridSpec(
        num_scalar_prefetch=1,
        grid=(slots // group,),
        in_specs=[row_spec, row_spec] + sel_specs + buf_specs
        + [pl.BlockSpec(transform.shape, lambda i, s: (0, 0))],
        out_specs=pl.BlockSpec((wins, group, lag_count), lambda i, s: (0, i, 0)),
    )
    return pl.pallas_call(
        cross_kernel,
        grid_spec=grid_spec,
        out_shape=jax.ShapeDtypeStruct((wins, slots, lag_count), jnp.float32),
        compiler_params=pltpu.CompilerParams(vmem_limit_bytes=56 * 1024 * 1024),
    )(spill, anchors, own, *sels, *bufs, transform)


def local(spectra, pair_anchor, pair_offset, pair_partner, pair_count, window_bins, bin_gain):
    block_chans, local_wins, spec_width = spectra.shape
    pair_slots = pair_anchor.shape[0]
    fast_rows = (block_chans // 2 + 15) // 16 * 16
    spill_rows = block_chans - fast_rows

    blocks = lax.axis_size("chan")
    block = lax.axis_index("chan")
    table = jnp.concatenate([pair_offset, pair_partner, pair_count])
    tables = gather_blocks(table, "chan")
    table_before = tables[(block + blocks - 1) % blocks]
    table_after = tables[(block + 1) % blocks]

    def needs_of(tab):
        return block_needs(tab[:pair_slots], tab[pair_slots:2 * pair_slots], tab[2 * pair_slots], block_chans)

    own_minus, own_plus, own_pos_minus, own_pos_plus = needs_of(table)
    up_need, _, up_pos, _ = needs_of(table_after)
    _, down_need, _, down_pos = needs_of(table_before)
    all_needs = jax.vmap(needs_of)(tables)
    need_most = jnp.maximum(
        jnp.max(jnp.sum(all_needs[0], axis=1, dtype=jnp.int32)),
        jnp.max(jnp.sum(all_needs[1], axis=1, dtype=jnp.int32)),
    )

    white = whiten(spectra)

    def send_selector(need, pos, first, rows):
        return onehot(pos - first, rows, need).T.astype(jnp.bfloat16)

    def gather_rows(first, rows, source):
        up_rows = jnp.einsum("jc,cwf->wjf", send_selector(up_need, up_pos, first, rows), source,
                             preferred_element_type=jnp.bfloat16)
        down_rows = jnp.einsum("jc,cwf->wjf", send_selector(down_need, down_pos, first, rows), source,
                               preferred_element_type=jnp.bfloat16)
        return ring_exchange(up_rows, down_rows, "chan")

    chunks = 2 if local_wins % 2 == 0 else 1
    chunk_wins = local_wins // chunks
    fast = [gather_rows(0, fast_rows, white[:, c * chunk_wins:(c + 1) * chunk_wins]) for c in range(chunks)]
    spill = need_most > fast_rows

    def do_spill(_):
        return gather_rows(fast_rows, spill_rows, white)

    def no_spill(_):
        empty = jnp.zeros((local_wins, spill_rows, spec_width), jnp.bfloat16)
        return empty, empty

    before_spill, after_spill = lax.cond(spill, do_spill, no_spill, 0)

    transform = lag_table(spec_width // 2, LAG)
    lag_count = transform.shape[1]
    live_count = pair_count[0]
    slot_ids = lax.broadcasted_iota(jnp.int32, (pair_slots,), 0)
    live = slot_ids < live_count

    def pick(selector, rows):
        return jnp.einsum("sc,cwf->wsf", selector.astype(jnp.bfloat16), rows, preferred_element_type=jnp.bfloat16)

    anchors = pick(onehot(pair_anchor, block_chans, live), white)
    own = pick(onehot(pair_partner, block_chans, live & (pair_offset == 1)), white)
    own_hit = onehot(pair_partner, block_chans, live)
    before_row = jnp.sum(jnp.where(own_hit, own_pos_minus[None, :], 0), axis=1)
    after_row = jnp.sum(jnp.where(own_hit, own_pos_plus[None, :], 0), axis=1)
    use_before = live & (pair_offset == 0)
    use_after = live & (pair_offset == 2)
    sels = [
        onehot(before_row, fast_rows, use_before).astype(jnp.bfloat16),
        onehot(after_row, fast_rows, use_after).astype(jnp.bfloat16),
        onehot(before_row - fast_rows, spill_rows, use_before).astype(jnp.bfloat16),
        onehot(after_row - fast_rows, spill_rows, use_after).astype(jnp.bfloat16),
    ]
    corr_full = jnp.concatenate([
        halo_cross(
            spill.astype(jnp.int32).reshape(1), c, chunk_wins, anchors, own, sels,
            [fast[c][0], fast[c][1], before_spill, after_spill], transform,
        )
        for c in range(chunks)
    ])
    corr_all = lax.reduce_precision(corr_full, exponent_bits=8, mantissa_bits=7)
    running = jnp.sum(corr_full, axis=0)

    ref_sum = butterfly_sum(running, "win")
    norm_scale = jnp.sqrt(jnp.float32(local_wins * lax.axis_size("win")))
    ref_stack = jnp.where(live[:, None], ref_sum / norm_scale, 0.0)
    window_gain = window_gains(window_bins, bin_gain)
    numerator, denominator = window_weights_wm(corr_all, ref_sum, window_gain)
    numerator, denominator = butterfly_sum((numerator, denominator), "win")
    restack = jnp.where(live[:, None], norm_scale * numerator / denominator[:, None], 0.0)
    return (ref_stack, restack)


def solution(mesh):
    in_specs = (
        P(("days", "chan"), "win", None),
        P("chan"),
        P("chan"),
        P("chan"),
        P("chan"),
        P(("days", "win")),
        P(),
    )
    out_specs = (P(("days", "chan"), None), P(("days", "chan"), None))
    return jax.shard_map(local, mesh=mesh, in_specs=in_specs, out_specs=out_specs, check_vma=False)
```

```python
import jax
import jax.numpy as jnp
from jax import lax
from jax.experimental import pallas as pl
from jax.experimental.pallas import tpu as pltpu
from jax.sharding import PartitionSpec as P

LAG = 128


EPS_POWER = 1e-05
EPS_LAG = 1e-06


def whiten(spectra):
    spectra_f = spectra.astype(jnp.float32)
    power_mean = jnp.mean(spectra_f * spectra_f, axis=-1, keepdims=True)
    return (spectra_f * lax.rsqrt(power_mean + EPS_POWER)).astype(jnp.bfloat16)


def lag_table(freq_count, lag_count):
    freq_ids = lax.broadcasted_iota(jnp.float32, (freq_count, lag_count), 0)
    lag_ids = lax.broadcasted_iota(jnp.float32, (freq_count, lag_count), 1) - lag_count // 2
    angles = 2.0 * jnp.pi / (2 * freq_count) * freq_ids * lag_ids
    norm_scale = 1.0 / jnp.sqrt(jnp.float32(freq_count))
    return jnp.concatenate(
        [jnp.cos(angles) * norm_scale, -jnp.sin(angles) * norm_scale], axis=0
    ).astype(jnp.bfloat16)


def cross_spectra(anchors, partners):
    half_width = anchors.shape[-1] // 2
    anchor_f = anchors.astype(jnp.float32)
    partner_f = partners.astype(jnp.float32)
    anchor_re = anchor_f[..., :half_width]
    anchor_im = anchor_f[..., half_width:]
    partner_re = partner_f[..., :half_width]
    partner_im = partner_f[..., half_width:]
    cross_re = anchor_re * partner_re + anchor_im * partner_im
    cross_im = anchor_im * partner_re - anchor_re * partner_im
    return jnp.concatenate([cross_re, cross_im], axis=-1).astype(jnp.bfloat16)


def window_gains(bins, gains):
    levels = lax.broadcasted_iota(jnp.int32, (bins.shape[0], gains.shape[0]), 1)
    return jnp.sum(jnp.where(bins[:, None] == levels, gains[None, :], jnp.float32(0.0)), axis=1)


def window_weights(lag_corr, ref_sum, window_gain):
    corr_f = lag_corr.astype(jnp.float32)
    inner_prod = jnp.mean(corr_f * ref_sum[:, None, :], axis=-1)
    corr_rms = jnp.sqrt(jnp.mean(corr_f * corr_f, axis=-1) + EPS_LAG)
    ref_rms = jnp.sqrt(jnp.mean(ref_sum * ref_sum, axis=-1) + EPS_LAG)
    coherence = inner_prod / (corr_rms * ref_rms[:, None])
    weights = window_gain[None, :] * jnp.exp(2.0 * coherence)
    numerator = jnp.sum(weights[:, :, None] * corr_f, axis=1)
    denominator = jnp.sum(weights, axis=1)
    return (numerator, denominator)


def select_rows(selector, rows):
    return jnp.einsum("sc,cwf->swf", selector, rows, preferred_element_type=jnp.bfloat16)


def butterfly_sum(value, axis):
    peers = lax.axis_size(axis)
    if peers & (peers - 1):
        return lax.psum(value, axis)
    step = 1
    while step < peers:
        pairs = [(i, i ^ step) for i in range(peers)]
        value = jax.tree.map(jnp.add, value, lax.ppermute(value, axis, pairs))
        step *= 2
    return value


def ring_exchange(up_rows, down_rows, axis):
    peers = lax.axis_size(axis)
    up = [(i, (i + 1) % peers) for i in range(peers)]
    down = [(j, i) for i, j in up]
    return lax.ppermute(up_rows, axis, up), lax.ppermute(down_rows, axis, down)


def gather_blocks(row, axis):
    peers = lax.axis_size(axis)
    if peers & (peers - 1):
        return lax.all_gather(row, axis)
    me = lax.axis_index(axis)
    acc = row[None]
    step = 1
    while step < peers:
        pairs = [(i, i ^ step) for i in range(peers)]
        got = lax.ppermute(acc, axis, pairs)
        acc = jnp.where((me & step) == 0, jnp.concatenate([acc, got]), jnp.concatenate([got, acc]))
        step *= 2
    return acc


def onehot(index, size, mask):
    return (index[:, None] == lax.broadcasted_iota(jnp.int32, (index.shape[0], size), 1)) & mask[:, None]


def window_weights_wm(corr_f, ref_sum, window_gain):
    inner_prod = jnp.mean(corr_f * ref_sum[None, :, :], axis=-1)
    corr_rms = jnp.sqrt(jnp.mean(corr_f * corr_f, axis=-1) + EPS_LAG)
    ref_rms = jnp.sqrt(jnp.mean(ref_sum * ref_sum, axis=-1) + EPS_LAG)
    coherence = inner_prod / (corr_rms * ref_rms[None, :])
    weights = window_gain[:, None] * jnp.exp(2.0 * coherence)
    numerator = jnp.sum(weights[:, :, None] * corr_f, axis=0)
    denominator = jnp.sum(weights, axis=0)
    return (numerator, denominator)


def block_needs(offs, parts, count, block_chans):
    live = lax.broadcasted_iota(jnp.int32, offs.shape, 0) < count
    hit = parts[:, None] == lax.broadcasted_iota(jnp.int32, (1, block_chans), 1)
    need_minus = jnp.any(hit & (live & (offs == 0))[:, None], axis=0)
    need_plus = jnp.any(hit & (live & (offs == 2))[:, None], axis=0)
    pos_minus = jnp.cumsum(need_minus, dtype=jnp.int32) - 1
    pos_plus = jnp.cumsum(need_plus, dtype=jnp.int32) - 1
    return need_minus, need_plus, pos_minus, pos_plus


def cross_kernel(spill_ref, anchor_ref, own_ref, sbf_ref, saf_ref, sbs_ref, sas_ref,
                 bf_ref, af_ref, bs_ref, as_ref, t_ref, corr_ref):
    wins = anchor_ref.shape[0]
    half = anchor_ref.shape[2] // 2
    t_re = t_ref[:half, :]
    t_im = t_ref[half:, :]
    sbf, saf = sbf_ref[...], saf_ref[...]

    def one_window(w, carry):
        raw = jnp.dot(sbf, bf_ref[w], preferred_element_type=jnp.float32) + jnp.dot(
            saf, af_ref[w], preferred_element_type=jnp.float32
        )

        def add_spill(p):
            return (
                p
                + jnp.dot(sbs_ref[...], bs_ref[w], preferred_element_type=jnp.float32)
                + jnp.dot(sas_ref[...], as_ref[w], preferred_element_type=jnp.float32)
            )

        raw = lax.cond(spill_ref[0] != 0, add_spill, lambda p: p, raw)
        power = jnp.mean(raw * raw, axis=-1, keepdims=True)
        halo = (raw * lax.rsqrt(power + EPS_POWER)).astype(jnp.bfloat16)
        part = own_ref[w].astype(jnp.float32) + halo.astype(jnp.float32)
        anc = anchor_ref[w].astype(jnp.float32)
        a_re, a_im = anc[:, :half], anc[:, half:]
        p_re, p_im = part[:, :half], part[:, half:]
        c_re = (a_re * p_re + a_im * p_im).astype(jnp.bfloat16)
        c_im = (a_im * p_re - a_re * p_im).astype(jnp.bfloat16)
        corr_ref[w] = jnp.dot(c_re, t_re, preferred_element_type=jnp.float32) + jnp.dot(
            c_im, t_im, preferred_element_type=jnp.float32
        )
        return carry

    lax.fori_loop(0, wins, one_window, 0)


def halo_cross(spill, chunk, wins, anchors, own, sels, bufs, transform):
    _, slots, width = anchors.shape
    lag_count = transform.shape[1]
    group = min(128, slots)
    row_spec = pl.BlockSpec((wins, group, width), lambda i, s: (chunk, i, 0))
    sel_specs = [pl.BlockSpec((group, sel.shape[1]), lambda i, s: (i, 0)) for sel in sels]
    buf_specs = [
        pl.BlockSpec((wins,) + buf.shape[1:], lambda i, s, c=(chunk if buf.shape[0] > wins else 0): (c, 0, 0)) for buf in bufs
    ]
    grid_spec = pltpu.PrefetchScalarGridSpec(
        num_scalar_prefetch=1,
        grid=(slots // group,),
        in_specs=[row_spec, row_spec] + sel_specs + buf_specs
        + [pl.BlockSpec(transform.shape, lambda i, s: (0, 0))],
        out_specs=pl.BlockSpec((wins, group, lag_count), lambda i, s: (0, i, 0)),
    )
    return pl.pallas_call(
        cross_kernel,
        grid_spec=grid_spec,
        out_shape=jax.ShapeDtypeStruct((wins, slots, lag_count), jnp.float32),
        compiler_params=pltpu.CompilerParams(vmem_limit_bytes=56 * 1024 * 1024),
    )(spill, anchors, own, *sels, *bufs, transform)


def local(spectra, pair_anchor, pair_offset, pair_partner, pair_count, window_bins, bin_gain):
    block_chans, local_wins, spec_width = spectra.shape
    pair_slots = pair_anchor.shape[0]
    fast_rows = (block_chans // 2 + 15) // 16 * 16
    spill_rows = block_chans - fast_rows

    blocks = lax.axis_size("chan")
    block = lax.axis_index("chan")
    table = jnp.concatenate([pair_offset, pair_partner, pair_count])
    tables = gather_blocks(table, "chan")
    table_before = tables[(block + blocks - 1) % blocks]
    table_after = tables[(block + 1) % blocks]

    def needs_of(tab):
        return block_needs(tab[:pair_slots], tab[pair_slots:2 * pair_slots], tab[2 * pair_slots], block_chans)

    own_minus, own_plus, own_pos_minus, own_pos_plus = needs_of(table)
    up_need, _, up_pos, _ = needs_of(table_after)
    _, down_need, _, down_pos = needs_of(table_before)
    all_needs = jax.vmap(needs_of)(tables)
    need_most = jnp.maximum(
        jnp.max(jnp.sum(all_needs[0], axis=1, dtype=jnp.int32)),
        jnp.max(jnp.sum(all_needs[1], axis=1, dtype=jnp.int32)),
    )

    white = whiten(spectra)

    def send_selector(need, pos, first, rows):
        return onehot(pos - first, rows, need).T.astype(jnp.bfloat16)

    def gather_rows(first, rows, source):
        up_rows = jnp.einsum("jc,cwf->wjf", send_selector(up_need, up_pos, first, rows), source,
                             preferred_element_type=jnp.bfloat16)
        down_rows = jnp.einsum("jc,cwf->wjf", send_selector(down_need, down_pos, first, rows), source,
                               preferred_element_type=jnp.bfloat16)
        return ring_exchange(up_rows, down_rows, "chan")

    chunks = 2 if local_wins % 2 == 0 else 1
    chunk_wins = local_wins // chunks
    fast = [gather_rows(0, fast_rows, spectra[:, c * chunk_wins:(c + 1) * chunk_wins]) for c in range(chunks)]
    spill = need_most > fast_rows

    def do_spill(_):
        return gather_rows(fast_rows, spill_rows, spectra)

    def no_spill(_):
        empty = jnp.zeros((local_wins, spill_rows, spec_width), jnp.bfloat16)
        return empty, empty

    before_spill, after_spill = lax.cond(spill, do_spill, no_spill, 0)

    transform = lag_table(spec_width // 2, LAG)
    lag_count = transform.shape[1]
    live_count = pair_count[0]
    slot_ids = lax.broadcasted_iota(jnp.int32, (pair_slots,), 0)
    live = slot_ids < live_count

    def pick(selector, rows):
        return jnp.einsum("sc,cwf->wsf", selector.astype(jnp.bfloat16), rows, preferred_element_type=jnp.bfloat16)

    anchors = pick(onehot(pair_anchor, block_chans, live), white)
    own = pick(onehot(pair_partner, block_chans, live & (pair_offset == 1)), white)
    own_hit = onehot(pair_partner, block_chans, live)
    before_row = jnp.sum(jnp.where(own_hit, own_pos_minus[None, :], 0), axis=1)
    after_row = jnp.sum(jnp.where(own_hit, own_pos_plus[None, :], 0), axis=1)
    use_before = live & (pair_offset == 0)
    use_after = live & (pair_offset == 2)
    sels = [
        onehot(before_row, fast_rows, use_before).astype(jnp.bfloat16),
        onehot(after_row, fast_rows, use_after).astype(jnp.bfloat16),
        onehot(before_row - fast_rows, spill_rows, use_before).astype(jnp.bfloat16),
        onehot(after_row - fast_rows, spill_rows, use_after).astype(jnp.bfloat16),
    ]
    corr_full = jnp.concatenate([
        halo_cross(
            spill.astype(jnp.int32).reshape(1), c, chunk_wins, anchors, own, sels,
            [fast[c][0], fast[c][1], before_spill, after_spill], transform,
        )
        for c in range(chunks)
    ])
    corr_all = lax.reduce_precision(corr_full, exponent_bits=8, mantissa_bits=7)
    running = jnp.sum(corr_full, axis=0)

    ref_sum = butterfly_sum(running, "win")
    norm_scale = jnp.sqrt(jnp.float32(local_wins * lax.axis_size("win")))
    ref_stack = jnp.where(live[:, None], ref_sum / norm_scale, 0.0)
    window_gain = window_gains(window_bins, bin_gain)
    numerator, denominator = window_weights_wm(corr_all, ref_sum, window_gain)
    numerator, denominator = butterfly_sum((numerator, denominator), "win")
    restack = jnp.where(live[:, None], norm_scale * numerator / denominator[:, None], 0.0)
    return (ref_stack, restack)


def solution(mesh):
    in_specs = (
        P(("days", "chan"), "win", None),
        P("chan"),
        P("chan"),
        P("chan"),
        P("chan"),
        P(("days", "win")),
        P(),
    )
    out_specs = (P(("days", "chan"), None), P(("days", "chan"), None))
    return jax.shard_map(local, mesh=mesh, in_specs=in_specs, out_specs=out_specs, check_vma=False)
```

```python
import jax
import jax.numpy as jnp
from jax import lax
from jax.experimental import pallas as pl
from jax.experimental.pallas import tpu as pltpu
from jax.sharding import PartitionSpec as P

LAG = 128


EPS_POWER = 1e-05
EPS_LAG = 1e-06


def whiten(spectra):
    spectra_f = spectra.astype(jnp.float32)
    power_mean = jnp.mean(spectra_f * spectra_f, axis=-1, keepdims=True)
    return (spectra_f * lax.rsqrt(power_mean + EPS_POWER)).astype(jnp.bfloat16)


def lag_table(freq_count, lag_count):
    freq_ids = lax.broadcasted_iota(jnp.float32, (freq_count, lag_count), 0)
    lag_ids = lax.broadcasted_iota(jnp.float32, (freq_count, lag_count), 1) - lag_count // 2
    angles = 2.0 * jnp.pi / (2 * freq_count) * freq_ids * lag_ids
    norm_scale = 1.0 / jnp.sqrt(jnp.float32(freq_count))
    return jnp.concatenate(
        [jnp.cos(angles) * norm_scale, -jnp.sin(angles) * norm_scale], axis=0
    ).astype(jnp.bfloat16)


def cross_spectra(anchors, partners):
    half_width = anchors.shape[-1] // 2
    anchor_f = anchors.astype(jnp.float32)
    partner_f = partners.astype(jnp.float32)
    anchor_re = anchor_f[..., :half_width]
    anchor_im = anchor_f[..., half_width:]
    partner_re = partner_f[..., :half_width]
    partner_im = partner_f[..., half_width:]
    cross_re = anchor_re * partner_re + anchor_im * partner_im
    cross_im = anchor_im * partner_re - anchor_re * partner_im
    return jnp.concatenate([cross_re, cross_im], axis=-1).astype(jnp.bfloat16)


def window_gains(bins, gains):
    levels = lax.broadcasted_iota(jnp.int32, (bins.shape[0], gains.shape[0]), 1)
    return jnp.sum(jnp.where(bins[:, None] == levels, gains[None, :], jnp.float32(0.0)), axis=1)


def window_weights(lag_corr, ref_sum, window_gain):
    corr_f = lag_corr.astype(jnp.float32)
    inner_prod = jnp.mean(corr_f * ref_sum[:, None, :], axis=-1)
    corr_rms = jnp.sqrt(jnp.mean(corr_f * corr_f, axis=-1) + EPS_LAG)
    ref_rms = jnp.sqrt(jnp.mean(ref_sum * ref_sum, axis=-1) + EPS_LAG)
    coherence = inner_prod / (corr_rms * ref_rms[:, None])
    weights = window_gain[None, :] * jnp.exp(2.0 * coherence)
    numerator = jnp.sum(weights[:, :, None] * corr_f, axis=1)
    denominator = jnp.sum(weights, axis=1)
    return (numerator, denominator)


def select_rows(selector, rows):
    return jnp.einsum("sc,cwf->swf", selector, rows, preferred_element_type=jnp.bfloat16)


def butterfly_sum(value, axis):
    peers = lax.axis_size(axis)
    if peers & (peers - 1):
        return lax.psum(value, axis)
    step = 1
    while step < peers:
        pairs = [(i, i ^ step) for i in range(peers)]
        value = jax.tree.map(jnp.add, value, lax.ppermute(value, axis, pairs))
        step *= 2
    return value


def ring_exchange(up_rows, down_rows, axis):
    peers = lax.axis_size(axis)
    up = [(i, (i + 1) % peers) for i in range(peers)]
    down = [(j, i) for i, j in up]
    return lax.ppermute(up_rows, axis, up), lax.ppermute(down_rows, axis, down)


def gather_blocks(row, axis):
    peers = lax.axis_size(axis)
    if peers & (peers - 1):
        return lax.all_gather(row, axis)
    me = lax.axis_index(axis)
    acc = row[None]
    step = 1
    while step < peers:
        pairs = [(i, i ^ step) for i in range(peers)]
        got = lax.ppermute(acc, axis, pairs)
        acc = jnp.where((me & step) == 0, jnp.concatenate([acc, got]), jnp.concatenate([got, acc]))
        step *= 2
    return acc


def onehot(index, size, mask):
    return (index[:, None] == lax.broadcasted_iota(jnp.int32, (index.shape[0], size), 1)) & mask[:, None]


def window_weights_wm(corr_f, ref_sum, window_gain):
    inner_prod = jnp.mean(corr_f * ref_sum[None, :, :], axis=-1)
    corr_rms = jnp.sqrt(jnp.mean(corr_f * corr_f, axis=-1) + EPS_LAG)
    ref_rms = jnp.sqrt(jnp.mean(ref_sum * ref_sum, axis=-1) + EPS_LAG)
    coherence = inner_prod / (corr_rms * ref_rms[None, :])
    weights = window_gain[:, None] * jnp.exp(2.0 * coherence)
    numerator = jnp.sum(weights[:, :, None] * corr_f, axis=0)
    denominator = jnp.sum(weights, axis=0)
    return (numerator, denominator)


def block_needs(offs, parts, count, block_chans):
    live = lax.broadcasted_iota(jnp.int32, offs.shape, 0) < count
    hit = parts[:, None] == lax.broadcasted_iota(jnp.int32, (1, block_chans), 1)
    need_minus = jnp.any(hit & (live & (offs == 0))[:, None], axis=0)
    need_plus = jnp.any(hit & (live & (offs == 2))[:, None], axis=0)
    pos_minus = jnp.cumsum(need_minus, dtype=jnp.int32) - 1
    pos_plus = jnp.cumsum(need_plus, dtype=jnp.int32) - 1
    return need_minus, need_plus, pos_minus, pos_plus


def cross_kernel(spill_ref, anchor_ref, own_ref, sbf_ref, saf_ref, sbs_ref, sas_ref,
                 bf_ref, af_ref, bs_ref, as_ref, t_ref, corr_ref):
    wins = anchor_ref.shape[0]
    half = anchor_ref.shape[2] // 2
    t_re = t_ref[:half, :]
    t_im = t_ref[half:, :]
    sbf, saf = sbf_ref[...], saf_ref[...]
    for w in range(wins):
        part = (
            own_ref[w].astype(jnp.float32)
            + jnp.dot(sbf, bf_ref[w], preferred_element_type=jnp.float32)
            + jnp.dot(saf, af_ref[w], preferred_element_type=jnp.float32)
        )

        def add_spill(p):
            return (
                p
                + jnp.dot(sbs_ref[...], bs_ref[w], preferred_element_type=jnp.float32)
                + jnp.dot(sas_ref[...], as_ref[w], preferred_element_type=jnp.float32)
            )

        part = lax.cond(spill_ref[0] != 0, add_spill, lambda p: p, part)
        anc = anchor_ref[w].astype(jnp.float32)
        a_re, a_im = anc[:, :half], anc[:, half:]
        p_re, p_im = part[:, :half], part[:, half:]
        c_re = (a_re * p_re + a_im * p_im).astype(jnp.bfloat16)
        c_im = (a_im * p_re - a_re * p_im).astype(jnp.bfloat16)
        corr_ref[w] = jnp.dot(c_re, t_re, preferred_element_type=jnp.float32) + jnp.dot(
            c_im, t_im, preferred_element_type=jnp.float32
        )


def halo_cross(spill, chunk, wins, anchors, own, sels, bufs, transform):
    _, slots, width = anchors.shape
    lag_count = transform.shape[1]
    group = min(128, slots)
    row_spec = pl.BlockSpec((wins, group, width), lambda i, s: (chunk, i, 0))
    sel_specs = [pl.BlockSpec((group, sel.shape[1]), lambda i, s: (i, 0)) for sel in sels]
    buf_specs = [
        pl.BlockSpec((wins,) + buf.shape[1:], lambda i, s, c=(chunk if buf.shape[0] > wins else 0): (c, 0, 0)) for buf in bufs
    ]
    grid_spec = pltpu.PrefetchScalarGridSpec(
        num_scalar_prefetch=1,
        grid=(slots // group,),
        in_specs=[row_spec, row_spec] + sel_specs + buf_specs
        + [pl.BlockSpec(transform.shape, lambda i, s: (0, 0))],
        out_specs=pl.BlockSpec((wins, group, lag_count), lambda i, s: (0, i, 0)),
    )
    return pl.pallas_call(
        cross_kernel,
        grid_spec=grid_spec,
        out_shape=jax.ShapeDtypeStruct((wins, slots, lag_count), jnp.float32),
        compiler_params=pltpu.CompilerParams(vmem_limit_bytes=56 * 1024 * 1024),
    )(spill, anchors, own, *sels, *bufs, transform)


def local(spectra, pair_anchor, pair_offset, pair_partner, pair_count, window_bins, bin_gain):
    block_chans, local_wins, spec_width = spectra.shape
    pair_slots = pair_anchor.shape[0]
    fast_rows = (block_chans // 2 + 15) // 16 * 16
    spill_rows = block_chans - fast_rows

    blocks = lax.axis_size("chan")
    block = lax.axis_index("chan")
    table = jnp.concatenate([pair_offset, pair_partner, pair_count])
    tables = gather_blocks(table, "chan")
    table_before, table_after = ring_exchange(table, table, "chan")

    def needs_of(tab):
        return block_needs(tab[:pair_slots], tab[pair_slots:2 * pair_slots], tab[2 * pair_slots], block_chans)

    own_minus, own_plus, own_pos_minus, own_pos_plus = needs_of(table)
    up_need, _, up_pos, _ = needs_of(table_after)
    _, down_need, _, down_pos = needs_of(table_before)
    all_needs = jax.vmap(needs_of)(tables)
    need_most = jnp.maximum(
        jnp.max(jnp.sum(all_needs[0], axis=1, dtype=jnp.int32)),
        jnp.max(jnp.sum(all_needs[1], axis=1, dtype=jnp.int32)),
    )

    def send_selector(need, pos, first, rows):
        return onehot(pos - first, rows, need).T.astype(jnp.bfloat16)

    def gather_rows(first, rows, source):
        up_rows = jnp.einsum("jc,cwf->wjf", send_selector(up_need, up_pos, first, rows), source,
                             preferred_element_type=jnp.bfloat16)
        down_rows = jnp.einsum("jc,cwf->wjf", send_selector(down_need, down_pos, first, rows), source,
                               preferred_element_type=jnp.bfloat16)
        return ring_exchange(up_rows, down_rows, "chan"), (up_rows, down_rows)

    chunks = 2 if local_wins % 2 == 0 else 1
    chunk_wins = local_wins // chunks
    fast_sent = [gather_rows(0, fast_rows, spectra[:, c * chunk_wins:(c + 1) * chunk_wins]) for c in range(chunks)]
    fast = [got for got, _ in fast_sent]
    spectra_late, _ = lax.optimization_barrier((spectra, [sent for _, sent in fast_sent]))
    white = whiten(spectra_late)
    fast = [(whiten(b), whiten(a)) for b, a in fast]
    spill = need_most > fast_rows

    def do_spill(_):
        (got_before, got_after), _ = gather_rows(fast_rows, spill_rows, spectra)
        return whiten(got_before), whiten(got_after)

    def no_spill(_):
        empty = jnp.zeros((local_wins, spill_rows, spec_width), jnp.bfloat16)
        return empty, empty

    before_spill, after_spill = lax.cond(spill, do_spill, no_spill, 0)

    transform = lag_table(spec_width // 2, LAG)
    lag_count = transform.shape[1]
    live_count = pair_count[0]
    slot_ids = lax.broadcasted_iota(jnp.int32, (pair_slots,), 0)
    live = slot_ids < live_count

    def pick(selector, rows):
        return jnp.einsum("sc,cwf->wsf", selector.astype(jnp.bfloat16), rows, preferred_element_type=jnp.bfloat16)

    anchors = pick(onehot(pair_anchor, block_chans, live), white)
    own = pick(onehot(pair_partner, block_chans, live & (pair_offset == 1)), white)
    own_hit = onehot(pair_partner, block_chans, live)
    before_row = jnp.sum(jnp.where(own_hit, own_pos_minus[None, :], 0), axis=1)
    after_row = jnp.sum(jnp.where(own_hit, own_pos_plus[None, :], 0), axis=1)
    use_before = live & (pair_offset == 0)
    use_after = live & (pair_offset == 2)
    sels = [
        onehot(before_row, fast_rows, use_before).astype(jnp.bfloat16),
        onehot(after_row, fast_rows, use_after).astype(jnp.bfloat16),
        onehot(before_row - fast_rows, spill_rows, use_before).astype(jnp.bfloat16),
        onehot(after_row - fast_rows, spill_rows, use_after).astype(jnp.bfloat16),
    ]
    corr_full = jnp.concatenate([
        halo_cross(
            spill.astype(jnp.int32).reshape(1), c, chunk_wins, anchors, own, sels,
            [fast[c][0], fast[c][1], before_spill, after_spill], transform,
        )
        for c in range(chunks)
    ])
    corr_all = lax.reduce_precision(corr_full, exponent_bits=8, mantissa_bits=7)
    running = jnp.sum(corr_full, axis=0)

    ref_sum = butterfly_sum(running, "win")
    norm_scale = jnp.sqrt(jnp.float32(local_wins * lax.axis_size("win")))
    ref_stack = jnp.where(live[:, None], ref_sum / norm_scale, 0.0)
    window_gain = window_gains(window_bins, bin_gain)
    numerator, denominator = window_weights_wm(corr_all, ref_sum, window_gain)
    numerator, denominator = butterfly_sum((numerator, denominator), "win")
    restack = jnp.where(live[:, None], norm_scale * numerator / denominator[:, None], 0.0)
    return (ref_stack, restack)


def solution(mesh):
    in_specs = (
        P(("days", "chan"), "win", None),
        P("chan"),
        P("chan"),
        P("chan"),
        P("chan"),
        P(("days", "win")),
        P(),
    )
    out_specs = (P(("days", "chan"), None), P(("days", "chan"), None))
    return jax.shard_map(local, mesh=mesh, in_specs=in_specs, out_specs=out_specs, check_vma=False)
```

```python
import jax
import jax.numpy as jnp
from jax import lax
from jax.experimental import pallas as pl
from jax.experimental.pallas import tpu as pltpu
from jax.sharding import PartitionSpec as P

LAG = 128


EPS_POWER = 1e-05
EPS_LAG = 1e-06


def whiten(spectra):
    spectra_f = spectra.astype(jnp.float32)
    power_mean = jnp.mean(spectra_f * spectra_f, axis=-1, keepdims=True)
    return (spectra_f * lax.rsqrt(power_mean + EPS_POWER)).astype(jnp.bfloat16)


def lag_table(freq_count, lag_count):
    freq_ids = lax.broadcasted_iota(jnp.float32, (freq_count, lag_count), 0)
    lag_ids = lax.broadcasted_iota(jnp.float32, (freq_count, lag_count), 1) - lag_count // 2
    angles = 2.0 * jnp.pi / (2 * freq_count) * freq_ids * lag_ids
    norm_scale = 1.0 / jnp.sqrt(jnp.float32(freq_count))
    return jnp.concatenate(
        [jnp.cos(angles) * norm_scale, -jnp.sin(angles) * norm_scale], axis=0
    ).astype(jnp.bfloat16)


def cross_spectra(anchors, partners):
    half_width = anchors.shape[-1] // 2
    anchor_f = anchors.astype(jnp.float32)
    partner_f = partners.astype(jnp.float32)
    anchor_re = anchor_f[..., :half_width]
    anchor_im = anchor_f[..., half_width:]
    partner_re = partner_f[..., :half_width]
    partner_im = partner_f[..., half_width:]
    cross_re = anchor_re * partner_re + anchor_im * partner_im
    cross_im = anchor_im * partner_re - anchor_re * partner_im
    return jnp.concatenate([cross_re, cross_im], axis=-1).astype(jnp.bfloat16)


def window_gains(bins, gains):
    levels = lax.broadcasted_iota(jnp.int32, (bins.shape[0], gains.shape[0]), 1)
    return jnp.sum(jnp.where(bins[:, None] == levels, gains[None, :], jnp.float32(0.0)), axis=1)


def window_weights(lag_corr, ref_sum, window_gain):
    corr_f = lag_corr.astype(jnp.float32)
    inner_prod = jnp.mean(corr_f * ref_sum[:, None, :], axis=-1)
    corr_rms = jnp.sqrt(jnp.mean(corr_f * corr_f, axis=-1) + EPS_LAG)
    ref_rms = jnp.sqrt(jnp.mean(ref_sum * ref_sum, axis=-1) + EPS_LAG)
    coherence = inner_prod / (corr_rms * ref_rms[:, None])
    weights = window_gain[None, :] * jnp.exp(2.0 * coherence)
    numerator = jnp.sum(weights[:, :, None] * corr_f, axis=1)
    denominator = jnp.sum(weights, axis=1)
    return (numerator, denominator)


def select_rows(selector, rows):
    return jnp.einsum("sc,cwf->swf", selector, rows, preferred_element_type=jnp.bfloat16)


def butterfly_sum(value, axis):
    peers = lax.axis_size(axis)
    if peers & (peers - 1):
        return lax.psum(value, axis)
    step = 1
    while step < peers:
        pairs = [(i, i ^ step) for i in range(peers)]
        value = jax.tree.map(jnp.add, value, lax.ppermute(value, axis, pairs))
        step *= 2
    return value


def ring_exchange(up_rows, down_rows, axis):
    peers = lax.axis_size(axis)
    up = [(i, (i + 1) % peers) for i in range(peers)]
    down = [(j, i) for i, j in up]
    return lax.ppermute(up_rows, axis, up), lax.ppermute(down_rows, axis, down)


def gather_blocks(row, axis):
    peers = lax.axis_size(axis)
    if peers & (peers - 1):
        return lax.all_gather(row, axis)
    me = lax.axis_index(axis)
    acc = row[None]
    step = 1
    while step < peers:
        pairs = [(i, i ^ step) for i in range(peers)]
        got = lax.ppermute(acc, axis, pairs)
        acc = jnp.where((me & step) == 0, jnp.concatenate([acc, got]), jnp.concatenate([got, acc]))
        step *= 2
    return acc


def onehot(index, size, mask):
    return (index[:, None] == lax.broadcasted_iota(jnp.int32, (index.shape[0], size), 1)) & mask[:, None]


def window_weights_wm(corr_f, ref_sum, window_gain):
    inner_prod = jnp.mean(corr_f * ref_sum[None, :, :], axis=-1)
    corr_rms = jnp.sqrt(jnp.mean(corr_f * corr_f, axis=-1) + EPS_LAG)
    ref_rms = jnp.sqrt(jnp.mean(ref_sum * ref_sum, axis=-1) + EPS_LAG)
    coherence = inner_prod / (corr_rms * ref_rms[None, :])
    weights = window_gain[:, None] * jnp.exp(2.0 * coherence)
    numerator = jnp.sum(weights[:, :, None] * corr_f, axis=0)
    denominator = jnp.sum(weights, axis=0)
    return (numerator, denominator)


def block_needs(offs, parts, count, block_chans):
    live = lax.broadcasted_iota(jnp.int32, offs.shape, 0) < count
    hit = parts[:, None] == lax.broadcasted_iota(jnp.int32, (1, block_chans), 1)
    need_minus = jnp.any(hit & (live & (offs == 0))[:, None], axis=0)
    need_plus = jnp.any(hit & (live & (offs == 2))[:, None], axis=0)
    pos_minus = jnp.cumsum(need_minus, dtype=jnp.int32) - 1
    pos_plus = jnp.cumsum(need_plus, dtype=jnp.int32) - 1
    return need_minus, need_plus, pos_minus, pos_plus


def cross_kernel(spill_ref, anchor_ref, own_ref, sbf_ref, saf_ref, sbs_ref, sas_ref,
                 bf_ref, af_ref, bs_ref, as_ref, t_ref, corr_ref):
    wins = anchor_ref.shape[0]
    half = anchor_ref.shape[2] // 2
    t_re = t_ref[:half, :]
    t_im = t_ref[half:, :]
    sbf, saf = sbf_ref[...], saf_ref[...]
    for w in range(wins):
        part = (
            own_ref[w].astype(jnp.float32)
            + jnp.dot(sbf, bf_ref[w], preferred_element_type=jnp.float32)
            + jnp.dot(saf, af_ref[w], preferred_element_type=jnp.float32)
        )

        def add_spill(p):
            return (
                p
                + jnp.dot(sbs_ref[...], bs_ref[w], preferred_element_type=jnp.float32)
                + jnp.dot(sas_ref[...], as_ref[w], preferred_element_type=jnp.float32)
            )

        part = lax.cond(spill_ref[0] != 0, add_spill, lambda p: p, part)
        anc = anchor_ref[w].astype(jnp.float32)
        a_re, a_im = anc[:, :half], anc[:, half:]
        p_re, p_im = part[:, :half], part[:, half:]
        c_re = (a_re * p_re + a_im * p_im).astype(jnp.bfloat16)
        c_im = (a_im * p_re - a_re * p_im).astype(jnp.bfloat16)
        corr_ref[w] = jnp.dot(c_re, t_re, preferred_element_type=jnp.float32) + jnp.dot(
            c_im, t_im, preferred_element_type=jnp.float32
        )


def halo_cross(spill, chunk, wins, anchors, own, sels, bufs, transform):
    _, slots, width = anchors.shape
    lag_count = transform.shape[1]
    group = min(128, slots)
    row_spec = pl.BlockSpec((wins, group, width), lambda i, s: (chunk, i, 0))
    sel_specs = [pl.BlockSpec((group, sel.shape[1]), lambda i, s: (i, 0)) for sel in sels]
    buf_specs = [
        pl.BlockSpec((wins,) + buf.shape[1:], lambda i, s, c=(chunk if buf.shape[0] > wins else 0): (c, 0, 0)) for buf in bufs
    ]
    grid_spec = pltpu.PrefetchScalarGridSpec(
        num_scalar_prefetch=1,
        grid=(slots // group,),
        in_specs=[row_spec, row_spec] + sel_specs + buf_specs
        + [pl.BlockSpec(transform.shape, lambda i, s: (0, 0))],
        out_specs=pl.BlockSpec((wins, group, lag_count), lambda i, s: (0, i, 0)),
    )
    return pl.pallas_call(
        cross_kernel,
        grid_spec=grid_spec,
        out_shape=jax.ShapeDtypeStruct((wins, slots, lag_count), jnp.float32),
        compiler_params=pltpu.CompilerParams(vmem_limit_bytes=56 * 1024 * 1024),
    )(spill, anchors, own, *sels, *bufs, transform)


def local(spectra, pair_anchor, pair_offset, pair_partner, pair_count, window_bins, bin_gain):
    block_chans, local_wins, spec_width = spectra.shape
    pair_slots = pair_anchor.shape[0]
    fast_rows = (block_chans // 2 + 15) // 16 * 16
    spill_rows = block_chans - fast_rows

    blocks = lax.axis_size("chan")
    block = lax.axis_index("chan")
    table = jnp.concatenate([pair_offset, pair_partner, pair_count])
    tables = gather_blocks(table, "chan")
    table_before = tables[(block + blocks - 1) % blocks]
    table_after = tables[(block + 1) % blocks]

    def needs_of(tab):
        return block_needs(tab[:pair_slots], tab[pair_slots:2 * pair_slots], tab[2 * pair_slots], block_chans)

    own_minus, own_plus, own_pos_minus, own_pos_plus = needs_of(table)
    up_need, _, up_pos, _ = needs_of(table_after)
    _, down_need, _, down_pos = needs_of(table_before)
    all_needs = jax.vmap(needs_of)(tables)
    need_most = jnp.maximum(
        jnp.max(jnp.sum(all_needs[0], axis=1, dtype=jnp.int32)),
        jnp.max(jnp.sum(all_needs[1], axis=1, dtype=jnp.int32)),
    )

    def send_selector(need, pos, first, rows):
        return onehot(pos - first, rows, need).T.astype(jnp.bfloat16)

    def gather_rows(first, rows, source):
        up_rows = jnp.einsum("jc,cwf->wjf", send_selector(up_need, up_pos, first, rows), source,
                             preferred_element_type=jnp.bfloat16)
        down_rows = jnp.einsum("jc,cwf->wjf", send_selector(down_need, down_pos, first, rows), source,
                               preferred_element_type=jnp.bfloat16)
        up_rows, down_rows = whiten(up_rows), whiten(down_rows)
        return ring_exchange(up_rows, down_rows, "chan"), (up_rows, down_rows)

    chunks = 2 if local_wins % 2 == 0 else 1
    chunk_wins = local_wins // chunks
    fast_sent = [gather_rows(0, fast_rows, spectra[:, c * chunk_wins:(c + 1) * chunk_wins]) for c in range(chunks)]
    fast = [got for got, _ in fast_sent]
    spectra_late, _ = lax.optimization_barrier((spectra, [sent for _, sent in fast_sent]))
    white = whiten(spectra_late)
    spill = need_most > fast_rows

    def do_spill(_):
        got, _ = gather_rows(fast_rows, spill_rows, spectra)
        return got

    def no_spill(_):
        empty = jnp.zeros((local_wins, spill_rows, spec_width), jnp.bfloat16)
        return empty, empty

    before_spill, after_spill = lax.cond(spill, do_spill, no_spill, 0)

    transform = lag_table(spec_width // 2, LAG)
    lag_count = transform.shape[1]
    live_count = pair_count[0]
    slot_ids = lax.broadcasted_iota(jnp.int32, (pair_slots,), 0)
    live = slot_ids < live_count

    def pick(selector, rows):
        return jnp.einsum("sc,cwf->wsf", selector.astype(jnp.bfloat16), rows, preferred_element_type=jnp.bfloat16)

    anchors = pick(onehot(pair_anchor, block_chans, live), white)
    own = pick(onehot(pair_partner, block_chans, live & (pair_offset == 1)), white)
    own_hit = onehot(pair_partner, block_chans, live)
    before_row = jnp.sum(jnp.where(own_hit, own_pos_minus[None, :], 0), axis=1)
    after_row = jnp.sum(jnp.where(own_hit, own_pos_plus[None, :], 0), axis=1)
    use_before = live & (pair_offset == 0)
    use_after = live & (pair_offset == 2)
    sels = [
        onehot(before_row, fast_rows, use_before).astype(jnp.bfloat16),
        onehot(after_row, fast_rows, use_after).astype(jnp.bfloat16),
        onehot(before_row - fast_rows, spill_rows, use_before).astype(jnp.bfloat16),
        onehot(after_row - fast_rows, spill_rows, use_after).astype(jnp.bfloat16),
    ]
    corr_full = jnp.concatenate([
        halo_cross(
            spill.astype(jnp.int32).reshape(1), c, chunk_wins, anchors, own, sels,
            [fast[c][0], fast[c][1], before_spill, after_spill], transform,
        )
        for c in range(chunks)
    ])
    corr_all = lax.reduce_precision(corr_full, exponent_bits=8, mantissa_bits=7)
    running = jnp.sum(corr_full, axis=0)

    ref_sum = butterfly_sum(running, "win")
    norm_scale = jnp.sqrt(jnp.float32(local_wins * lax.axis_size("win")))
    ref_stack = jnp.where(live[:, None], ref_sum / norm_scale, 0.0)
    window_gain = window_gains(window_bins, bin_gain)
    numerator, denominator = window_weights_wm(corr_all, ref_sum, window_gain)
    numerator, denominator = butterfly_sum((numerator, denominator), "win")
    restack = jnp.where(live[:, None], norm_scale * numerator / denominator[:, None], 0.0)
    return (ref_stack, restack)


def solution(mesh):
    in_specs = (
        P(("days", "chan"), "win", None),
        P("chan"),
        P("chan"),
        P("chan"),
        P("chan"),
        P(("days", "win")),
        P(),
    )
    out_specs = (P(("days", "chan"), None), P(("days", "chan"), None))
    return jax.shard_map(local, mesh=mesh, in_specs=in_specs, out_specs=out_specs, check_vma=False)
```

```python
import jax
import jax.numpy as jnp
from jax import lax
from jax.experimental import pallas as pl
from jax.experimental.pallas import tpu as pltpu
from jax.sharding import PartitionSpec as P

LAG = 128


EPS_POWER = 1e-05
EPS_LAG = 1e-06


def whiten(spectra):
    spectra_f = spectra.astype(jnp.float32)
    power_mean = jnp.mean(spectra_f * spectra_f, axis=-1, keepdims=True)
    return (spectra_f * lax.rsqrt(power_mean + EPS_POWER)).astype(jnp.bfloat16)


def lag_table(freq_count, lag_count):
    freq_ids = lax.broadcasted_iota(jnp.float32, (freq_count, lag_count), 0)
    lag_ids = lax.broadcasted_iota(jnp.float32, (freq_count, lag_count), 1) - lag_count // 2
    angles = 2.0 * jnp.pi / (2 * freq_count) * freq_ids * lag_ids
    norm_scale = 1.0 / jnp.sqrt(jnp.float32(freq_count))
    return jnp.concatenate(
        [jnp.cos(angles) * norm_scale, -jnp.sin(angles) * norm_scale], axis=0
    ).astype(jnp.bfloat16)


def cross_spectra(anchors, partners):
    half_width = anchors.shape[-1] // 2
    anchor_f = anchors.astype(jnp.float32)
    partner_f = partners.astype(jnp.float32)
    anchor_re = anchor_f[..., :half_width]
    anchor_im = anchor_f[..., half_width:]
    partner_re = partner_f[..., :half_width]
    partner_im = partner_f[..., half_width:]
    cross_re = anchor_re * partner_re + anchor_im * partner_im
    cross_im = anchor_im * partner_re - anchor_re * partner_im
    return jnp.concatenate([cross_re, cross_im], axis=-1).astype(jnp.bfloat16)


def window_gains(bins, gains):
    levels = lax.broadcasted_iota(jnp.int32, (bins.shape[0], gains.shape[0]), 1)
    return jnp.sum(jnp.where(bins[:, None] == levels, gains[None, :], jnp.float32(0.0)), axis=1)


def window_weights(lag_corr, ref_sum, window_gain):
    corr_f = lag_corr.astype(jnp.float32)
    inner_prod = jnp.mean(corr_f * ref_sum[:, None, :], axis=-1)
    corr_rms = jnp.sqrt(jnp.mean(corr_f * corr_f, axis=-1) + EPS_LAG)
    ref_rms = jnp.sqrt(jnp.mean(ref_sum * ref_sum, axis=-1) + EPS_LAG)
    coherence = inner_prod / (corr_rms * ref_rms[:, None])
    weights = window_gain[None, :] * jnp.exp(2.0 * coherence)
    numerator = jnp.sum(weights[:, :, None] * corr_f, axis=1)
    denominator = jnp.sum(weights, axis=1)
    return (numerator, denominator)


def select_rows(selector, rows):
    return jnp.einsum("sc,cwf->swf", selector, rows, preferred_element_type=jnp.bfloat16)


def butterfly_sum(value, axis):
    peers = lax.axis_size(axis)
    if peers & (peers - 1):
        return lax.psum(value, axis)
    step = 1
    while step < peers:
        pairs = [(i, i ^ step) for i in range(peers)]
        value = jax.tree.map(jnp.add, value, lax.ppermute(value, axis, pairs))
        step *= 2
    return value


def ring_exchange(up_rows, down_rows, axis):
    peers = lax.axis_size(axis)
    up = [(i, (i + 1) % peers) for i in range(peers)]
    down = [(j, i) for i, j in up]
    return lax.ppermute(up_rows, axis, up), lax.ppermute(down_rows, axis, down)


def gather_blocks(row, axis):
    peers = lax.axis_size(axis)
    if peers & (peers - 1):
        return lax.all_gather(row, axis)
    me = lax.axis_index(axis)
    acc = row[None]
    step = 1
    while step < peers:
        pairs = [(i, i ^ step) for i in range(peers)]
        got = lax.ppermute(acc, axis, pairs)
        acc = jnp.where((me & step) == 0, jnp.concatenate([acc, got]), jnp.concatenate([got, acc]))
        step *= 2
    return acc


def onehot(index, size, mask):
    return (index[:, None] == lax.broadcasted_iota(jnp.int32, (index.shape[0], size), 1)) & mask[:, None]


def window_weights_wm(corr_f, ref_sum, window_gain):
    inner_prod = jnp.mean(corr_f * ref_sum[None, :, :], axis=-1)
    corr_rms = jnp.sqrt(jnp.mean(corr_f * corr_f, axis=-1) + EPS_LAG)
    ref_rms = jnp.sqrt(jnp.mean(ref_sum * ref_sum, axis=-1) + EPS_LAG)
    coherence = inner_prod / (corr_rms * ref_rms[None, :])
    weights = window_gain[:, None] * jnp.exp(2.0 * coherence)
    numerator = jnp.sum(weights[:, :, None] * corr_f, axis=0)
    denominator = jnp.sum(weights, axis=0)
    return (numerator, denominator)


def block_needs(offs, parts, count, block_chans):
    live = lax.broadcasted_iota(jnp.int32, offs.shape, 0) < count
    hit = parts[:, None] == lax.broadcasted_iota(jnp.int32, (1, block_chans), 1)
    need_minus = jnp.any(hit & (live & (offs == 0))[:, None], axis=0)
    need_plus = jnp.any(hit & (live & (offs == 2))[:, None], axis=0)
    pos_minus = jnp.cumsum(need_minus, dtype=jnp.int32) - 1
    pos_plus = jnp.cumsum(need_plus, dtype=jnp.int32) - 1
    return need_minus, need_plus, pos_minus, pos_plus


def cross_kernel(anchor_ref, own_ref, sbf_ref, saf_ref, bf_ref, af_ref, t_ref, corr_ref):
    wins = anchor_ref.shape[0]
    half = anchor_ref.shape[2] // 2
    t_re = t_ref[:half, :]
    t_im = t_ref[half:, :]
    sbf, saf = sbf_ref[...], saf_ref[...]
    for w in range(wins):
        part = (
            own_ref[w].astype(jnp.float32)
            + jnp.dot(sbf, bf_ref[w], preferred_element_type=jnp.float32)
            + jnp.dot(saf, af_ref[w], preferred_element_type=jnp.float32)
        )
        anc = anchor_ref[w].astype(jnp.float32)
        a_re, a_im = anc[:, :half], anc[:, half:]
        p_re, p_im = part[:, :half], part[:, half:]
        c_re = (a_re * p_re + a_im * p_im).astype(jnp.bfloat16)
        c_im = (a_im * p_re - a_re * p_im).astype(jnp.bfloat16)
        corr_ref[w] = jnp.dot(c_re, t_re, preferred_element_type=jnp.float32) + jnp.dot(
            c_im, t_im, preferred_element_type=jnp.float32
        )


def halo_cross(chunk, wins, anchors, own, sels, bufs, transform):
    _, slots, width = anchors.shape
    lag_count = transform.shape[1]
    group = min(128, slots)
    row_spec = pl.BlockSpec((wins, group, width), lambda i: (chunk, i, 0))
    sel_specs = [pl.BlockSpec((group, sel.shape[1]), lambda i: (i, 0)) for sel in sels]
    buf_specs = [pl.BlockSpec((wins,) + buf.shape[1:], lambda i: (0, 0, 0)) for buf in bufs]
    return pl.pallas_call(
        cross_kernel,
        grid=(slots // group,),
        in_specs=[row_spec, row_spec] + sel_specs + buf_specs + [pl.BlockSpec(transform.shape, lambda i: (0, 0))],
        out_specs=pl.BlockSpec((wins, group, lag_count), lambda i: (0, i, 0)),
        out_shape=jax.ShapeDtypeStruct((wins, slots, lag_count), jnp.float32),
        compiler_params=pltpu.CompilerParams(vmem_limit_bytes=56 * 1024 * 1024),
    )(anchors, own, *sels, *bufs, transform)


def local(spectra, pair_anchor, pair_offset, pair_partner, pair_count, window_bins, bin_gain):
    block_chans, local_wins, spec_width = spectra.shape
    pair_slots = pair_anchor.shape[0]
    fast_rows = (block_chans // 2 + 15) // 16 * 16
    spill_rows = block_chans - fast_rows

    blocks = lax.axis_size("chan")
    block = lax.axis_index("chan")
    table = jnp.concatenate([pair_offset, pair_partner, pair_count])
    tables = gather_blocks(table, "chan")
    table_before = tables[(block + blocks - 1) % blocks]
    table_after = tables[(block + 1) % blocks]

    def needs_of(tab):
        return block_needs(tab[:pair_slots], tab[pair_slots:2 * pair_slots], tab[2 * pair_slots], block_chans)

    own_minus, own_plus, own_pos_minus, own_pos_plus = needs_of(table)
    up_need, _, up_pos, _ = needs_of(table_after)
    _, down_need, _, down_pos = needs_of(table_before)
    all_needs = jax.vmap(needs_of)(tables)
    need_most = jnp.maximum(
        jnp.max(jnp.sum(all_needs[0], axis=1, dtype=jnp.int32)),
        jnp.max(jnp.sum(all_needs[1], axis=1, dtype=jnp.int32)),
    )

    def send_selector(need, pos, first, rows):
        return onehot(pos - first, rows, need).T.astype(jnp.bfloat16)

    def gather_rows(first, rows, source):
        up_rows = jnp.einsum("jc,cwf->wjf", send_selector(up_need, up_pos, first, rows), source,
                             preferred_element_type=jnp.bfloat16)
        down_rows = jnp.einsum("jc,cwf->wjf", send_selector(down_need, down_pos, first, rows), source,
                               preferred_element_type=jnp.bfloat16)
        up_rows, down_rows = whiten(up_rows), whiten(down_rows)
        return ring_exchange(up_rows, down_rows, "chan"), (up_rows, down_rows)

    chunks = 2 if local_wins % 2 == 0 else 1
    chunk_wins = local_wins // chunks
    fast_sent = [gather_rows(0, fast_rows, spectra[:, c * chunk_wins:(c + 1) * chunk_wins]) for c in range(chunks)]
    fast = [got for got, _ in fast_sent]
    spectra_late, _ = lax.optimization_barrier((spectra, [sent for _, sent in fast_sent]))
    white = whiten(spectra_late)
    spill = need_most > fast_rows

    transform = lag_table(spec_width // 2, LAG)
    lag_count = transform.shape[1]
    live_count = pair_count[0]
    slot_ids = lax.broadcasted_iota(jnp.int32, (pair_slots,), 0)
    live = slot_ids < live_count

    def pick(selector, rows):
        return jnp.einsum("sc,cwf->wsf", selector.astype(jnp.bfloat16), rows, preferred_element_type=jnp.bfloat16)

    anchors = pick(onehot(pair_anchor, block_chans, live), white)
    own = pick(onehot(pair_partner, block_chans, live & (pair_offset == 1)), white)
    own_hit = onehot(pair_partner, block_chans, live)
    before_row = jnp.sum(jnp.where(own_hit, own_pos_minus[None, :], 0), axis=1)
    after_row = jnp.sum(jnp.where(own_hit, own_pos_plus[None, :], 0), axis=1)
    use_before = live & (pair_offset == 0)
    use_after = live & (pair_offset == 2)
    sels = [
        onehot(before_row, fast_rows, use_before).astype(jnp.bfloat16),
        onehot(after_row, fast_rows, use_after).astype(jnp.bfloat16),
    ]
    corr_full = jnp.concatenate([
        halo_cross(c, chunk_wins, anchors, own, sels, [fast[c][0], fast[c][1]], transform)
        for c in range(chunks)
    ])

    def add_spill(corr):
        (got_before, got_after), _ = gather_rows(fast_rows, spill_rows, spectra)
        spill_sels = [
            onehot(before_row - fast_rows, spill_rows, use_before).astype(jnp.bfloat16),
            onehot(after_row - fast_rows, spill_rows, use_after).astype(jnp.bfloat16),
        ]
        zero_own = jnp.zeros_like(own)
        extra = jnp.concatenate([
            halo_cross(c, chunk_wins, anchors, zero_own, spill_sels,
                       [got_before[c * chunk_wins:(c + 1) * chunk_wins], got_after[c * chunk_wins:(c + 1) * chunk_wins]],
                       transform)
            for c in range(chunks)
        ])
        return corr + extra

    corr_full = lax.cond(spill, add_spill, lambda corr: corr, corr_full)
    corr_all = lax.reduce_precision(corr_full, exponent_bits=8, mantissa_bits=7)
    running = jnp.sum(corr_full, axis=0)

    ref_sum = butterfly_sum(running, "win")
    norm_scale = jnp.sqrt(jnp.float32(local_wins * lax.axis_size("win")))
    ref_stack = jnp.where(live[:, None], ref_sum / norm_scale, 0.0)
    window_gain = window_gains(window_bins, bin_gain)
    numerator, denominator = window_weights_wm(corr_all, ref_sum, window_gain)
    numerator, denominator = butterfly_sum((numerator, denominator), "win")
    restack = jnp.where(live[:, None], norm_scale * numerator / denominator[:, None], 0.0)
    return (ref_stack, restack)


def solution(mesh):
    in_specs = (
        P(("days", "chan"), "win", None),
        P("chan"),
        P("chan"),
        P("chan"),
        P("chan"),
        P(("days", "win")),
        P(),
    )
    out_specs = (P(("days", "chan"), None), P(("days", "chan"), None))
    return jax.shard_map(local, mesh=mesh, in_specs=in_specs, out_specs=out_specs, check_vma=False)
```

```python
import jax
import jax.numpy as jnp
from jax import lax
from jax.experimental import pallas as pl
from jax.experimental.pallas import tpu as pltpu
from jax.sharding import PartitionSpec as P

LAG = 128


EPS_POWER = 1e-05
EPS_LAG = 1e-06


def whiten(spectra):
    spectra_f = spectra.astype(jnp.float32)
    power_mean = jnp.mean(spectra_f * spectra_f, axis=-1, keepdims=True)
    return (spectra_f * lax.rsqrt(power_mean + EPS_POWER)).astype(jnp.bfloat16)


def lag_table(freq_count, lag_count):
    freq_ids = lax.broadcasted_iota(jnp.float32, (freq_count, lag_count), 0)
    lag_ids = lax.broadcasted_iota(jnp.float32, (freq_count, lag_count), 1) - lag_count // 2
    angles = 2.0 * jnp.pi / (2 * freq_count) * freq_ids * lag_ids
    norm_scale = 1.0 / jnp.sqrt(jnp.float32(freq_count))
    return jnp.concatenate(
        [jnp.cos(angles) * norm_scale, -jnp.sin(angles) * norm_scale], axis=0
    ).astype(jnp.bfloat16)


def cross_spectra(anchors, partners):
    half_width = anchors.shape[-1] // 2
    anchor_f = anchors.astype(jnp.float32)
    partner_f = partners.astype(jnp.float32)
    anchor_re = anchor_f[..., :half_width]
    anchor_im = anchor_f[..., half_width:]
    partner_re = partner_f[..., :half_width]
    partner_im = partner_f[..., half_width:]
    cross_re = anchor_re * partner_re + anchor_im * partner_im
    cross_im = anchor_im * partner_re - anchor_re * partner_im
    return jnp.concatenate([cross_re, cross_im], axis=-1).astype(jnp.bfloat16)


def window_gains(bins, gains):
    levels = lax.broadcasted_iota(jnp.int32, (bins.shape[0], gains.shape[0]), 1)
    return jnp.sum(jnp.where(bins[:, None] == levels, gains[None, :], jnp.float32(0.0)), axis=1)


def window_weights(lag_corr, ref_sum, window_gain):
    corr_f = lag_corr.astype(jnp.float32)
    inner_prod = jnp.mean(corr_f * ref_sum[:, None, :], axis=-1)
    corr_rms = jnp.sqrt(jnp.mean(corr_f * corr_f, axis=-1) + EPS_LAG)
    ref_rms = jnp.sqrt(jnp.mean(ref_sum * ref_sum, axis=-1) + EPS_LAG)
    coherence = inner_prod / (corr_rms * ref_rms[:, None])
    weights = window_gain[None, :] * jnp.exp(2.0 * coherence)
    numerator = jnp.sum(weights[:, :, None] * corr_f, axis=1)
    denominator = jnp.sum(weights, axis=1)
    return (numerator, denominator)


def select_rows(selector, rows):
    return jnp.einsum("sc,cwf->swf", selector, rows, preferred_element_type=jnp.bfloat16)


def butterfly_sum(value, axis):
    peers = lax.axis_size(axis)
    if peers & (peers - 1):
        return lax.psum(value, axis)
    step = 1
    while step < peers:
        pairs = [(i, i ^ step) for i in range(peers)]
        value = jax.tree.map(jnp.add, value, lax.ppermute(value, axis, pairs))
        step *= 2
    return value


def ring_exchange(up_rows, down_rows, axis):
    peers = lax.axis_size(axis)
    up = [(i, (i + 1) % peers) for i in range(peers)]
    down = [(j, i) for i, j in up]
    return lax.ppermute(up_rows, axis, up), lax.ppermute(down_rows, axis, down)


def gather_blocks(row, axis):
    peers = lax.axis_size(axis)
    if peers & (peers - 1):
        return lax.all_gather(row, axis)
    me = lax.axis_index(axis)
    acc = row[None]
    step = 1
    while step < peers:
        pairs = [(i, i ^ step) for i in range(peers)]
        got = lax.ppermute(acc, axis, pairs)
        acc = jnp.where((me & step) == 0, jnp.concatenate([acc, got]), jnp.concatenate([got, acc]))
        step *= 2
    return acc


def onehot(index, size, mask):
    return (index[:, None] == lax.broadcasted_iota(jnp.int32, (index.shape[0], size), 1)) & mask[:, None]


def window_weights_wm(corr_f, ref_sum, window_gain):
    inner_prod = jnp.mean(corr_f * ref_sum[None, :, :], axis=-1)
    corr_rms = jnp.sqrt(jnp.mean(corr_f * corr_f, axis=-1) + EPS_LAG)
    ref_rms = jnp.sqrt(jnp.mean(ref_sum * ref_sum, axis=-1) + EPS_LAG)
    coherence = inner_prod / (corr_rms * ref_rms[None, :])
    weights = window_gain[:, None] * jnp.exp(2.0 * coherence)
    numerator = jnp.sum(weights[:, :, None] * corr_f, axis=0)
    denominator = jnp.sum(weights, axis=0)
    return (numerator, denominator)


def block_needs(offs, parts, count, block_chans):
    live = lax.broadcasted_iota(jnp.int32, offs.shape, 0) < count
    hit = parts[:, None] == lax.broadcasted_iota(jnp.int32, (1, block_chans), 1)
    need_minus = jnp.any(hit & (live & (offs == 0))[:, None], axis=0)
    need_plus = jnp.any(hit & (live & (offs == 2))[:, None], axis=0)
    pos_minus = jnp.cumsum(need_minus, dtype=jnp.int32) - 1
    pos_plus = jnp.cumsum(need_plus, dtype=jnp.int32) - 1
    return need_minus, need_plus, pos_minus, pos_plus


def cross_kernel(anchor_ref, own_ref, sbf_ref, saf_ref, bf_ref, af_ref, t_ref, corr_ref):
    wins = anchor_ref.shape[0]
    half = anchor_ref.shape[2] // 2
    t_re = t_ref[:half, :]
    t_im = t_ref[half:, :]
    sbf, saf = sbf_ref[...], saf_ref[...]
    for w in range(wins):
        part = (
            own_ref[w].astype(jnp.float32)
            + jnp.dot(sbf, bf_ref[w], preferred_element_type=jnp.float32)
            + jnp.dot(saf, af_ref[w], preferred_element_type=jnp.float32)
        )
        anc = anchor_ref[w].astype(jnp.float32)
        a_re, a_im = anc[:, :half], anc[:, half:]
        p_re, p_im = part[:, :half], part[:, half:]
        c_re = (a_re * p_re + a_im * p_im).astype(jnp.bfloat16)
        c_im = (a_im * p_re - a_re * p_im).astype(jnp.bfloat16)
        corr_ref[w] = jnp.dot(c_re, t_re, preferred_element_type=jnp.float32) + jnp.dot(
            c_im, t_im, preferred_element_type=jnp.float32
        )


def halo_cross(chunk, wins, anchors, own, sels, bufs, transform):
    _, slots, width = anchors.shape
    lag_count = transform.shape[1]
    group = min(128, slots)
    row_spec = pl.BlockSpec((wins, group, width), lambda i: (chunk, i, 0))
    sel_specs = [pl.BlockSpec((group, sel.shape[1]), lambda i: (i, 0)) for sel in sels]
    buf_specs = [pl.BlockSpec((wins,) + buf.shape[1:], lambda i: (0, 0, 0)) for buf in bufs]
    return pl.pallas_call(
        cross_kernel,
        grid=(slots // group,),
        in_specs=[row_spec, row_spec] + sel_specs + buf_specs + [pl.BlockSpec(transform.shape, lambda i: (0, 0))],
        out_specs=pl.BlockSpec((wins, group, lag_count), lambda i: (0, i, 0)),
        out_shape=jax.ShapeDtypeStruct((wins, slots, lag_count), jnp.float32),
        compiler_params=pltpu.CompilerParams(vmem_limit_bytes=56 * 1024 * 1024),
    )(anchors, own, *sels, *bufs, transform)


def local(spectra, pair_anchor, pair_offset, pair_partner, pair_count, window_bins, bin_gain):
    block_chans, local_wins, spec_width = spectra.shape
    pair_slots = pair_anchor.shape[0]
    fast_rows = (block_chans // 2 + 15) // 16 * 16
    spill_rows = block_chans - fast_rows

    blocks = lax.axis_size("chan")
    block = lax.axis_index("chan")
    table = jnp.concatenate([pair_offset, pair_partner, pair_count])
    tables = gather_blocks(table, "chan")
    table_before = tables[(block + blocks - 1) % blocks]
    table_after = tables[(block + 1) % blocks]

    def needs_of(tab):
        return block_needs(tab[:pair_slots], tab[pair_slots:2 * pair_slots], tab[2 * pair_slots], block_chans)

    own_minus, own_plus, own_pos_minus, own_pos_plus = needs_of(table)
    up_need, _, up_pos, _ = needs_of(table_after)
    _, down_need, _, down_pos = needs_of(table_before)
    all_needs = jax.vmap(needs_of)(tables)
    need_most = jnp.maximum(
        jnp.max(jnp.sum(all_needs[0], axis=1, dtype=jnp.int32)),
        jnp.max(jnp.sum(all_needs[1], axis=1, dtype=jnp.int32)),
    )

    def send_selector(need, pos, first, rows):
        return onehot(pos - first, rows, need).T.astype(jnp.bfloat16)

    def gather_rows(first, rows, source):
        up_rows = jnp.einsum("jc,cwf->wjf", send_selector(up_need, up_pos, first, rows), source,
                             preferred_element_type=jnp.bfloat16)
        down_rows = jnp.einsum("jc,cwf->wjf", send_selector(down_need, down_pos, first, rows), source,
                               preferred_element_type=jnp.bfloat16)
        up_rows, down_rows = whiten(up_rows), whiten(down_rows)
        return ring_exchange(up_rows, down_rows, "chan"), (up_rows, down_rows)

    chunks = 2 if local_wins % 2 == 0 else 1
    chunk_wins = local_wins // chunks
    fast_sent = [gather_rows(0, fast_rows, spectra[:, c * chunk_wins:(c + 1) * chunk_wins]) for c in range(chunks)]
    fast = [got for got, _ in fast_sent]
    spectra_late, _ = lax.optimization_barrier((spectra, [sent for _, sent in fast_sent]))
    white = whiten(spectra_late)
    spill = need_most > fast_rows

    transform = lag_table(spec_width // 2, LAG)
    lag_count = transform.shape[1]
    live_count = pair_count[0]
    slot_ids = lax.broadcasted_iota(jnp.int32, (pair_slots,), 0)
    live = slot_ids < live_count

    def pick(selector, rows):
        return jnp.einsum("sc,cwf->wsf", selector.astype(jnp.bfloat16), rows, preferred_element_type=jnp.bfloat16)

    anchors = pick(onehot(pair_anchor, block_chans, live), white)
    own = pick(onehot(pair_partner, block_chans, live & (pair_offset == 1)), white)
    own_hit = onehot(pair_partner, block_chans, live)
    before_row = jnp.sum(jnp.where(own_hit, own_pos_minus[None, :], 0), axis=1)
    after_row = jnp.sum(jnp.where(own_hit, own_pos_plus[None, :], 0), axis=1)
    use_before = live & (pair_offset == 0)
    use_after = live & (pair_offset == 2)
    sels = [
        onehot(before_row, fast_rows, use_before).astype(jnp.bfloat16),
        onehot(after_row, fast_rows, use_after).astype(jnp.bfloat16),
    ]
    corr_full = jnp.concatenate([
        halo_cross(c, chunk_wins, anchors, own, sels, [fast[c][0], fast[c][1]], transform)
        for c in range(chunks)
    ])

    def spill_extra(_):
        (got_before, got_after), _ = gather_rows(fast_rows, spill_rows, spectra)
        spill_sels = [
            onehot(before_row - fast_rows, spill_rows, use_before).astype(jnp.bfloat16),
            onehot(after_row - fast_rows, spill_rows, use_after).astype(jnp.bfloat16),
        ]
        zero_own = jnp.zeros_like(own)
        extra = jnp.concatenate([
            halo_cross(c, chunk_wins, anchors, zero_own, spill_sels,
                       [got_before[c * chunk_wins:(c + 1) * chunk_wins], got_after[c * chunk_wins:(c + 1) * chunk_wins]],
                       transform)
            for c in range(chunks)
        ])
        return extra

    def no_extra(_):
        return jnp.zeros((local_wins, pair_slots, lag_count), jnp.float32)

    spill_late, _ = lax.optimization_barrier((spill, fast[0]))
    corr_full = corr_full + lax.cond(spill_late, spill_extra, no_extra, 0)
    corr_all = lax.reduce_precision(corr_full, exponent_bits=8, mantissa_bits=7)
    running = jnp.sum(corr_full, axis=0)

    ref_sum = butterfly_sum(running, "win")
    norm_scale = jnp.sqrt(jnp.float32(local_wins * lax.axis_size("win")))
    ref_stack = jnp.where(live[:, None], ref_sum / norm_scale, 0.0)
    window_gain = window_gains(window_bins, bin_gain)
    numerator, denominator = window_weights_wm(corr_all, ref_sum, window_gain)
    numerator, denominator = butterfly_sum((numerator, denominator), "win")
    restack = jnp.where(live[:, None], norm_scale * numerator / denominator[:, None], 0.0)
    return (ref_stack, restack)


def solution(mesh):
    in_specs = (
        P(("days", "chan"), "win", None),
        P("chan"),
        P("chan"),
        P("chan"),
        P("chan"),
        P(("days", "win")),
        P(),
    )
    out_specs = (P(("days", "chan"), None), P(("days", "chan"), None))
    return jax.shard_map(local, mesh=mesh, in_specs=in_specs, out_specs=out_specs, check_vma=False)
```

```python
import jax
import jax.numpy as jnp
from jax import lax
from jax.experimental import pallas as pl
from jax.experimental.pallas import tpu as pltpu
from jax.sharding import PartitionSpec as P

LAG = 128


EPS_POWER = 1e-05
EPS_LAG = 1e-06


def whiten(spectra):
    spectra_f = spectra.astype(jnp.float32)
    power_mean = jnp.mean(spectra_f * spectra_f, axis=-1, keepdims=True)
    return (spectra_f * lax.rsqrt(power_mean + EPS_POWER)).astype(jnp.bfloat16)


def lag_table(freq_count, lag_count):
    freq_ids = lax.broadcasted_iota(jnp.float32, (freq_count, lag_count), 0)
    lag_ids = lax.broadcasted_iota(jnp.float32, (freq_count, lag_count), 1) - lag_count // 2
    angles = 2.0 * jnp.pi / (2 * freq_count) * freq_ids * lag_ids
    norm_scale = 1.0 / jnp.sqrt(jnp.float32(freq_count))
    return jnp.concatenate(
        [jnp.cos(angles) * norm_scale, -jnp.sin(angles) * norm_scale], axis=0
    ).astype(jnp.bfloat16)


def cross_spectra(anchors, partners):
    half_width = anchors.shape[-1] // 2
    anchor_f = anchors.astype(jnp.float32)
    partner_f = partners.astype(jnp.float32)
    anchor_re = anchor_f[..., :half_width]
    anchor_im = anchor_f[..., half_width:]
    partner_re = partner_f[..., :half_width]
    partner_im = partner_f[..., half_width:]
    cross_re = anchor_re * partner_re + anchor_im * partner_im
    cross_im = anchor_im * partner_re - anchor_re * partner_im
    return jnp.concatenate([cross_re, cross_im], axis=-1).astype(jnp.bfloat16)


def window_gains(bins, gains):
    levels = lax.broadcasted_iota(jnp.int32, (bins.shape[0], gains.shape[0]), 1)
    return jnp.sum(jnp.where(bins[:, None] == levels, gains[None, :], jnp.float32(0.0)), axis=1)


def window_weights(lag_corr, ref_sum, window_gain):
    corr_f = lag_corr.astype(jnp.float32)
    inner_prod = jnp.mean(corr_f * ref_sum[:, None, :], axis=-1)
    corr_rms = jnp.sqrt(jnp.mean(corr_f * corr_f, axis=-1) + EPS_LAG)
    ref_rms = jnp.sqrt(jnp.mean(ref_sum * ref_sum, axis=-1) + EPS_LAG)
    coherence = inner_prod / (corr_rms * ref_rms[:, None])
    weights = window_gain[None, :] * jnp.exp(2.0 * coherence)
    numerator = jnp.sum(weights[:, :, None] * corr_f, axis=1)
    denominator = jnp.sum(weights, axis=1)
    return (numerator, denominator)


def select_rows(selector, rows):
    return jnp.einsum("sc,cwf->swf", selector, rows, preferred_element_type=jnp.bfloat16)


def butterfly_sum(value, axis):
    peers = lax.axis_size(axis)
    if peers & (peers - 1):
        return lax.psum(value, axis)
    step = 1
    while step < peers:
        pairs = [(i, i ^ step) for i in range(peers)]
        value = jax.tree.map(jnp.add, value, lax.ppermute(value, axis, pairs))
        step *= 2
    return value


def ring_exchange(up_rows, down_rows, axis):
    peers = lax.axis_size(axis)
    up = [(i, (i + 1) % peers) for i in range(peers)]
    down = [(j, i) for i, j in up]
    return lax.ppermute(up_rows, axis, up), lax.ppermute(down_rows, axis, down)


def gather_blocks(row, axis):
    peers = lax.axis_size(axis)
    if peers & (peers - 1):
        return lax.all_gather(row, axis)
    me = lax.axis_index(axis)
    acc = row[None]
    step = 1
    while step < peers:
        pairs = [(i, i ^ step) for i in range(peers)]
        got = lax.ppermute(acc, axis, pairs)
        acc = jnp.where((me & step) == 0, jnp.concatenate([acc, got]), jnp.concatenate([got, acc]))
        step *= 2
    return acc


def onehot(index, size, mask):
    return (index[:, None] == lax.broadcasted_iota(jnp.int32, (index.shape[0], size), 1)) & mask[:, None]


def window_weights_wm(corr_f, ref_sum, window_gain):
    inner_prod = jnp.mean(corr_f * ref_sum[None, :, :], axis=-1)
    corr_rms = jnp.sqrt(jnp.mean(corr_f * corr_f, axis=-1) + EPS_LAG)
    ref_rms = jnp.sqrt(jnp.mean(ref_sum * ref_sum, axis=-1) + EPS_LAG)
    coherence = inner_prod / (corr_rms * ref_rms[None, :])
    weights = window_gain[:, None] * jnp.exp(2.0 * coherence)
    numerator = jnp.sum(weights[:, :, None] * corr_f, axis=0)
    denominator = jnp.sum(weights, axis=0)
    return (numerator, denominator)


def block_needs(offs, parts, count, block_chans):
    live = lax.broadcasted_iota(jnp.int32, offs.shape, 0) < count
    hit = parts[:, None] == lax.broadcasted_iota(jnp.int32, (1, block_chans), 1)
    need_minus = jnp.any(hit & (live & (offs == 0))[:, None], axis=0)
    need_plus = jnp.any(hit & (live & (offs == 2))[:, None], axis=0)
    pos_minus = jnp.cumsum(need_minus, dtype=jnp.int32) - 1
    pos_plus = jnp.cumsum(need_plus, dtype=jnp.int32) - 1
    return need_minus, need_plus, pos_minus, pos_plus


def cross_kernel(anchor_ref, own_ref, sbf_ref, saf_ref, bf_ref, af_ref, t_ref, corr_ref):
    wins = anchor_ref.shape[0]
    half = anchor_ref.shape[2] // 2
    t_re = t_ref[:half, :]
    t_im = t_ref[half:, :]
    sbf, saf = sbf_ref[...], saf_ref[...]
    for w in range(wins):
        part = (
            own_ref[w].astype(jnp.float32)
            + jnp.dot(sbf, bf_ref[w], preferred_element_type=jnp.float32)
            + jnp.dot(saf, af_ref[w], preferred_element_type=jnp.float32)
        )
        anc = anchor_ref[w].astype(jnp.float32)
        a_re, a_im = anc[:, :half], anc[:, half:]
        p_re, p_im = part[:, :half], part[:, half:]
        c_re = (a_re * p_re + a_im * p_im).astype(jnp.bfloat16)
        c_im = (a_im * p_re - a_re * p_im).astype(jnp.bfloat16)
        corr_ref[w] = jnp.dot(c_re, t_re, preferred_element_type=jnp.float32) + jnp.dot(
            c_im, t_im, preferred_element_type=jnp.float32
        )


def halo_cross(first_win, wins, anchors, own, sels, bufs, transform):
    _, slots, width = anchors.shape
    lag_count = transform.shape[1]
    group = min(128, slots)
    row_spec = pl.BlockSpec((wins, group, width), lambda i: (first_win // wins, i, 0))
    sel_specs = [pl.BlockSpec((group, sel.shape[1]), lambda i: (i, 0)) for sel in sels]
    buf_specs = [pl.BlockSpec((wins,) + buf.shape[1:], lambda i: (0, 0, 0)) for buf in bufs]
    return pl.pallas_call(
        cross_kernel,
        grid=(slots // group,),
        in_specs=[row_spec, row_spec] + sel_specs + buf_specs + [pl.BlockSpec(transform.shape, lambda i: (0, 0))],
        out_specs=pl.BlockSpec((wins, group, lag_count), lambda i: (0, i, 0)),
        out_shape=jax.ShapeDtypeStruct((wins, slots, lag_count), jnp.float32),
        compiler_params=pltpu.CompilerParams(vmem_limit_bytes=56 * 1024 * 1024),
    )(anchors, own, *sels, *bufs, transform)


def local(spectra, pair_anchor, pair_offset, pair_partner, pair_count, window_bins, bin_gain):
    block_chans, local_wins, spec_width = spectra.shape
    pair_slots = pair_anchor.shape[0]
    fast_rows = (block_chans // 2 + 15) // 16 * 16
    spill_rows = block_chans - fast_rows

    blocks = lax.axis_size("chan")
    block = lax.axis_index("chan")
    table = jnp.concatenate([pair_offset, pair_partner, pair_count])
    tables = gather_blocks(table, "chan")
    table_before = tables[(block + blocks - 1) % blocks]
    table_after = tables[(block + 1) % blocks]

    def needs_of(tab):
        return block_needs(tab[:pair_slots], tab[pair_slots:2 * pair_slots], tab[2 * pair_slots], block_chans)

    own_minus, own_plus, own_pos_minus, own_pos_plus = needs_of(table)
    up_need, _, up_pos, _ = needs_of(table_after)
    _, down_need, _, down_pos = needs_of(table_before)
    all_needs = jax.vmap(needs_of)(tables)
    need_most = jnp.maximum(
        jnp.max(jnp.sum(all_needs[0], axis=1, dtype=jnp.int32)),
        jnp.max(jnp.sum(all_needs[1], axis=1, dtype=jnp.int32)),
    )

    def send_selector(need, pos, first, rows):
        return onehot(pos - first, rows, need).T.astype(jnp.bfloat16)

    def gather_rows(first, rows, source):
        up_rows = jnp.einsum("jc,cwf->wjf", send_selector(up_need, up_pos, first, rows), source,
                             preferred_element_type=jnp.bfloat16)
        down_rows = jnp.einsum("jc,cwf->wjf", send_selector(down_need, down_pos, first, rows), source,
                               preferred_element_type=jnp.bfloat16)
        up_rows, down_rows = whiten(up_rows), whiten(down_rows)
        return ring_exchange(up_rows, down_rows, "chan"), (up_rows, down_rows)

    tail_wins = local_wins // 4 if local_wins % 4 == 0 else local_wins
    bounds = [0, local_wins - tail_wins, local_wins] if tail_wins < local_wins else [0, local_wins]
    spans = list(zip(bounds[:-1], bounds[1:]))
    fast_sent = [gather_rows(0, fast_rows, spectra[:, lo:hi]) for lo, hi in spans]
    fast = [got for got, _ in fast_sent]
    spectra_late, _ = lax.optimization_barrier((spectra, [sent for _, sent in fast_sent]))
    white = whiten(spectra_late)
    spill = need_most > fast_rows

    transform = lag_table(spec_width // 2, LAG)
    lag_count = transform.shape[1]
    live_count = pair_count[0]
    slot_ids = lax.broadcasted_iota(jnp.int32, (pair_slots,), 0)
    live = slot_ids < live_count

    def pick(selector, rows):
        return jnp.einsum("sc,cwf->wsf", selector.astype(jnp.bfloat16), rows, preferred_element_type=jnp.bfloat16)

    anchors = pick(onehot(pair_anchor, block_chans, live), white)
    own = pick(onehot(pair_partner, block_chans, live & (pair_offset == 1)), white)
    own_hit = onehot(pair_partner, block_chans, live)
    before_row = jnp.sum(jnp.where(own_hit, own_pos_minus[None, :], 0), axis=1)
    after_row = jnp.sum(jnp.where(own_hit, own_pos_plus[None, :], 0), axis=1)
    use_before = live & (pair_offset == 0)
    use_after = live & (pair_offset == 2)
    sels = [
        onehot(before_row, fast_rows, use_before).astype(jnp.bfloat16),
        onehot(after_row, fast_rows, use_after).astype(jnp.bfloat16),
    ]
    corr_full = jnp.concatenate([
        halo_cross(lo, hi - lo, anchors, own, sels, [fast[c][0], fast[c][1]], transform)
        for c, (lo, hi) in enumerate(spans)
    ])

    def spill_extra(_):
        (got_before, got_after), _ = gather_rows(fast_rows, spill_rows, spectra)
        spill_sels = [
            onehot(before_row - fast_rows, spill_rows, use_before).astype(jnp.bfloat16),
            onehot(after_row - fast_rows, spill_rows, use_after).astype(jnp.bfloat16),
        ]
        zero_own = jnp.zeros_like(own)
        extra = jnp.concatenate([
            halo_cross(lo, hi - lo, anchors, zero_own, spill_sels,
                       [got_before[lo:hi], got_after[lo:hi]],
                       transform)
            for lo, hi in spans
        ])
        return extra

    def no_extra(_):
        return jnp.zeros((local_wins, pair_slots, lag_count), jnp.float32)

    spill_late, _ = lax.optimization_barrier((spill, fast[0]))
    corr_full = corr_full + lax.cond(spill_late, spill_extra, no_extra, 0)
    corr_all = lax.reduce_precision(corr_full, exponent_bits=8, mantissa_bits=7)
    running = jnp.sum(corr_full, axis=0)

    ref_sum = butterfly_sum(running, "win")
    norm_scale = jnp.sqrt(jnp.float32(local_wins * lax.axis_size("win")))
    ref_stack = jnp.where(live[:, None], ref_sum / norm_scale, 0.0)
    window_gain = window_gains(window_bins, bin_gain)
    numerator, denominator = window_weights_wm(corr_all, ref_sum, window_gain)
    numerator, denominator = butterfly_sum((numerator, denominator), "win")
    restack = jnp.where(live[:, None], norm_scale * numerator / denominator[:, None], 0.0)
    return (ref_stack, restack)


def solution(mesh):
    in_specs = (
        P(("days", "chan"), "win", None),
        P("chan"),
        P("chan"),
        P("chan"),
        P("chan"),
        P(("days", "win")),
        P(),
    )
    out_specs = (P(("days", "chan"), None), P(("days", "chan"), None))
    return jax.shard_map(local, mesh=mesh, in_specs=in_specs, out_specs=out_specs, check_vma=False)
```

```python
import jax
import jax.numpy as jnp
from jax import lax
from jax.experimental import pallas as pl
from jax.experimental.pallas import tpu as pltpu
from jax.sharding import PartitionSpec as P

LAG = 128


EPS_POWER = 1e-05
EPS_LAG = 1e-06


def whiten(spectra):
    spectra_f = spectra.astype(jnp.float32)
    power_mean = jnp.mean(spectra_f * spectra_f, axis=-1, keepdims=True)
    return (spectra_f * lax.rsqrt(power_mean + EPS_POWER)).astype(jnp.bfloat16)


def lag_table(freq_count, lag_count):
    freq_ids = lax.broadcasted_iota(jnp.float32, (freq_count, lag_count), 0)
    lag_ids = lax.broadcasted_iota(jnp.float32, (freq_count, lag_count), 1) - lag_count // 2
    angles = 2.0 * jnp.pi / (2 * freq_count) * freq_ids * lag_ids
    norm_scale = 1.0 / jnp.sqrt(jnp.float32(freq_count))
    return jnp.concatenate(
        [jnp.cos(angles) * norm_scale, -jnp.sin(angles) * norm_scale], axis=0
    ).astype(jnp.bfloat16)


def cross_spectra(anchors, partners):
    half_width = anchors.shape[-1] // 2
    anchor_f = anchors.astype(jnp.float32)
    partner_f = partners.astype(jnp.float32)
    anchor_re = anchor_f[..., :half_width]
    anchor_im = anchor_f[..., half_width:]
    partner_re = partner_f[..., :half_width]
    partner_im = partner_f[..., half_width:]
    cross_re = anchor_re * partner_re + anchor_im * partner_im
    cross_im = anchor_im * partner_re - anchor_re * partner_im
    return jnp.concatenate([cross_re, cross_im], axis=-1).astype(jnp.bfloat16)


def window_gains(bins, gains):
    levels = lax.broadcasted_iota(jnp.int32, (bins.shape[0], gains.shape[0]), 1)
    return jnp.sum(jnp.where(bins[:, None] == levels, gains[None, :], jnp.float32(0.0)), axis=1)


def window_weights(lag_corr, ref_sum, window_gain):
    corr_f = lag_corr.astype(jnp.float32)
    inner_prod = jnp.mean(corr_f * ref_sum[:, None, :], axis=-1)
    corr_rms = jnp.sqrt(jnp.mean(corr_f * corr_f, axis=-1) + EPS_LAG)
    ref_rms = jnp.sqrt(jnp.mean(ref_sum * ref_sum, axis=-1) + EPS_LAG)
    coherence = inner_prod / (corr_rms * ref_rms[:, None])
    weights = window_gain[None, :] * jnp.exp(2.0 * coherence)
    numerator = jnp.sum(weights[:, :, None] * corr_f, axis=1)
    denominator = jnp.sum(weights, axis=1)
    return (numerator, denominator)


def select_rows(selector, rows):
    return jnp.einsum("sc,cwf->swf", selector, rows, preferred_element_type=jnp.bfloat16)


def butterfly_sum(value, axis):
    peers = lax.axis_size(axis)
    if peers & (peers - 1):
        return lax.psum(value, axis)
    step = 1
    while step < peers:
        pairs = [(i, i ^ step) for i in range(peers)]
        value = jax.tree.map(jnp.add, value, lax.ppermute(value, axis, pairs))
        step *= 2
    return value


def ring_exchange(up_rows, down_rows, axis):
    peers = lax.axis_size(axis)
    up = [(i, (i + 1) % peers) for i in range(peers)]
    down = [(j, i) for i, j in up]
    return lax.ppermute(up_rows, axis, up), lax.ppermute(down_rows, axis, down)


def gather_blocks(row, axis):
    peers = lax.axis_size(axis)
    if peers & (peers - 1):
        return lax.all_gather(row, axis)
    me = lax.axis_index(axis)
    acc = row[None]
    step = 1
    while step < peers:
        pairs = [(i, i ^ step) for i in range(peers)]
        got = lax.ppermute(acc, axis, pairs)
        acc = jnp.where((me & step) == 0, jnp.concatenate([acc, got]), jnp.concatenate([got, acc]))
        step *= 2
    return acc


def onehot(index, size, mask):
    return (index[:, None] == lax.broadcasted_iota(jnp.int32, (index.shape[0], size), 1)) & mask[:, None]


def window_weights_wm(corr_f, ref_sum, window_gain):
    inner_prod = jnp.mean(corr_f * ref_sum[None, :, :], axis=-1)
    corr_rms = jnp.sqrt(jnp.mean(corr_f * corr_f, axis=-1) + EPS_LAG)
    ref_rms = jnp.sqrt(jnp.mean(ref_sum * ref_sum, axis=-1) + EPS_LAG)
    coherence = inner_prod / (corr_rms * ref_rms[None, :])
    weights = window_gain[:, None] * jnp.exp(2.0 * coherence)
    numerator = jnp.sum(weights[:, :, None] * corr_f, axis=0)
    denominator = jnp.sum(weights, axis=0)
    return (numerator, denominator)


def block_needs(offs, parts, count, block_chans):
    live = lax.broadcasted_iota(jnp.int32, offs.shape, 0) < count
    hit = parts[:, None] == lax.broadcasted_iota(jnp.int32, (1, block_chans), 1)
    need_minus = jnp.any(hit & (live & (offs == 0))[:, None], axis=0)
    need_plus = jnp.any(hit & (live & (offs == 2))[:, None], axis=0)
    pos_minus = jnp.cumsum(need_minus, dtype=jnp.int32) - 1
    pos_plus = jnp.cumsum(need_plus, dtype=jnp.int32) - 1
    return need_minus, need_plus, pos_minus, pos_plus


def cross_kernel(anchor_ref, own_ref, sbf_ref, saf_ref, bf_ref, af_ref, t_ref, corr_ref):
    wins = anchor_ref.shape[0]
    half = anchor_ref.shape[2] // 2
    t_re = t_ref[:half, :]
    t_im = t_ref[half:, :]
    sbf, saf = sbf_ref[...], saf_ref[...]
    for w in range(wins):
        part = (
            own_ref[w].astype(jnp.float32)
            + jnp.dot(sbf, bf_ref[w], preferred_element_type=jnp.float32)
            + jnp.dot(saf, af_ref[w], preferred_element_type=jnp.float32)
        )
        anc = anchor_ref[w].astype(jnp.float32)
        a_re, a_im = anc[:, :half], anc[:, half:]
        p_re, p_im = part[:, :half], part[:, half:]
        c_re = (a_re * p_re + a_im * p_im).astype(jnp.bfloat16)
        c_im = (a_im * p_re - a_re * p_im).astype(jnp.bfloat16)
        corr_ref[w] = jnp.dot(c_re, t_re, preferred_element_type=jnp.float32) + jnp.dot(
            c_im, t_im, preferred_element_type=jnp.float32
        )


def halo_cross(chunk, wins, anchors, own, sels, bufs, transform):
    _, slots, width = anchors.shape
    lag_count = transform.shape[1]
    group = min(128, slots)
    row_spec = pl.BlockSpec((wins, group, width), lambda i: (chunk, i, 0))
    sel_specs = [pl.BlockSpec((group, sel.shape[1]), lambda i: (i, 0)) for sel in sels]
    buf_specs = [pl.BlockSpec((wins,) + buf.shape[1:], lambda i: (0, 0, 0)) for buf in bufs]
    return pl.pallas_call(
        cross_kernel,
        grid=(slots // group,),
        in_specs=[row_spec, row_spec] + sel_specs + buf_specs + [pl.BlockSpec(transform.shape, lambda i: (0, 0))],
        out_specs=pl.BlockSpec((wins, group, lag_count), lambda i: (0, i, 0)),
        out_shape=jax.ShapeDtypeStruct((wins, slots, lag_count), jnp.float32),
        compiler_params=pltpu.CompilerParams(vmem_limit_bytes=56 * 1024 * 1024),
    )(anchors, own, *sels, *bufs, transform)


def local(spectra, pair_anchor, pair_offset, pair_partner, pair_count, window_bins, bin_gain):
    block_chans, local_wins, spec_width = spectra.shape
    pair_slots = pair_anchor.shape[0]
    fast_rows = (block_chans // 2 + 15) // 16 * 16
    spill_rows = block_chans - fast_rows

    blocks = lax.axis_size("chan")
    block = lax.axis_index("chan")
    table = jnp.concatenate([pair_offset, pair_partner, pair_count])
    tables = gather_blocks(table, "chan")
    table_before = tables[(block + blocks - 1) % blocks]
    table_after = tables[(block + 1) % blocks]

    def needs_of(tab):
        return block_needs(tab[:pair_slots], tab[pair_slots:2 * pair_slots], tab[2 * pair_slots], block_chans)

    own_minus, own_plus, own_pos_minus, own_pos_plus = needs_of(table)
    up_need, _, up_pos, _ = needs_of(table_after)
    _, down_need, _, down_pos = needs_of(table_before)
    all_needs = jax.vmap(needs_of)(tables)
    need_most = jnp.maximum(
        jnp.max(jnp.sum(all_needs[0], axis=1, dtype=jnp.int32)),
        jnp.max(jnp.sum(all_needs[1], axis=1, dtype=jnp.int32)),
    )

    def send_selector(need, pos, first, rows):
        return onehot(pos - first, rows, need).T.astype(jnp.bfloat16)

    def gather_rows(first, rows, source, whitened=False):
        up_rows = jnp.einsum("jc,cwf->wjf", send_selector(up_need, up_pos, first, rows), source,
                             preferred_element_type=jnp.bfloat16)
        down_rows = jnp.einsum("jc,cwf->wjf", send_selector(down_need, down_pos, first, rows), source,
                               preferred_element_type=jnp.bfloat16)
        if not whitened:
            up_rows, down_rows = whiten(up_rows), whiten(down_rows)
        return ring_exchange(up_rows, down_rows, "chan"), (up_rows, down_rows)

    chunks = 2 if local_wins % 2 == 0 else 1
    chunk_wins = local_wins // chunks
    fast_sent = [gather_rows(0, fast_rows, spectra[:, c * chunk_wins:(c + 1) * chunk_wins]) for c in range(chunks)]
    fast = [got for got, _ in fast_sent]
    spectra_late, _ = lax.optimization_barrier((spectra, [sent for _, sent in fast_sent]))
    white = whiten(spectra_late)
    spill = need_most > fast_rows

    transform = lag_table(spec_width // 2, LAG)
    lag_count = transform.shape[1]
    live_count = pair_count[0]
    slot_ids = lax.broadcasted_iota(jnp.int32, (pair_slots,), 0)
    live = slot_ids < live_count

    def pick(selector, rows):
        return jnp.einsum("sc,cwf->wsf", selector.astype(jnp.bfloat16), rows, preferred_element_type=jnp.bfloat16)

    anchors = pick(onehot(pair_anchor, block_chans, live), white)
    own = pick(onehot(pair_partner, block_chans, live & (pair_offset == 1)), white)
    own_hit = onehot(pair_partner, block_chans, live)
    before_row = jnp.sum(jnp.where(own_hit, own_pos_minus[None, :], 0), axis=1)
    after_row = jnp.sum(jnp.where(own_hit, own_pos_plus[None, :], 0), axis=1)
    use_before = live & (pair_offset == 0)
    use_after = live & (pair_offset == 2)
    sels = [
        onehot(before_row, fast_rows, use_before).astype(jnp.bfloat16),
        onehot(after_row, fast_rows, use_after).astype(jnp.bfloat16),
    ]
    corr_full = jnp.concatenate([
        halo_cross(c, chunk_wins, anchors, own, sels, [fast[c][0], fast[c][1]], transform)
        for c in range(chunks)
    ])

    def spill_extra(_):
        (got_before, got_after), _ = gather_rows(fast_rows, spill_rows, white, whitened=True)
        spill_sels = [
            onehot(before_row - fast_rows, spill_rows, use_before).astype(jnp.bfloat16),
            onehot(after_row - fast_rows, spill_rows, use_after).astype(jnp.bfloat16),
        ]
        zero_own = jnp.zeros_like(own)
        extra = jnp.concatenate([
            halo_cross(c, chunk_wins, anchors, zero_own, spill_sels,
                       [got_before[c * chunk_wins:(c + 1) * chunk_wins], got_after[c * chunk_wins:(c + 1) * chunk_wins]],
                       transform)
            for c in range(chunks)
        ])
        return extra

    def no_extra(_):
        return jnp.zeros((local_wins, pair_slots, lag_count), jnp.float32)

    spill_late, _ = lax.optimization_barrier((spill, fast[0]))
    corr_full = corr_full + lax.cond(spill_late, spill_extra, no_extra, 0)
    corr_all = lax.reduce_precision(corr_full, exponent_bits=8, mantissa_bits=7)
    running = jnp.sum(corr_full, axis=0)

    ref_sum = butterfly_sum(running, "win")
    norm_scale = jnp.sqrt(jnp.float32(local_wins * lax.axis_size("win")))
    ref_stack = jnp.where(live[:, None], ref_sum / norm_scale, 0.0)
    window_gain = window_gains(window_bins, bin_gain)
    numerator, denominator = window_weights_wm(corr_all, ref_sum, window_gain)
    numerator, denominator = butterfly_sum((numerator, denominator), "win")
    restack = jnp.where(live[:, None], norm_scale * numerator / denominator[:, None], 0.0)
    return (ref_stack, restack)


def solution(mesh):
    in_specs = (
        P(("days", "chan"), "win", None),
        P("chan"),
        P("chan"),
        P("chan"),
        P("chan"),
        P(("days", "win")),
        P(),
    )
    out_specs = (P(("days", "chan"), None), P(("days", "chan"), None))
    return jax.shard_map(local, mesh=mesh, in_specs=in_specs, out_specs=out_specs, check_vma=False)
```

```python
import jax
import jax.numpy as jnp
from jax import lax
from jax.experimental import pallas as pl
from jax.experimental.pallas import tpu as pltpu
from jax.sharding import PartitionSpec as P

LAG = 128


EPS_POWER = 1e-05
EPS_LAG = 1e-06


def whiten(spectra):
    spectra_f = spectra.astype(jnp.float32)
    power_mean = jnp.mean(spectra_f * spectra_f, axis=-1, keepdims=True)
    return (spectra_f * lax.rsqrt(power_mean + EPS_POWER)).astype(jnp.bfloat16)


def lag_table(freq_count, lag_count):
    freq_ids = lax.broadcasted_iota(jnp.float32, (freq_count, lag_count), 0)
    lag_ids = lax.broadcasted_iota(jnp.float32, (freq_count, lag_count), 1) - lag_count // 2
    angles = 2.0 * jnp.pi / (2 * freq_count) * freq_ids * lag_ids
    norm_scale = 1.0 / jnp.sqrt(jnp.float32(freq_count))
    return jnp.concatenate(
        [jnp.cos(angles) * norm_scale, -jnp.sin(angles) * norm_scale], axis=0
    ).astype(jnp.bfloat16)


def cross_spectra(anchors, partners):
    half_width = anchors.shape[-1] // 2
    anchor_f = anchors.astype(jnp.float32)
    partner_f = partners.astype(jnp.float32)
    anchor_re = anchor_f[..., :half_width]
    anchor_im = anchor_f[..., half_width:]
    partner_re = partner_f[..., :half_width]
    partner_im = partner_f[..., half_width:]
    cross_re = anchor_re * partner_re + anchor_im * partner_im
    cross_im = anchor_im * partner_re - anchor_re * partner_im
    return jnp.concatenate([cross_re, cross_im], axis=-1).astype(jnp.bfloat16)


def window_gains(bins, gains):
    levels = lax.broadcasted_iota(jnp.int32, (bins.shape[0], gains.shape[0]), 1)
    return jnp.sum(jnp.where(bins[:, None] == levels, gains[None, :], jnp.float32(0.0)), axis=1)


def window_weights(lag_corr, ref_sum, window_gain):
    corr_f = lag_corr.astype(jnp.float32)
    inner_prod = jnp.mean(corr_f * ref_sum[:, None, :], axis=-1)
    corr_rms = jnp.sqrt(jnp.mean(corr_f * corr_f, axis=-1) + EPS_LAG)
    ref_rms = jnp.sqrt(jnp.mean(ref_sum * ref_sum, axis=-1) + EPS_LAG)
    coherence = inner_prod / (corr_rms * ref_rms[:, None])
    weights = window_gain[None, :] * jnp.exp(2.0 * coherence)
    numerator = jnp.sum(weights[:, :, None] * corr_f, axis=1)
    denominator = jnp.sum(weights, axis=1)
    return (numerator, denominator)


def select_rows(selector, rows):
    return jnp.einsum("sc,cwf->swf", selector, rows, preferred_element_type=jnp.bfloat16)


def butterfly_sum(value, axis):
    peers = lax.axis_size(axis)
    if peers & (peers - 1):
        return lax.psum(value, axis)
    step = 1
    while step < peers:
        pairs = [(i, i ^ step) for i in range(peers)]
        value = jax.tree.map(jnp.add, value, lax.ppermute(value, axis, pairs))
        step *= 2
    return value


def ring_exchange(up_rows, down_rows, axis):
    peers = lax.axis_size(axis)
    up = [(i, (i + 1) % peers) for i in range(peers)]
    down = [(j, i) for i, j in up]
    return lax.ppermute(up_rows, axis, up), lax.ppermute(down_rows, axis, down)


def gather_blocks(row, axis):
    peers = lax.axis_size(axis)
    if peers & (peers - 1):
        return lax.all_gather(row, axis)
    me = lax.axis_index(axis)
    acc = row[None]
    step = 1
    while step < peers:
        pairs = [(i, i ^ step) for i in range(peers)]
        got = lax.ppermute(acc, axis, pairs)
        acc = jnp.where((me & step) == 0, jnp.concatenate([acc, got]), jnp.concatenate([got, acc]))
        step *= 2
    return acc


def onehot(index, size, mask):
    return (index[:, None] == lax.broadcasted_iota(jnp.int32, (index.shape[0], size), 1)) & mask[:, None]


def window_weights_wm(corr_f, ref_sum, window_gain):
    inner_prod = jnp.mean(corr_f * ref_sum[None, :, :], axis=-1)
    corr_rms = jnp.sqrt(jnp.mean(corr_f * corr_f, axis=-1) + EPS_LAG)
    ref_rms = jnp.sqrt(jnp.mean(ref_sum * ref_sum, axis=-1) + EPS_LAG)
    coherence = inner_prod / (corr_rms * ref_rms[None, :])
    weights = window_gain[:, None] * jnp.exp(2.0 * coherence)
    numerator = jnp.sum(weights[:, :, None] * corr_f, axis=0)
    denominator = jnp.sum(weights, axis=0)
    return (numerator, denominator)


def block_needs(offs, parts, count, block_chans):
    live = lax.broadcasted_iota(jnp.int32, offs.shape, 0) < count
    hit = parts[:, None] == lax.broadcasted_iota(jnp.int32, (1, block_chans), 1)
    need_minus = jnp.any(hit & (live & (offs == 0))[:, None], axis=0)
    need_plus = jnp.any(hit & (live & (offs == 2))[:, None], axis=0)
    pos_minus = jnp.cumsum(need_minus, dtype=jnp.int32) - 1
    pos_plus = jnp.cumsum(need_plus, dtype=jnp.int32) - 1
    return need_minus, need_plus, pos_minus, pos_plus


def cross_kernel(anchor_ref, own_ref, sbf_ref, saf_ref, bf_ref, af_ref, t_ref, corr_ref):
    wins = anchor_ref.shape[0]
    half = anchor_ref.shape[2] // 2
    t_re = t_ref[:half, :]
    t_im = t_ref[half:, :]
    sbf, saf = sbf_ref[...], saf_ref[...]

    def one_window(w, carry):
        part = (
            own_ref[w].astype(jnp.float32)
            + jnp.dot(sbf, bf_ref[w], preferred_element_type=jnp.float32)
            + jnp.dot(saf, af_ref[w], preferred_element_type=jnp.float32)
        )
        anc = anchor_ref[w].astype(jnp.float32)
        a_re, a_im = anc[:, :half], anc[:, half:]
        p_re, p_im = part[:, :half], part[:, half:]
        c_re = (a_re * p_re + a_im * p_im).astype(jnp.bfloat16)
        c_im = (a_im * p_re - a_re * p_im).astype(jnp.bfloat16)
        corr_ref[w] = jnp.dot(c_re, t_re, preferred_element_type=jnp.float32) + jnp.dot(
            c_im, t_im, preferred_element_type=jnp.float32
        )
        return carry

    lax.fori_loop(0, wins, one_window, 0)


def halo_cross(chunk, wins, anchors, own, sels, bufs, transform):
    _, slots, width = anchors.shape
    lag_count = transform.shape[1]
    group = min(128, slots)
    row_spec = pl.BlockSpec((wins, group, width), lambda i: (chunk, i, 0))
    sel_specs = [pl.BlockSpec((group, sel.shape[1]), lambda i: (i, 0)) for sel in sels]
    buf_specs = [pl.BlockSpec((wins,) + buf.shape[1:], lambda i: (0, 0, 0)) for buf in bufs]
    return pl.pallas_call(
        cross_kernel,
        grid=(slots // group,),
        in_specs=[row_spec, row_spec] + sel_specs + buf_specs + [pl.BlockSpec(transform.shape, lambda i: (0, 0))],
        out_specs=pl.BlockSpec((wins, group, lag_count), lambda i: (0, i, 0)),
        out_shape=jax.ShapeDtypeStruct((wins, slots, lag_count), jnp.float32),
        compiler_params=pltpu.CompilerParams(vmem_limit_bytes=56 * 1024 * 1024),
    )(anchors, own, *sels, *bufs, transform)


def local(spectra, pair_anchor, pair_offset, pair_partner, pair_count, window_bins, bin_gain):
    block_chans, local_wins, spec_width = spectra.shape
    pair_slots = pair_anchor.shape[0]
    fast_rows = (block_chans // 2 + 15) // 16 * 16
    spill_rows = block_chans - fast_rows

    blocks = lax.axis_size("chan")
    block = lax.axis_index("chan")
    table = jnp.concatenate([pair_offset, pair_partner, pair_count])
    tables = gather_blocks(table, "chan")
    table_before = tables[(block + blocks - 1) % blocks]
    table_after = tables[(block + 1) % blocks]

    def needs_of(tab):
        return block_needs(tab[:pair_slots], tab[pair_slots:2 * pair_slots], tab[2 * pair_slots], block_chans)

    own_minus, own_plus, own_pos_minus, own_pos_plus = needs_of(table)
    up_need, _, up_pos, _ = needs_of(table_after)
    _, down_need, _, down_pos = needs_of(table_before)
    all_needs = jax.vmap(needs_of)(tables)
    need_most = jnp.maximum(
        jnp.max(jnp.sum(all_needs[0], axis=1, dtype=jnp.int32)),
        jnp.max(jnp.sum(all_needs[1], axis=1, dtype=jnp.int32)),
    )

    def send_selector(need, pos, first, rows):
        return onehot(pos - first, rows, need).T.astype(jnp.bfloat16)

    def gather_rows(first, rows, source, whitened=False):
        up_rows = jnp.einsum("jc,cwf->wjf", send_selector(up_need, up_pos, first, rows), source,
                             preferred_element_type=jnp.bfloat16)
        down_rows = jnp.einsum("jc,cwf->wjf", send_selector(down_need, down_pos, first, rows), source,
                               preferred_element_type=jnp.bfloat16)
        if not whitened:
            up_rows, down_rows = whiten(up_rows), whiten(down_rows)
        return ring_exchange(up_rows, down_rows, "chan"), (up_rows, down_rows)

    chunks = 2 if local_wins % 2 == 0 else 1
    chunk_wins = local_wins // chunks
    fast_sent = [gather_rows(0, fast_rows, spectra[:, c * chunk_wins:(c + 1) * chunk_wins]) for c in range(chunks)]
    fast = [got for got, _ in fast_sent]
    spectra_late, _ = lax.optimization_barrier((spectra, [sent for _, sent in fast_sent]))
    white = whiten(spectra_late)
    spill = need_most > fast_rows

    transform = lag_table(spec_width // 2, LAG)
    lag_count = transform.shape[1]
    live_count = pair_count[0]
    slot_ids = lax.broadcasted_iota(jnp.int32, (pair_slots,), 0)
    live = slot_ids < live_count

    def pick(selector, rows):
        return jnp.einsum("sc,cwf->wsf", selector.astype(jnp.bfloat16), rows, preferred_element_type=jnp.bfloat16)

    anchors = pick(onehot(pair_anchor, block_chans, live), white)
    own = pick(onehot(pair_partner, block_chans, live & (pair_offset == 1)), white)
    own_hit = onehot(pair_partner, block_chans, live)
    before_row = jnp.sum(jnp.where(own_hit, own_pos_minus[None, :], 0), axis=1)
    after_row = jnp.sum(jnp.where(own_hit, own_pos_plus[None, :], 0), axis=1)
    use_before = live & (pair_offset == 0)
    use_after = live & (pair_offset == 2)
    sels = [
        onehot(before_row, fast_rows, use_before).astype(jnp.bfloat16),
        onehot(after_row, fast_rows, use_after).astype(jnp.bfloat16),
    ]
    corr_full = jnp.concatenate([
        halo_cross(c, chunk_wins, anchors, own, sels, [fast[c][0], fast[c][1]], transform)
        for c in range(chunks)
    ])

    def spill_extra(_):
        (got_before, got_after), _ = gather_rows(fast_rows, spill_rows, white, whitened=True)
        spill_sels = [
            onehot(before_row - fast_rows, spill_rows, use_before).astype(jnp.bfloat16),
            onehot(after_row - fast_rows, spill_rows, use_after).astype(jnp.bfloat16),
        ]
        extra = halo_cross(0, local_wins, anchors, jnp.zeros_like(own), spill_sels,
                           [got_before, got_after], transform)
        return extra

    def no_extra(_):
        return jnp.zeros((local_wins, pair_slots, lag_count), jnp.float32)

    spill_late, _ = lax.optimization_barrier((spill, fast[0]))
    corr_full = corr_full + lax.cond(spill_late, spill_extra, no_extra, 0)
    corr_all = lax.reduce_precision(corr_full, exponent_bits=8, mantissa_bits=7)
    running = jnp.sum(corr_full, axis=0)

    ref_sum = butterfly_sum(running, "win")
    norm_scale = jnp.sqrt(jnp.float32(local_wins * lax.axis_size("win")))
    ref_stack = jnp.where(live[:, None], ref_sum / norm_scale, 0.0)
    window_gain = window_gains(window_bins, bin_gain)
    numerator, denominator = window_weights_wm(corr_all, ref_sum, window_gain)
    numerator, denominator = butterfly_sum((numerator, denominator), "win")
    restack = jnp.where(live[:, None], norm_scale * numerator / denominator[:, None], 0.0)
    return (ref_stack, restack)


def solution(mesh):
    in_specs = (
        P(("days", "chan"), "win", None),
        P("chan"),
        P("chan"),
        P("chan"),
        P("chan"),
        P(("days", "win")),
        P(),
    )
    out_specs = (P(("days", "chan"), None), P(("days", "chan"), None))
    return jax.shard_map(local, mesh=mesh, in_specs=in_specs, out_specs=out_specs, check_vma=False)
```

```python
import jax
import jax.numpy as jnp
from jax import lax
from jax.experimental import pallas as pl
from jax.experimental.pallas import tpu as pltpu
from jax.sharding import PartitionSpec as P

LAG = 128


EPS_POWER = 1e-05
EPS_LAG = 1e-06


def whiten(spectra):
    spectra_f = spectra.astype(jnp.float32)
    power_mean = jnp.mean(spectra_f * spectra_f, axis=-1, keepdims=True)
    return (spectra_f * lax.rsqrt(power_mean + EPS_POWER)).astype(jnp.bfloat16)


def lag_table(freq_count, lag_count):
    freq_ids = lax.broadcasted_iota(jnp.float32, (freq_count, lag_count), 0)
    lag_ids = lax.broadcasted_iota(jnp.float32, (freq_count, lag_count), 1) - lag_count // 2
    angles = 2.0 * jnp.pi / (2 * freq_count) * freq_ids * lag_ids
    norm_scale = 1.0 / jnp.sqrt(jnp.float32(freq_count))
    return jnp.concatenate(
        [jnp.cos(angles) * norm_scale, -jnp.sin(angles) * norm_scale], axis=0
    ).astype(jnp.bfloat16)


def cross_spectra(anchors, partners):
    half_width = anchors.shape[-1] // 2
    anchor_f = anchors.astype(jnp.float32)
    partner_f = partners.astype(jnp.float32)
    anchor_re = anchor_f[..., :half_width]
    anchor_im = anchor_f[..., half_width:]
    partner_re = partner_f[..., :half_width]
    partner_im = partner_f[..., half_width:]
    cross_re = anchor_re * partner_re + anchor_im * partner_im
    cross_im = anchor_im * partner_re - anchor_re * partner_im
    return jnp.concatenate([cross_re, cross_im], axis=-1).astype(jnp.bfloat16)


def window_gains(bins, gains):
    levels = lax.broadcasted_iota(jnp.int32, (bins.shape[0], gains.shape[0]), 1)
    return jnp.sum(jnp.where(bins[:, None] == levels, gains[None, :], jnp.float32(0.0)), axis=1)


def window_weights(lag_corr, ref_sum, window_gain):
    corr_f = lag_corr.astype(jnp.float32)
    inner_prod = jnp.mean(corr_f * ref_sum[:, None, :], axis=-1)
    corr_rms = jnp.sqrt(jnp.mean(corr_f * corr_f, axis=-1) + EPS_LAG)
    ref_rms = jnp.sqrt(jnp.mean(ref_sum * ref_sum, axis=-1) + EPS_LAG)
    coherence = inner_prod / (corr_rms * ref_rms[:, None])
    weights = window_gain[None, :] * jnp.exp(2.0 * coherence)
    numerator = jnp.sum(weights[:, :, None] * corr_f, axis=1)
    denominator = jnp.sum(weights, axis=1)
    return (numerator, denominator)


def select_rows(selector, rows):
    return jnp.einsum("sc,cwf->swf", selector, rows, preferred_element_type=jnp.bfloat16)


def butterfly_sum(value, axis):
    peers = lax.axis_size(axis)
    if peers & (peers - 1):
        return lax.psum(value, axis)
    step = 1
    while step < peers:
        pairs = [(i, i ^ step) for i in range(peers)]
        value = jax.tree.map(jnp.add, value, lax.ppermute(value, axis, pairs))
        step *= 2
    return value


def ring_exchange(up_rows, down_rows, axis):
    peers = lax.axis_size(axis)
    up = [(i, (i + 1) % peers) for i in range(peers)]
    down = [(j, i) for i, j in up]
    return lax.ppermute(up_rows, axis, up), lax.ppermute(down_rows, axis, down)


def gather_blocks(row, axis):
    peers = lax.axis_size(axis)
    if peers & (peers - 1):
        return lax.all_gather(row, axis)
    me = lax.axis_index(axis)
    acc = row[None]
    step = 1
    while step < peers:
        pairs = [(i, i ^ step) for i in range(peers)]
        got = lax.ppermute(acc, axis, pairs)
        acc = jnp.where((me & step) == 0, jnp.concatenate([acc, got]), jnp.concatenate([got, acc]))
        step *= 2
    return acc


def onehot(index, size, mask):
    return (index[:, None] == lax.broadcasted_iota(jnp.int32, (index.shape[0], size), 1)) & mask[:, None]


def window_weights_wm(corr_f, ref_sum, window_gain):
    inner_prod = jnp.mean(corr_f * ref_sum[None, :, :], axis=-1)
    corr_rms = jnp.sqrt(jnp.mean(corr_f * corr_f, axis=-1) + EPS_LAG)
    ref_rms = jnp.sqrt(jnp.mean(ref_sum * ref_sum, axis=-1) + EPS_LAG)
    coherence = inner_prod / (corr_rms * ref_rms[None, :])
    weights = window_gain[:, None] * jnp.exp(2.0 * coherence)
    numerator = jnp.sum(weights[:, :, None] * corr_f, axis=0)
    denominator = jnp.sum(weights, axis=0)
    return (numerator, denominator)


def block_needs(offs, parts, count, block_chans):
    live = lax.broadcasted_iota(jnp.int32, offs.shape, 0) < count
    hit = parts[:, None] == lax.broadcasted_iota(jnp.int32, (1, block_chans), 1)
    need_minus = jnp.any(hit & (live & (offs == 0))[:, None], axis=0)
    need_plus = jnp.any(hit & (live & (offs == 2))[:, None], axis=0)
    pos_minus = jnp.cumsum(need_minus, dtype=jnp.int32) - 1
    pos_plus = jnp.cumsum(need_plus, dtype=jnp.int32) - 1
    return need_minus, need_plus, pos_minus, pos_plus


def cross_kernel(anchor_ref, own_ref, sbf_ref, saf_ref, bf_ref, af_ref, t_ref, corr_ref):
    wins = anchor_ref.shape[0]
    half = anchor_ref.shape[2] // 2
    t_re = t_ref[:half, :]
    t_im = t_ref[half:, :]
    sbf, saf = sbf_ref[...], saf_ref[...]

    def one_window(w, carry):
        part = (
            own_ref[w].astype(jnp.float32)
            + jnp.dot(sbf, bf_ref[w], preferred_element_type=jnp.float32)
            + jnp.dot(saf, af_ref[w], preferred_element_type=jnp.float32)
        )
        anc = anchor_ref[w].astype(jnp.float32)
        a_re, a_im = anc[:, :half], anc[:, half:]
        p_re, p_im = part[:, :half], part[:, half:]
        c_re = (a_re * p_re + a_im * p_im).astype(jnp.bfloat16)
        c_im = (a_im * p_re - a_re * p_im).astype(jnp.bfloat16)
        corr_ref[w] = jnp.dot(c_re, t_re, preferred_element_type=jnp.float32) + jnp.dot(
            c_im, t_im, preferred_element_type=jnp.float32
        )
        return carry

    lax.fori_loop(0, wins, one_window, 0)


def halo_cross(chunk, wins, anchors, own, sels, bufs, transform):
    _, slots, width = anchors.shape
    lag_count = transform.shape[1]
    group = min(128, slots)
    row_spec = pl.BlockSpec((wins, group, width), lambda i: (chunk, i, 0))
    sel_specs = [pl.BlockSpec((group, sel.shape[1]), lambda i: (i, 0)) for sel in sels]
    buf_specs = [pl.BlockSpec((wins,) + buf.shape[1:], lambda i: (0, 0, 0)) for buf in bufs]
    return pl.pallas_call(
        cross_kernel,
        grid=(slots // group,),
        in_specs=[row_spec, row_spec] + sel_specs + buf_specs + [pl.BlockSpec(transform.shape, lambda i: (0, 0))],
        out_specs=pl.BlockSpec((wins, group, lag_count), lambda i: (0, i, 0)),
        out_shape=jax.ShapeDtypeStruct((wins, slots, lag_count), jnp.float32),
        compiler_params=pltpu.CompilerParams(vmem_limit_bytes=56 * 1024 * 1024),
    )(anchors, own, *sels, *bufs, transform)


def local(spectra, pair_anchor, pair_offset, pair_partner, pair_count, window_bins, bin_gain):
    block_chans, local_wins, spec_width = spectra.shape
    pair_slots = pair_anchor.shape[0]
    fast_rows = (block_chans // 2 + 15) // 16 * 16
    spill_rows = block_chans - fast_rows

    blocks = lax.axis_size("chan")
    block = lax.axis_index("chan")
    table = jnp.concatenate([pair_offset, pair_partner, pair_count])
    tables = gather_blocks(table, "chan")
    table_before = tables[(block + blocks - 1) % blocks]
    table_after = tables[(block + 1) % blocks]

    def needs_of(tab):
        return block_needs(tab[:pair_slots], tab[pair_slots:2 * pair_slots], tab[2 * pair_slots], block_chans)

    own_minus, own_plus, own_pos_minus, own_pos_plus = needs_of(table)
    up_need, _, up_pos, _ = needs_of(table_after)
    _, down_need, _, down_pos = needs_of(table_before)
    all_needs = jax.vmap(needs_of)(tables)
    need_most = jnp.maximum(
        jnp.max(jnp.sum(all_needs[0], axis=1, dtype=jnp.int32)),
        jnp.max(jnp.sum(all_needs[1], axis=1, dtype=jnp.int32)),
    )

    def send_selector(need, pos, first, rows):
        return onehot(pos - first, rows, need).T.astype(jnp.bfloat16)

    def gather_rows(first, rows, source, whitened=False):
        up_rows = jnp.einsum("jc,cwf->wjf", send_selector(up_need, up_pos, first, rows), source,
                             preferred_element_type=jnp.bfloat16)
        down_rows = jnp.einsum("jc,cwf->wjf", send_selector(down_need, down_pos, first, rows), source,
                               preferred_element_type=jnp.bfloat16)
        if not whitened:
            up_rows, down_rows = whiten(up_rows), whiten(down_rows)
        return ring_exchange(up_rows, down_rows, "chan"), (up_rows, down_rows)

    chunks = 2 if local_wins % 2 == 0 else 1
    chunk_wins = local_wins // chunks
    fast_sent = [gather_rows(0, fast_rows, spectra[:, c * chunk_wins:(c + 1) * chunk_wins]) for c in range(chunks)]
    fast = [got for got, _ in fast_sent]
    spectra_late, _ = lax.optimization_barrier((spectra, [sent for _, sent in fast_sent]))
    white = whiten(spectra_late)
    spill = need_most > fast_rows

    transform = lag_table(spec_width // 2, LAG)
    lag_count = transform.shape[1]
    live_count = pair_count[0]
    slot_ids = lax.broadcasted_iota(jnp.int32, (pair_slots,), 0)
    live = slot_ids < live_count

    def pick(selector, rows):
        return jnp.einsum("sc,cwf->wsf", selector.astype(jnp.bfloat16), rows, preferred_element_type=jnp.bfloat16)

    anchors = pick(onehot(pair_anchor, block_chans, live), white)
    own = pick(onehot(pair_partner, block_chans, live & (pair_offset == 1)), white)
    own_hit = onehot(pair_partner, block_chans, live)
    before_row = jnp.sum(jnp.where(own_hit, own_pos_minus[None, :], 0), axis=1)
    after_row = jnp.sum(jnp.where(own_hit, own_pos_plus[None, :], 0), axis=1)
    use_before = live & (pair_offset == 0)
    use_after = live & (pair_offset == 2)
    sels = [
        onehot(before_row, fast_rows, use_before).astype(jnp.bfloat16),
        onehot(after_row, fast_rows, use_after).astype(jnp.bfloat16),
    ]
    corr_full = jnp.concatenate([
        halo_cross(c, chunk_wins, anchors, own, sels, [fast[c][0], fast[c][1]], transform)
        for c in range(chunks)
    ])

    def spill_extra(_):
        (got_before, got_after), _ = gather_rows(fast_rows, spill_rows, white, whitened=True)
        spill_sels = [
            onehot(before_row - fast_rows, spill_rows, use_before).astype(jnp.bfloat16),
            onehot(after_row - fast_rows, spill_rows, use_after).astype(jnp.bfloat16),
        ]
        extra = halo_cross(0, local_wins, anchors, jnp.zeros_like(own), spill_sels,
                           [got_before, got_after], transform)
        return extra

    def no_extra(_):
        return jnp.zeros((local_wins, pair_slots, lag_count), jnp.float32)

    spill_late, _ = lax.optimization_barrier((spill, fast[0]))
    corr_full = corr_full + lax.cond(spill_late, spill_extra, no_extra, 0)
    corr_all = lax.reduce_precision(corr_full, exponent_bits=8, mantissa_bits=7)
    running = jnp.sum(corr_full, axis=0)

    ref_sum = butterfly_sum(running, "win")
    norm_scale = jnp.sqrt(jnp.float32(local_wins * lax.axis_size("win")))
    ref_stack = jnp.where(live[:, None], ref_sum / norm_scale, 0.0)
    window_gain = window_gains(window_bins, bin_gain)
    numerator, denominator = window_weights_wm(corr_all, ref_sum, window_gain)
    if pair_slots % lag_count == 0:
        packed = jnp.concatenate([numerator, denominator.reshape(-1, lag_count)])
        packed = butterfly_sum(packed, "win")
        numerator, denominator = packed[:pair_slots], packed[pair_slots:].reshape(-1)
    else:
        numerator, denominator = butterfly_sum((numerator, denominator), "win")
    restack = jnp.where(live[:, None], norm_scale * numerator / denominator[:, None], 0.0)
    return (ref_stack, restack)


def solution(mesh):
    in_specs = (
        P(("days", "chan"), "win", None),
        P("chan"),
        P("chan"),
        P("chan"),
        P("chan"),
        P(("days", "win")),
        P(),
    )
    out_specs = (P(("days", "chan"), None), P(("days", "chan"), None))
    return jax.shard_map(local, mesh=mesh, in_specs=in_specs, out_specs=out_specs, check_vma=False)
```

```python
import jax
import jax.numpy as jnp
from jax import lax
from jax.experimental import pallas as pl
from jax.experimental.pallas import tpu as pltpu
from jax.sharding import PartitionSpec as P

LAG = 128


EPS_POWER = 1e-05
EPS_LAG = 1e-06


def whiten(spectra):
    spectra_f = spectra.astype(jnp.float32)
    power_mean = jnp.mean(spectra_f * spectra_f, axis=-1, keepdims=True)
    return (spectra_f * lax.rsqrt(power_mean + EPS_POWER)).astype(jnp.bfloat16)


def lag_table(freq_count, lag_count):
    freq_ids = lax.broadcasted_iota(jnp.float32, (freq_count, lag_count), 0)
    lag_ids = lax.broadcasted_iota(jnp.float32, (freq_count, lag_count), 1) - lag_count // 2
    angles = 2.0 * jnp.pi / (2 * freq_count) * freq_ids * lag_ids
    norm_scale = 1.0 / jnp.sqrt(jnp.float32(freq_count))
    return jnp.concatenate(
        [jnp.cos(angles) * norm_scale, -jnp.sin(angles) * norm_scale], axis=0
    ).astype(jnp.bfloat16)


def cross_spectra(anchors, partners):
    half_width = anchors.shape[-1] // 2
    anchor_f = anchors.astype(jnp.float32)
    partner_f = partners.astype(jnp.float32)
    anchor_re = anchor_f[..., :half_width]
    anchor_im = anchor_f[..., half_width:]
    partner_re = partner_f[..., :half_width]
    partner_im = partner_f[..., half_width:]
    cross_re = anchor_re * partner_re + anchor_im * partner_im
    cross_im = anchor_im * partner_re - anchor_re * partner_im
    return jnp.concatenate([cross_re, cross_im], axis=-1).astype(jnp.bfloat16)


def window_gains(bins, gains):
    levels = lax.broadcasted_iota(jnp.int32, (bins.shape[0], gains.shape[0]), 1)
    return jnp.sum(jnp.where(bins[:, None] == levels, gains[None, :], jnp.float32(0.0)), axis=1)


def window_weights(lag_corr, ref_sum, window_gain):
    corr_f = lag_corr.astype(jnp.float32)
    inner_prod = jnp.mean(corr_f * ref_sum[:, None, :], axis=-1)
    corr_rms = jnp.sqrt(jnp.mean(corr_f * corr_f, axis=-1) + EPS_LAG)
    ref_rms = jnp.sqrt(jnp.mean(ref_sum * ref_sum, axis=-1) + EPS_LAG)
    coherence = inner_prod / (corr_rms * ref_rms[:, None])
    weights = window_gain[None, :] * jnp.exp(2.0 * coherence)
    numerator = jnp.sum(weights[:, :, None] * corr_f, axis=1)
    denominator = jnp.sum(weights, axis=1)
    return (numerator, denominator)


def select_rows(selector, rows):
    return jnp.einsum("sc,cwf->swf", selector, rows, preferred_element_type=jnp.bfloat16)


def butterfly_sum(value, axis):
    peers = lax.axis_size(axis)
    if peers & (peers - 1):
        return lax.psum(value, axis)
    step = 1
    while step < peers:
        pairs = [(i, i ^ step) for i in range(peers)]
        value = jax.tree.map(jnp.add, value, lax.ppermute(value, axis, pairs))
        step *= 2
    return value


def ring_exchange(up_rows, down_rows, axis):
    peers = lax.axis_size(axis)
    up = [(i, (i + 1) % peers) for i in range(peers)]
    down = [(j, i) for i, j in up]
    return lax.ppermute(up_rows, axis, up), lax.ppermute(down_rows, axis, down)


def gather_blocks(row, axis):
    peers = lax.axis_size(axis)
    if peers & (peers - 1):
        return lax.all_gather(row, axis)
    me = lax.axis_index(axis)
    acc = row[None]
    step = 1
    while step < peers:
        pairs = [(i, i ^ step) for i in range(peers)]
        got = lax.ppermute(acc, axis, pairs)
        acc = jnp.where((me & step) == 0, jnp.concatenate([acc, got]), jnp.concatenate([got, acc]))
        step *= 2
    return acc


def onehot(index, size, mask):
    return (index[:, None] == lax.broadcasted_iota(jnp.int32, (index.shape[0], size), 1)) & mask[:, None]


def window_weights_wm(corr_f, ref_sum, window_gain):
    inner_prod = jnp.mean(corr_f * ref_sum[None, :, :], axis=-1)
    corr_rms = jnp.sqrt(jnp.mean(corr_f * corr_f, axis=-1) + EPS_LAG)
    ref_rms = jnp.sqrt(jnp.mean(ref_sum * ref_sum, axis=-1) + EPS_LAG)
    coherence = inner_prod / (corr_rms * ref_rms[None, :])
    weights = window_gain[:, None] * jnp.exp(2.0 * coherence)
    numerator = jnp.sum(weights[:, :, None] * corr_f, axis=0)
    denominator = jnp.sum(weights, axis=0)
    return (numerator, denominator)


def block_needs(offs, parts, count, block_chans):
    live = lax.broadcasted_iota(jnp.int32, offs.shape, 0) < count
    hit = parts[:, None] == lax.broadcasted_iota(jnp.int32, (1, block_chans), 1)
    need_minus = jnp.any(hit & (live & (offs == 0))[:, None], axis=0)
    need_plus = jnp.any(hit & (live & (offs == 2))[:, None], axis=0)
    pos_minus = jnp.cumsum(need_minus, dtype=jnp.int32) - 1
    pos_plus = jnp.cumsum(need_plus, dtype=jnp.int32) - 1
    return need_minus, need_plus, pos_minus, pos_plus


def cross_kernel(anchor_ref, own_ref, sbf_ref, saf_ref, bf_ref, af_ref, t_ref, corr_ref):
    wins = anchor_ref.shape[0]
    half = anchor_ref.shape[2] // 2
    t_re = t_ref[:half, :]
    t_im = t_ref[half:, :]
    sbf, saf = sbf_ref[...], saf_ref[...]
    for w in range(wins):
        part = (
            own_ref[w].astype(jnp.float32)
            + jnp.dot(sbf, bf_ref[w], preferred_element_type=jnp.float32)
            + jnp.dot(saf, af_ref[w], preferred_element_type=jnp.float32)
        )
        anc = anchor_ref[w].astype(jnp.float32)
        a_re, a_im = anc[:, :half], anc[:, half:]
        p_re, p_im = part[:, :half], part[:, half:]
        c_re = (a_re * p_re + a_im * p_im).astype(jnp.bfloat16)
        c_im = (a_im * p_re - a_re * p_im).astype(jnp.bfloat16)
        corr_ref[w] = jnp.dot(c_re, t_re, preferred_element_type=jnp.float32) + jnp.dot(
            c_im, t_im, preferred_element_type=jnp.float32
        )


def halo_cross(chunk, wins, anchors, own, sels, bufs, transform):
    _, slots, width = anchors.shape
    lag_count = transform.shape[1]
    group = min(128, slots)
    row_spec = pl.BlockSpec((wins, group, width), lambda i: (chunk, i, 0))
    sel_specs = [pl.BlockSpec((group, sel.shape[1]), lambda i: (i, 0)) for sel in sels]
    buf_specs = [pl.BlockSpec((wins,) + buf.shape[1:], lambda i: (0, 0, 0)) for buf in bufs]
    return pl.pallas_call(
        cross_kernel,
        grid=(slots // group,),
        in_specs=[row_spec, row_spec] + sel_specs + buf_specs + [pl.BlockSpec(transform.shape, lambda i: (0, 0))],
        out_specs=pl.BlockSpec((wins, group, lag_count), lambda i: (0, i, 0)),
        out_shape=jax.ShapeDtypeStruct((wins, slots, lag_count), jnp.float32),
        compiler_params=pltpu.CompilerParams(vmem_limit_bytes=56 * 1024 * 1024),
    )(anchors, own, *sels, *bufs, transform)


def local(spectra, pair_anchor, pair_offset, pair_partner, pair_count, window_bins, bin_gain):
    block_chans, local_wins, spec_width = spectra.shape
    pair_slots = pair_anchor.shape[0]
    fast_rows = (block_chans // 2 + 15) // 16 * 16
    spill_rows = block_chans - fast_rows

    blocks = lax.axis_size("chan")
    block = lax.axis_index("chan")
    table = jnp.concatenate([pair_offset, pair_partner, pair_count])
    tables = gather_blocks(table, "chan")
    table_before = tables[(block + blocks - 1) % blocks]
    table_after = tables[(block + 1) % blocks]

    def needs_of(tab):
        return block_needs(tab[:pair_slots], tab[pair_slots:2 * pair_slots], tab[2 * pair_slots], block_chans)

    own_minus, own_plus, own_pos_minus, own_pos_plus = needs_of(table)
    up_need, _, up_pos, _ = needs_of(table_after)
    _, down_need, _, down_pos = needs_of(table_before)
    all_needs = jax.vmap(needs_of)(tables)
    need_most = jnp.maximum(
        jnp.max(jnp.sum(all_needs[0], axis=1, dtype=jnp.int32)),
        jnp.max(jnp.sum(all_needs[1], axis=1, dtype=jnp.int32)),
    )

    def send_selector(need, pos, first, rows):
        return onehot(pos - first, rows, need).T.astype(jnp.bfloat16)

    def gather_rows(first, rows, source, whitened=False):
        up_rows = jnp.einsum("jc,cwf->wjf", send_selector(up_need, up_pos, first, rows), source,
                             preferred_element_type=jnp.bfloat16)
        down_rows = jnp.einsum("jc,cwf->wjf", send_selector(down_need, down_pos, first, rows), source,
                               preferred_element_type=jnp.bfloat16)
        if not whitened:
            up_rows, down_rows = whiten(up_rows), whiten(down_rows)
        return ring_exchange(up_rows, down_rows, "chan"), (up_rows, down_rows)

    chunks = 2 if local_wins % 2 == 0 else 1
    chunk_wins = local_wins // chunks
    fast_sent = [gather_rows(0, fast_rows, spectra[:, c * chunk_wins:(c + 1) * chunk_wins]) for c in range(chunks)]
    fast = [got for got, _ in fast_sent]
    spectra_late, _ = lax.optimization_barrier((spectra, [sent for _, sent in fast_sent]))
    white = whiten(spectra_late)
    spill = need_most > fast_rows

    transform = lag_table(spec_width // 2, LAG)
    lag_count = transform.shape[1]
    live_count = pair_count[0]
    slot_ids = lax.broadcasted_iota(jnp.int32, (pair_slots,), 0)
    live = slot_ids < live_count

    def pick(selector, rows):
        return jnp.einsum("sc,cwf->wsf", selector.astype(jnp.bfloat16), rows, preferred_element_type=jnp.bfloat16)

    anchors = pick(onehot(pair_anchor, block_chans, live), white)
    own = pick(onehot(pair_partner, block_chans, live & (pair_offset == 1)), white)
    own_hit = onehot(pair_partner, block_chans, live)
    before_row = jnp.sum(jnp.where(own_hit, own_pos_minus[None, :], 0), axis=1)
    after_row = jnp.sum(jnp.where(own_hit, own_pos_plus[None, :], 0), axis=1)
    use_before = live & (pair_offset == 0)
    use_after = live & (pair_offset == 2)
    sels = [
        onehot(before_row, fast_rows, use_before).astype(jnp.bfloat16),
        onehot(after_row, fast_rows, use_after).astype(jnp.bfloat16),
    ]
    corr_full = jnp.concatenate([
        halo_cross(c, chunk_wins, anchors, own, sels, [fast[c][0], fast[c][1]], transform)
        for c in range(chunks)
    ])

    def spill_extra(_):
        (got_before, got_after), _ = gather_rows(fast_rows, spill_rows, white, whitened=True)
        spill_sels = [
            onehot(before_row - fast_rows, spill_rows, use_before).astype(jnp.bfloat16),
            onehot(after_row - fast_rows, spill_rows, use_after).astype(jnp.bfloat16),
        ]
        zero_own = jnp.zeros_like(own)
        extra = jnp.concatenate([
            halo_cross(c, chunk_wins, anchors, zero_own, spill_sels,
                       [got_before[c * chunk_wins:(c + 1) * chunk_wins], got_after[c * chunk_wins:(c + 1) * chunk_wins]],
                       transform)
            for c in range(chunks)
        ])
        return extra

    def no_extra(_):
        return jnp.zeros((local_wins, pair_slots, lag_count), jnp.float32)

    spill_late, _ = lax.optimization_barrier((spill, fast[0]))
    corr_full = corr_full + lax.cond(spill_late, spill_extra, no_extra, 0)
    corr_all = lax.reduce_precision(corr_full, exponent_bits=8, mantissa_bits=7)
    running = jnp.sum(corr_full, axis=0)

    ref_sum = butterfly_sum(running, "win")
    norm_scale = jnp.sqrt(jnp.float32(local_wins * lax.axis_size("win")))
    ref_stack = jnp.where(live[:, None], ref_sum / norm_scale, 0.0)
    window_gain = window_gains(window_bins, bin_gain)
    numerator, denominator = window_weights_wm(corr_all, ref_sum, window_gain)
    if pair_slots % lag_count == 0:
        packed = jnp.concatenate([numerator, denominator.reshape(-1, lag_count)])
        packed = butterfly_sum(packed, "win")
        numerator, denominator = packed[:pair_slots], packed[pair_slots:].reshape(-1)
    else:
        numerator, denominator = butterfly_sum((numerator, denominator), "win")
    restack = jnp.where(live[:, None], norm_scale * numerator / denominator[:, None], 0.0)
    return (ref_stack, restack)


def solution(mesh):
    in_specs = (
        P(("days", "chan"), "win", None),
        P("chan"),
        P("chan"),
        P("chan"),
        P("chan"),
        P(("days", "win")),
        P(),
    )
    out_specs = (P(("days", "chan"), None), P(("days", "chan"), None))
    return jax.shard_map(local, mesh=mesh, in_specs=in_specs, out_specs=out_specs, check_vma=False)
```

```python
import jax
import jax.numpy as jnp
from jax import lax
from jax.experimental import pallas as pl
from jax.experimental.pallas import tpu as pltpu
from jax.sharding import PartitionSpec as P

LAG = 128


EPS_POWER = 1e-05
EPS_LAG = 1e-06


def whiten(spectra):
    spectra_f = spectra.astype(jnp.float32)
    power_mean = jnp.mean(spectra_f * spectra_f, axis=-1, keepdims=True)
    return (spectra_f * lax.rsqrt(power_mean + EPS_POWER)).astype(jnp.bfloat16)


def lag_table(freq_count, lag_count):
    freq_ids = lax.broadcasted_iota(jnp.float32, (freq_count, lag_count), 0)
    lag_ids = lax.broadcasted_iota(jnp.float32, (freq_count, lag_count), 1) - lag_count // 2
    angles = 2.0 * jnp.pi / (2 * freq_count) * freq_ids * lag_ids
    norm_scale = 1.0 / jnp.sqrt(jnp.float32(freq_count))
    return jnp.concatenate(
        [jnp.cos(angles) * norm_scale, -jnp.sin(angles) * norm_scale], axis=0
    ).astype(jnp.bfloat16)


def cross_spectra(anchors, partners):
    half_width = anchors.shape[-1] // 2
    anchor_f = anchors.astype(jnp.float32)
    partner_f = partners.astype(jnp.float32)
    anchor_re = anchor_f[..., :half_width]
    anchor_im = anchor_f[..., half_width:]
    partner_re = partner_f[..., :half_width]
    partner_im = partner_f[..., half_width:]
    cross_re = anchor_re * partner_re + anchor_im * partner_im
    cross_im = anchor_im * partner_re - anchor_re * partner_im
    return jnp.concatenate([cross_re, cross_im], axis=-1).astype(jnp.bfloat16)


def window_gains(bins, gains):
    levels = lax.broadcasted_iota(jnp.int32, (bins.shape[0], gains.shape[0]), 1)
    return jnp.sum(jnp.where(bins[:, None] == levels, gains[None, :], jnp.float32(0.0)), axis=1)


def window_weights(lag_corr, ref_sum, window_gain):
    corr_f = lag_corr.astype(jnp.float32)
    inner_prod = jnp.mean(corr_f * ref_sum[:, None, :], axis=-1)
    corr_rms = jnp.sqrt(jnp.mean(corr_f * corr_f, axis=-1) + EPS_LAG)
    ref_rms = jnp.sqrt(jnp.mean(ref_sum * ref_sum, axis=-1) + EPS_LAG)
    coherence = inner_prod / (corr_rms * ref_rms[:, None])
    weights = window_gain[None, :] * jnp.exp(2.0 * coherence)
    numerator = jnp.sum(weights[:, :, None] * corr_f, axis=1)
    denominator = jnp.sum(weights, axis=1)
    return (numerator, denominator)


def select_rows(selector, rows):
    return jnp.einsum("sc,cwf->swf", selector, rows, preferred_element_type=jnp.bfloat16)


def butterfly_sum(value, axis):
    peers = lax.axis_size(axis)
    if peers & (peers - 1):
        return lax.psum(value, axis)
    step = 1
    while step < peers:
        pairs = [(i, i ^ step) for i in range(peers)]
        value = jax.tree.map(jnp.add, value, lax.ppermute(value, axis, pairs))
        step *= 2
    return value


def ring_exchange(up_rows, down_rows, axis):
    peers = lax.axis_size(axis)
    up = [(i, (i + 1) % peers) for i in range(peers)]
    down = [(j, i) for i, j in up]
    return lax.ppermute(up_rows, axis, up), lax.ppermute(down_rows, axis, down)


def gather_blocks(row, axis):
    peers = lax.axis_size(axis)
    if peers & (peers - 1):
        return lax.all_gather(row, axis)
    me = lax.axis_index(axis)
    acc = row[None]
    step = 1
    while step < peers:
        pairs = [(i, i ^ step) for i in range(peers)]
        got = lax.ppermute(acc, axis, pairs)
        acc = jnp.where((me & step) == 0, jnp.concatenate([acc, got]), jnp.concatenate([got, acc]))
        step *= 2
    return acc


def onehot(index, size, mask):
    return (index[:, None] == lax.broadcasted_iota(jnp.int32, (index.shape[0], size), 1)) & mask[:, None]


def window_weights_wm(corr_f, ref_sum, window_gain):
    inner_prod = jnp.mean(corr_f * ref_sum[None, :, :], axis=-1)
    corr_rms = jnp.sqrt(jnp.mean(corr_f * corr_f, axis=-1) + EPS_LAG)
    ref_rms = jnp.sqrt(jnp.mean(ref_sum * ref_sum, axis=-1) + EPS_LAG)
    coherence = inner_prod / (corr_rms * ref_rms[None, :])
    weights = window_gain[:, None] * jnp.exp(2.0 * coherence)
    numerator = jnp.sum(weights[:, :, None] * corr_f, axis=0)
    denominator = jnp.sum(weights, axis=0)
    return (numerator, denominator)


def block_needs(offs, parts, count, block_chans):
    live = lax.broadcasted_iota(jnp.int32, offs.shape, 0) < count
    hit = parts[:, None] == lax.broadcasted_iota(jnp.int32, (1, block_chans), 1)
    need_minus = jnp.any(hit & (live & (offs == 0))[:, None], axis=0)
    need_plus = jnp.any(hit & (live & (offs == 2))[:, None], axis=0)
    pos_minus = jnp.cumsum(need_minus, dtype=jnp.int32) - 1
    pos_plus = jnp.cumsum(need_plus, dtype=jnp.int32) - 1
    return need_minus, need_plus, pos_minus, pos_plus


def cross_kernel(anchor_ref, own_ref, sbf_ref, saf_ref, bf_ref, af_ref, t_ref, corr_ref):
    wins = anchor_ref.shape[0]
    half = anchor_ref.shape[2] // 2
    t_re = t_ref[:half, :]
    t_im = t_ref[half:, :]
    sbf, saf = sbf_ref[...], saf_ref[...]
    for w in range(wins):
        part = (
            own_ref[w].astype(jnp.float32)
            + jnp.dot(sbf, bf_ref[w], preferred_element_type=jnp.float32)
            + jnp.dot(saf, af_ref[w], preferred_element_type=jnp.float32)
        )
        anc = anchor_ref[w].astype(jnp.float32)
        a_re, a_im = anc[:, :half], anc[:, half:]
        p_re, p_im = part[:, :half], part[:, half:]
        c_re = (a_re * p_re + a_im * p_im).astype(jnp.bfloat16)
        c_im = (a_im * p_re - a_re * p_im).astype(jnp.bfloat16)
        corr_ref[w] = jnp.dot(c_re, t_re, preferred_element_type=jnp.float32) + jnp.dot(
            c_im, t_im, preferred_element_type=jnp.float32
        )


def halo_cross(chunk, wins, anchors, own, sels, bufs, transform):
    _, slots, width = anchors.shape
    lag_count = transform.shape[1]
    group = min(128, slots)
    row_spec = pl.BlockSpec((wins, group, width), lambda i: (chunk, i, 0))
    sel_specs = [pl.BlockSpec((group, sel.shape[1]), lambda i: (i, 0)) for sel in sels]
    buf_specs = [pl.BlockSpec((wins,) + buf.shape[1:], lambda i: (0, 0, 0)) for buf in bufs]
    return pl.pallas_call(
        cross_kernel,
        grid=(slots // group,),
        in_specs=[row_spec, row_spec] + sel_specs + buf_specs + [pl.BlockSpec(transform.shape, lambda i: (0, 0))],
        out_specs=pl.BlockSpec((wins, group, lag_count), lambda i: (0, i, 0)),
        out_shape=jax.ShapeDtypeStruct((wins, slots, lag_count), jnp.float32),
        compiler_params=pltpu.CompilerParams(vmem_limit_bytes=56 * 1024 * 1024),
    )(anchors, own, *sels, *bufs, transform)


def local(spectra, pair_anchor, pair_offset, pair_partner, pair_count, window_bins, bin_gain):
    block_chans, local_wins, spec_width = spectra.shape
    pair_slots = pair_anchor.shape[0]
    fast_rows = (block_chans // 2 + 15) // 16 * 16
    spill_rows = block_chans - fast_rows

    blocks = lax.axis_size("chan")
    block = lax.axis_index("chan")
    table = jnp.concatenate([pair_offset, pair_partner, pair_count])
    tables = gather_blocks(table, "chan")
    table_before, table_after = ring_exchange(table, table, "chan")

    def needs_of(tab):
        return block_needs(tab[:pair_slots], tab[pair_slots:2 * pair_slots], tab[2 * pair_slots], block_chans)

    own_minus, own_plus, own_pos_minus, own_pos_plus = needs_of(table)
    up_need, _, up_pos, _ = needs_of(table_after)
    _, down_need, _, down_pos = needs_of(table_before)
    all_needs = jax.vmap(needs_of)(tables)
    need_most = jnp.maximum(
        jnp.max(jnp.sum(all_needs[0], axis=1, dtype=jnp.int32)),
        jnp.max(jnp.sum(all_needs[1], axis=1, dtype=jnp.int32)),
    )

    def send_selector(need, pos, first, rows):
        return onehot(pos - first, rows, need).T.astype(jnp.bfloat16)

    def gather_rows(first, rows, source, whitened=False):
        up_rows = jnp.einsum("jc,cwf->wjf", send_selector(up_need, up_pos, first, rows), source,
                             preferred_element_type=jnp.bfloat16)
        down_rows = jnp.einsum("jc,cwf->wjf", send_selector(down_need, down_pos, first, rows), source,
                               preferred_element_type=jnp.bfloat16)
        if not whitened:
            up_rows, down_rows = whiten(up_rows), whiten(down_rows)
        return ring_exchange(up_rows, down_rows, "chan"), (up_rows, down_rows)

    chunks = 2 if local_wins % 2 == 0 else 1
    chunk_wins = local_wins // chunks
    fast_sent = [gather_rows(0, fast_rows, spectra[:, c * chunk_wins:(c + 1) * chunk_wins]) for c in range(chunks)]
    fast = [got for got, _ in fast_sent]
    spectra_late, _ = lax.optimization_barrier((spectra, [sent for _, sent in fast_sent]))
    white = whiten(spectra_late)
    spill = need_most > fast_rows

    transform = lag_table(spec_width // 2, LAG)
    lag_count = transform.shape[1]
    live_count = pair_count[0]
    slot_ids = lax.broadcasted_iota(jnp.int32, (pair_slots,), 0)
    live = slot_ids < live_count

    def pick(selector, rows):
        return jnp.einsum("sc,cwf->wsf", selector.astype(jnp.bfloat16), rows, preferred_element_type=jnp.bfloat16)

    anchors = pick(onehot(pair_anchor, block_chans, live), white)
    own = pick(onehot(pair_partner, block_chans, live & (pair_offset == 1)), white)
    own_hit = onehot(pair_partner, block_chans, live)
    before_row = jnp.sum(jnp.where(own_hit, own_pos_minus[None, :], 0), axis=1)
    after_row = jnp.sum(jnp.where(own_hit, own_pos_plus[None, :], 0), axis=1)
    use_before = live & (pair_offset == 0)
    use_after = live & (pair_offset == 2)
    sels = [
        onehot(before_row, fast_rows, use_before).astype(jnp.bfloat16),
        onehot(after_row, fast_rows, use_after).astype(jnp.bfloat16),
    ]
    corr_full = jnp.concatenate([
        halo_cross(c, chunk_wins, anchors, own, sels, [fast[c][0], fast[c][1]], transform)
        for c in range(chunks)
    ])

    def spill_extra(_):
        (got_before, got_after), _ = gather_rows(fast_rows, spill_rows, white, whitened=True)
        spill_sels = [
            onehot(before_row - fast_rows, spill_rows, use_before).astype(jnp.bfloat16),
            onehot(after_row - fast_rows, spill_rows, use_after).astype(jnp.bfloat16),
        ]
        zero_own = jnp.zeros_like(own)
        extra = jnp.concatenate([
            halo_cross(c, chunk_wins, anchors, zero_own, spill_sels,
                       [got_before[c * chunk_wins:(c + 1) * chunk_wins], got_after[c * chunk_wins:(c + 1) * chunk_wins]],
                       transform)
            for c in range(chunks)
        ])
        return extra

    def no_extra(_):
        return jnp.zeros((local_wins, pair_slots, lag_count), jnp.float32)

    spill_late, _ = lax.optimization_barrier((spill, fast[0]))
    corr_full = corr_full + lax.cond(spill_late, spill_extra, no_extra, 0)
    corr_all = lax.reduce_precision(corr_full, exponent_bits=8, mantissa_bits=7)
    running = jnp.sum(corr_full, axis=0)

    ref_sum = butterfly_sum(running, "win")
    norm_scale = jnp.sqrt(jnp.float32(local_wins * lax.axis_size("win")))
    ref_stack = jnp.where(live[:, None], ref_sum / norm_scale, 0.0)
    window_gain = window_gains(window_bins, bin_gain)
    numerator, denominator = window_weights_wm(corr_all, ref_sum, window_gain)
    numerator, denominator = butterfly_sum((numerator, denominator), "win")
    restack = jnp.where(live[:, None], norm_scale * numerator / denominator[:, None], 0.0)
    return (ref_stack, restack)


def solution(mesh):
    in_specs = (
        P(("days", "chan"), "win", None),
        P("chan"),
        P("chan"),
        P("chan"),
        P("chan"),
        P(("days", "win")),
        P(),
    )
    out_specs = (P(("days", "chan"), None), P(("days", "chan"), None))
    return jax.shard_map(local, mesh=mesh, in_specs=in_specs, out_specs=out_specs, check_vma=False)
```

```python
import jax
import jax.numpy as jnp
from jax import lax
from jax.experimental import pallas as pl
from jax.experimental.pallas import tpu as pltpu
from jax.sharding import PartitionSpec as P

LAG = 128


EPS_POWER = 1e-05
EPS_LAG = 1e-06


def whiten(spectra):
    spectra_f = spectra.astype(jnp.float32)
    power_mean = jnp.mean(spectra_f * spectra_f, axis=-1, keepdims=True)
    return (spectra_f * lax.rsqrt(power_mean + EPS_POWER)).astype(jnp.bfloat16)


def lag_table(freq_count, lag_count):
    freq_ids = lax.broadcasted_iota(jnp.float32, (freq_count, lag_count), 0)
    lag_ids = lax.broadcasted_iota(jnp.float32, (freq_count, lag_count), 1) - lag_count // 2
    angles = 2.0 * jnp.pi / (2 * freq_count) * freq_ids * lag_ids
    norm_scale = 1.0 / jnp.sqrt(jnp.float32(freq_count))
    return jnp.concatenate(
        [jnp.cos(angles) * norm_scale, -jnp.sin(angles) * norm_scale], axis=0
    ).astype(jnp.bfloat16)


def cross_spectra(anchors, partners):
    half_width = anchors.shape[-1] // 2
    anchor_f = anchors.astype(jnp.float32)
    partner_f = partners.astype(jnp.float32)
    anchor_re = anchor_f[..., :half_width]
    anchor_im = anchor_f[..., half_width:]
    partner_re = partner_f[..., :half_width]
    partner_im = partner_f[..., half_width:]
    cross_re = anchor_re * partner_re + anchor_im * partner_im
    cross_im = anchor_im * partner_re - anchor_re * partner_im
    return jnp.concatenate([cross_re, cross_im], axis=-1).astype(jnp.bfloat16)


def window_gains(bins, gains):
    levels = lax.broadcasted_iota(jnp.int32, (bins.shape[0], gains.shape[0]), 1)
    return jnp.sum(jnp.where(bins[:, None] == levels, gains[None, :], jnp.float32(0.0)), axis=1)


def window_weights(lag_corr, ref_sum, window_gain):
    corr_f = lag_corr.astype(jnp.float32)
    inner_prod = jnp.mean(corr_f * ref_sum[:, None, :], axis=-1)
    corr_rms = jnp.sqrt(jnp.mean(corr_f * corr_f, axis=-1) + EPS_LAG)
    ref_rms = jnp.sqrt(jnp.mean(ref_sum * ref_sum, axis=-1) + EPS_LAG)
    coherence = inner_prod / (corr_rms * ref_rms[:, None])
    weights = window_gain[None, :] * jnp.exp(2.0 * coherence)
    numerator = jnp.sum(weights[:, :, None] * corr_f, axis=1)
    denominator = jnp.sum(weights, axis=1)
    return (numerator, denominator)


def select_rows(selector, rows):
    return jnp.einsum("sc,cwf->swf", selector, rows, preferred_element_type=jnp.bfloat16)


def butterfly_sum(value, axis):
    peers = lax.axis_size(axis)
    if peers & (peers - 1):
        return lax.psum(value, axis)
    step = 1
    while step < peers:
        pairs = [(i, i ^ step) for i in range(peers)]
        value = jax.tree.map(jnp.add, value, lax.ppermute(value, axis, pairs))
        step *= 2
    return value


def ring_exchange(up_rows, down_rows, axis):
    peers = lax.axis_size(axis)
    up = [(i, (i + 1) % peers) for i in range(peers)]
    down = [(j, i) for i, j in up]
    return lax.ppermute(up_rows, axis, up), lax.ppermute(down_rows, axis, down)


def gather_blocks(row, axis):
    peers = lax.axis_size(axis)
    if peers & (peers - 1):
        return lax.all_gather(row, axis)
    me = lax.axis_index(axis)
    acc = row[None]
    step = 1
    while step < peers:
        pairs = [(i, i ^ step) for i in range(peers)]
        got = lax.ppermute(acc, axis, pairs)
        acc = jnp.where((me & step) == 0, jnp.concatenate([acc, got]), jnp.concatenate([got, acc]))
        step *= 2
    return acc


def onehot(index, size, mask):
    return (index[:, None] == lax.broadcasted_iota(jnp.int32, (index.shape[0], size), 1)) & mask[:, None]


def window_weights_wm(corr_f, ref_sum, window_gain):
    inner_prod = jnp.mean(corr_f * ref_sum[None, :, :], axis=-1)
    corr_rms = jnp.sqrt(jnp.mean(corr_f * corr_f, axis=-1) + EPS_LAG)
    ref_rms = jnp.sqrt(jnp.mean(ref_sum * ref_sum, axis=-1) + EPS_LAG)
    coherence = inner_prod / (corr_rms * ref_rms[None, :])
    weights = window_gain[:, None] * jnp.exp(2.0 * coherence)
    numerator = jnp.sum(weights[:, :, None] * corr_f, axis=0)
    denominator = jnp.sum(weights, axis=0)
    return (numerator, denominator)


def block_needs(offs, parts, count, block_chans):
    live = lax.broadcasted_iota(jnp.int32, offs.shape, 0) < count
    hit = parts[:, None] == lax.broadcasted_iota(jnp.int32, (1, block_chans), 1)
    need_minus = jnp.any(hit & (live & (offs == 0))[:, None], axis=0)
    need_plus = jnp.any(hit & (live & (offs == 2))[:, None], axis=0)
    pos_minus = jnp.cumsum(need_minus, dtype=jnp.int32) - 1
    pos_plus = jnp.cumsum(need_plus, dtype=jnp.int32) - 1
    return need_minus, need_plus, pos_minus, pos_plus


def make_cross_kernel(has_own, has_halo):
    def cross_kernel(*refs):
        refs = list(refs)
        anchor_ref = refs.pop(0)
        own_ref = refs.pop(0) if has_own else None
        if has_halo:
            sbf_ref, saf_ref, bf_ref, af_ref = refs[:4]
            refs = refs[4:]
        t_ref, corr_ref = refs
        wins = anchor_ref.shape[0]
        half = anchor_ref.shape[2] // 2
        t_re = t_ref[:half, :]
        t_im = t_ref[half:, :]
        for w in range(wins):
            part = None
            if has_own:
                part = own_ref[w].astype(jnp.float32)
            if has_halo:
                got = jnp.dot(sbf_ref[...], bf_ref[w], preferred_element_type=jnp.float32) + jnp.dot(
                    saf_ref[...], af_ref[w], preferred_element_type=jnp.float32
                )
                part = got if part is None else part + got
            anc = anchor_ref[w].astype(jnp.float32)
            a_re, a_im = anc[:, :half], anc[:, half:]
            p_re, p_im = part[:, :half], part[:, half:]
            c_re = (a_re * p_re + a_im * p_im).astype(jnp.bfloat16)
            c_im = (a_im * p_re - a_re * p_im).astype(jnp.bfloat16)
            corr_ref[w] = jnp.dot(c_re, t_re, preferred_element_type=jnp.float32) + jnp.dot(
                c_im, t_im, preferred_element_type=jnp.float32
            )

    return cross_kernel


def halo_cross(chunk, wins, anchors, own, sels, bufs, transform):
    _, slots, width = anchors.shape
    lag_count = transform.shape[1]
    group = min(128, slots)
    row_spec = pl.BlockSpec((wins, group, width), lambda i: (chunk, i, 0))
    sel_specs = [pl.BlockSpec((group, sel.shape[1]), lambda i: (i, 0)) for sel in sels]
    buf_specs = [pl.BlockSpec((wins,) + buf.shape[1:], lambda i: (0, 0, 0)) for buf in bufs]
    rows = [anchors] + ([own] if own is not None else [])
    return pl.pallas_call(
        make_cross_kernel(own is not None, bool(bufs)),
        grid=(slots // group,),
        in_specs=[row_spec] * len(rows) + sel_specs + buf_specs + [pl.BlockSpec(transform.shape, lambda i: (0, 0))],
        out_specs=pl.BlockSpec((wins, group, lag_count), lambda i: (0, i, 0)),
        out_shape=jax.ShapeDtypeStruct((wins, slots, lag_count), jnp.float32),
        compiler_params=pltpu.CompilerParams(vmem_limit_bytes=56 * 1024 * 1024),
    )(*rows, *sels, *bufs, transform)


def local(spectra, pair_anchor, pair_offset, pair_partner, pair_count, window_bins, bin_gain):
    block_chans, local_wins, spec_width = spectra.shape
    pair_slots = pair_anchor.shape[0]
    fast_rows = (block_chans // 2 + 15) // 16 * 16
    spill_rows = block_chans - fast_rows

    blocks = lax.axis_size("chan")
    block = lax.axis_index("chan")
    table = jnp.concatenate([pair_offset, pair_partner, pair_count])
    tables = gather_blocks(table, "chan")
    table_before = tables[(block + blocks - 1) % blocks]
    table_after = tables[(block + 1) % blocks]

    def needs_of(tab):
        return block_needs(tab[:pair_slots], tab[pair_slots:2 * pair_slots], tab[2 * pair_slots], block_chans)

    own_minus, own_plus, own_pos_minus, own_pos_plus = needs_of(table)
    up_need, _, up_pos, _ = needs_of(table_after)
    _, down_need, _, down_pos = needs_of(table_before)
    all_needs = jax.vmap(needs_of)(tables)
    need_most = jnp.maximum(
        jnp.max(jnp.sum(all_needs[0], axis=1, dtype=jnp.int32)),
        jnp.max(jnp.sum(all_needs[1], axis=1, dtype=jnp.int32)),
    )

    def send_selector(need, pos, first, rows):
        return onehot(pos - first, rows, need).T.astype(jnp.bfloat16)

    def gather_rows(first, rows, source, whitened=False):
        up_rows = jnp.einsum("jc,cwf->wjf", send_selector(up_need, up_pos, first, rows), source,
                             preferred_element_type=jnp.bfloat16)
        down_rows = jnp.einsum("jc,cwf->wjf", send_selector(down_need, down_pos, first, rows), source,
                               preferred_element_type=jnp.bfloat16)
        if not whitened:
            up_rows, down_rows = whiten(up_rows), whiten(down_rows)
        return ring_exchange(up_rows, down_rows, "chan"), (up_rows, down_rows)

    chunks = 2 if local_wins % 2 == 0 else 1
    chunk_wins = local_wins // chunks
    fast_sent = [gather_rows(0, fast_rows, spectra[:, c * chunk_wins:(c + 1) * chunk_wins]) for c in range(chunks)]
    fast = [got for got, _ in fast_sent]
    spectra_late, _ = lax.optimization_barrier((spectra, [sent for _, sent in fast_sent]))
    white = whiten(spectra_late)
    spill = need_most > fast_rows

    transform = lag_table(spec_width // 2, LAG)
    lag_count = transform.shape[1]
    live_count = pair_count[0]
    slot_ids = lax.broadcasted_iota(jnp.int32, (pair_slots,), 0)
    live = slot_ids < live_count

    def pick(selector, rows):
        return jnp.einsum("sc,cwf->wsf", selector.astype(jnp.bfloat16), rows, preferred_element_type=jnp.bfloat16)

    anchors = pick(onehot(pair_anchor, block_chans, live), white)
    own = pick(onehot(pair_partner, block_chans, live & (pair_offset == 1)), white)
    own_hit = onehot(pair_partner, block_chans, live)
    before_row = jnp.sum(jnp.where(own_hit, own_pos_minus[None, :], 0), axis=1)
    after_row = jnp.sum(jnp.where(own_hit, own_pos_plus[None, :], 0), axis=1)
    use_before = live & (pair_offset == 0)
    use_after = live & (pair_offset == 2)
    sels = [
        onehot(before_row, fast_rows, use_before).astype(jnp.bfloat16),
        onehot(after_row, fast_rows, use_after).astype(jnp.bfloat16),
    ]

    def spill_extra(_):
        (got_before, got_after), _ = gather_rows(fast_rows, spill_rows, white, whitened=True)
        spill_sels = [
            onehot(before_row - fast_rows, spill_rows, use_before).astype(jnp.bfloat16),
            onehot(after_row - fast_rows, spill_rows, use_after).astype(jnp.bfloat16),
        ]
        extra = jnp.concatenate([
            halo_cross(c, chunk_wins, anchors, None, spill_sels,
                       [got_before[c * chunk_wins:(c + 1) * chunk_wins], got_after[c * chunk_wins:(c + 1) * chunk_wins]],
                       transform)
            for c in range(chunks)
        ])
        return extra

    def no_extra(_):
        return jnp.zeros((local_wins, pair_slots, lag_count), jnp.float32)

    spill_late, _ = lax.optimization_barrier((spill, fast[0]))
    extra = lax.cond(spill_late, spill_extra, no_extra, 0)
    parts = [halo_cross(c, chunk_wins, anchors, own, sels, [fast[c][0], fast[c][1]], transform)
             for c in range(chunks - 1)]
    last = chunks - 1
    own_part = halo_cross(last, chunk_wins, anchors, own, [], [], transform)
    last_bufs, _ = lax.optimization_barrier(([fast[last][0], fast[last][1]], [parts, extra]))
    parts.append(own_part + halo_cross(last, chunk_wins, anchors, None, sels, last_bufs, transform))
    corr_full = jnp.concatenate(parts)
    corr_full = corr_full + extra
    corr_all = lax.reduce_precision(corr_full, exponent_bits=8, mantissa_bits=7)
    running = jnp.sum(corr_full, axis=0)

    ref_sum = butterfly_sum(running, "win")
    norm_scale = jnp.sqrt(jnp.float32(local_wins * lax.axis_size("win")))
    ref_stack = jnp.where(live[:, None], ref_sum / norm_scale, 0.0)
    window_gain = window_gains(window_bins, bin_gain)
    numerator, denominator = window_weights_wm(corr_all, ref_sum, window_gain)
    numerator, denominator = butterfly_sum((numerator, denominator), "win")
    restack = jnp.where(live[:, None], norm_scale * numerator / denominator[:, None], 0.0)
    return (ref_stack, restack)


def solution(mesh):
    in_specs = (
        P(("days", "chan"), "win", None),
        P("chan"),
        P("chan"),
        P("chan"),
        P("chan"),
        P(("days", "win")),
        P(),
    )
    out_specs = (P(("days", "chan"), None), P(("days", "chan"), None))
    return jax.shard_map(local, mesh=mesh, in_specs=in_specs, out_specs=out_specs, check_vma=False)
```

```python
import jax
import jax.numpy as jnp
from jax import lax
from jax.experimental import pallas as pl
from jax.experimental.pallas import tpu as pltpu
from jax.sharding import PartitionSpec as P

LAG = 128


EPS_POWER = 1e-05
EPS_LAG = 1e-06


def whiten(spectra):
    spectra_f = spectra.astype(jnp.float32)
    power_mean = jnp.mean(spectra_f * spectra_f, axis=-1, keepdims=True)
    return (spectra_f * lax.rsqrt(power_mean + EPS_POWER)).astype(jnp.bfloat16)


def lag_table(freq_count, lag_count):
    freq_ids = lax.broadcasted_iota(jnp.float32, (freq_count, lag_count), 0)
    lag_ids = lax.broadcasted_iota(jnp.float32, (freq_count, lag_count), 1) - lag_count // 2
    angles = 2.0 * jnp.pi / (2 * freq_count) * freq_ids * lag_ids
    norm_scale = 1.0 / jnp.sqrt(jnp.float32(freq_count))
    return jnp.concatenate(
        [jnp.cos(angles) * norm_scale, -jnp.sin(angles) * norm_scale], axis=0
    ).astype(jnp.bfloat16)


def cross_spectra(anchors, partners):
    half_width = anchors.shape[-1] // 2
    anchor_f = anchors.astype(jnp.float32)
    partner_f = partners.astype(jnp.float32)
    anchor_re = anchor_f[..., :half_width]
    anchor_im = anchor_f[..., half_width:]
    partner_re = partner_f[..., :half_width]
    partner_im = partner_f[..., half_width:]
    cross_re = anchor_re * partner_re + anchor_im * partner_im
    cross_im = anchor_im * partner_re - anchor_re * partner_im
    return jnp.concatenate([cross_re, cross_im], axis=-1).astype(jnp.bfloat16)


def window_gains(bins, gains):
    levels = lax.broadcasted_iota(jnp.int32, (bins.shape[0], gains.shape[0]), 1)
    return jnp.sum(jnp.where(bins[:, None] == levels, gains[None, :], jnp.float32(0.0)), axis=1)


def window_weights(lag_corr, ref_sum, window_gain):
    corr_f = lag_corr.astype(jnp.float32)
    inner_prod = jnp.mean(corr_f * ref_sum[:, None, :], axis=-1)
    corr_rms = jnp.sqrt(jnp.mean(corr_f * corr_f, axis=-1) + EPS_LAG)
    ref_rms = jnp.sqrt(jnp.mean(ref_sum * ref_sum, axis=-1) + EPS_LAG)
    coherence = inner_prod / (corr_rms * ref_rms[:, None])
    weights = window_gain[None, :] * jnp.exp(2.0 * coherence)
    numerator = jnp.sum(weights[:, :, None] * corr_f, axis=1)
    denominator = jnp.sum(weights, axis=1)
    return (numerator, denominator)


def select_rows(selector, rows):
    return jnp.einsum("sc,cwf->swf", selector, rows, preferred_element_type=jnp.bfloat16)


def butterfly_sum(value, axis):
    peers = lax.axis_size(axis)
    if peers & (peers - 1):
        return lax.psum(value, axis)
    step = 1
    while step < peers:
        pairs = [(i, i ^ step) for i in range(peers)]
        value = jax.tree.map(jnp.add, value, lax.ppermute(value, axis, pairs))
        step *= 2
    return value


def ring_exchange(up_rows, down_rows, axis):
    peers = lax.axis_size(axis)
    up = [(i, (i + 1) % peers) for i in range(peers)]
    down = [(j, i) for i, j in up]
    return lax.ppermute(up_rows, axis, up), lax.ppermute(down_rows, axis, down)


def gather_blocks(row, axis):
    peers = lax.axis_size(axis)
    if peers & (peers - 1):
        return lax.all_gather(row, axis)
    me = lax.axis_index(axis)
    acc = row[None]
    step = 1
    while step < peers:
        pairs = [(i, i ^ step) for i in range(peers)]
        got = lax.ppermute(acc, axis, pairs)
        acc = jnp.where((me & step) == 0, jnp.concatenate([acc, got]), jnp.concatenate([got, acc]))
        step *= 2
    return acc


def onehot(index, size, mask):
    return (index[:, None] == lax.broadcasted_iota(jnp.int32, (index.shape[0], size), 1)) & mask[:, None]


def window_weights_wm(corr_f, ref_sum, window_gain):
    inner_prod = jnp.mean(corr_f * ref_sum[None, :, :], axis=-1)
    corr_rms = jnp.sqrt(jnp.mean(corr_f * corr_f, axis=-1) + EPS_LAG)
    ref_rms = jnp.sqrt(jnp.mean(ref_sum * ref_sum, axis=-1) + EPS_LAG)
    coherence = inner_prod / (corr_rms * ref_rms[None, :])
    weights = window_gain[:, None] * jnp.exp(2.0 * coherence)
    numerator = jnp.sum(weights[:, :, None] * corr_f, axis=0)
    denominator = jnp.sum(weights, axis=0)
    return (numerator, denominator)


def block_needs(offs, parts, count, block_chans):
    live = lax.broadcasted_iota(jnp.int32, offs.shape, 0) < count
    hit = parts[:, None] == lax.broadcasted_iota(jnp.int32, (1, block_chans), 1)
    need_minus = jnp.any(hit & (live & (offs == 0))[:, None], axis=0)
    need_plus = jnp.any(hit & (live & (offs == 2))[:, None], axis=0)
    pos_minus = jnp.cumsum(need_minus, dtype=jnp.int32) - 1
    pos_plus = jnp.cumsum(need_plus, dtype=jnp.int32) - 1
    return need_minus, need_plus, pos_minus, pos_plus


def cross_kernel(anchor_ref, own_ref, sbf_ref, saf_ref, bf_ref, af_ref, t_ref, corr_ref):
    wins = anchor_ref.shape[0]
    half = anchor_ref.shape[2] // 2
    t_re = t_ref[:half, :]
    t_im = t_ref[half:, :]
    sbf, saf = sbf_ref[...], saf_ref[...]
    for w in range(wins):
        part = (
            own_ref[w].astype(jnp.float32)
            + jnp.dot(sbf, bf_ref[w], preferred_element_type=jnp.float32)
            + jnp.dot(saf, af_ref[w], preferred_element_type=jnp.float32)
        )
        anc = anchor_ref[w].astype(jnp.float32)
        a_re, a_im = anc[:, :half], anc[:, half:]
        p_re, p_im = part[:, :half], part[:, half:]
        c_re = (a_re * p_re + a_im * p_im).astype(jnp.bfloat16)
        c_im = (a_im * p_re - a_re * p_im).astype(jnp.bfloat16)
        corr_ref[w] = jnp.dot(c_re, t_re, preferred_element_type=jnp.float32) + jnp.dot(
            c_im, t_im, preferred_element_type=jnp.float32
        )


def halo_cross(chunk, wins, anchors, own, sels, bufs, transform):
    _, slots, width = anchors.shape
    lag_count = transform.shape[1]
    group = min(256, slots)
    row_spec = pl.BlockSpec((wins, group, width), lambda i: (chunk, i, 0))
    sel_specs = [pl.BlockSpec((group, sel.shape[1]), lambda i: (i, 0)) for sel in sels]
    buf_specs = [pl.BlockSpec((wins,) + buf.shape[1:], lambda i: (0, 0, 0)) for buf in bufs]
    return pl.pallas_call(
        cross_kernel,
        grid=(slots // group,),
        in_specs=[row_spec, row_spec] + sel_specs + buf_specs + [pl.BlockSpec(transform.shape, lambda i: (0, 0))],
        out_specs=pl.BlockSpec((wins, group, lag_count), lambda i: (0, i, 0)),
        out_shape=jax.ShapeDtypeStruct((wins, slots, lag_count), jnp.float32),
        compiler_params=pltpu.CompilerParams(vmem_limit_bytes=56 * 1024 * 1024),
    )(anchors, own, *sels, *bufs, transform)


def local(spectra, pair_anchor, pair_offset, pair_partner, pair_count, window_bins, bin_gain):
    block_chans, local_wins, spec_width = spectra.shape
    pair_slots = pair_anchor.shape[0]
    fast_rows = (block_chans // 2 + 15) // 16 * 16
    spill_rows = block_chans - fast_rows

    blocks = lax.axis_size("chan")
    block = lax.axis_index("chan")
    table = jnp.concatenate([pair_offset, pair_partner, pair_count])
    tables = gather_blocks(table, "chan")
    table_before = tables[(block + blocks - 1) % blocks]
    table_after = tables[(block + 1) % blocks]

    def needs_of(tab):
        return block_needs(tab[:pair_slots], tab[pair_slots:2 * pair_slots], tab[2 * pair_slots], block_chans)

    own_minus, own_plus, own_pos_minus, own_pos_plus = needs_of(table)
    up_need, _, up_pos, _ = needs_of(table_after)
    _, down_need, _, down_pos = needs_of(table_before)
    all_needs = jax.vmap(needs_of)(tables)
    need_most = jnp.maximum(
        jnp.max(jnp.sum(all_needs[0], axis=1, dtype=jnp.int32)),
        jnp.max(jnp.sum(all_needs[1], axis=1, dtype=jnp.int32)),
    )

    def send_selector(need, pos, first, rows):
        return onehot(pos - first, rows, need).T.astype(jnp.bfloat16)

    def gather_rows(first, rows, source, whitened=False):
        up_rows = jnp.einsum("jc,cwf->wjf", send_selector(up_need, up_pos, first, rows), source,
                             preferred_element_type=jnp.bfloat16)
        down_rows = jnp.einsum("jc,cwf->wjf", send_selector(down_need, down_pos, first, rows), source,
                               preferred_element_type=jnp.bfloat16)
        if not whitened:
            up_rows, down_rows = whiten(up_rows), whiten(down_rows)
        return ring_exchange(up_rows, down_rows, "chan"), (up_rows, down_rows)

    chunks = 2 if local_wins % 2 == 0 else 1
    chunk_wins = local_wins // chunks
    fast_sent = [gather_rows(0, fast_rows, spectra[:, c * chunk_wins:(c + 1) * chunk_wins]) for c in range(chunks)]
    fast = [got for got, _ in fast_sent]
    spectra_late, _ = lax.optimization_barrier((spectra, [sent for _, sent in fast_sent]))
    white = whiten(spectra_late)
    spill = need_most > fast_rows

    transform = lag_table(spec_width // 2, LAG)
    lag_count = transform.shape[1]
    live_count = pair_count[0]
    slot_ids = lax.broadcasted_iota(jnp.int32, (pair_slots,), 0)
    live = slot_ids < live_count

    def pick(selector, rows):
        return jnp.einsum("sc,cwf->wsf", selector.astype(jnp.bfloat16), rows, preferred_element_type=jnp.bfloat16)

    anchors = pick(onehot(pair_anchor, block_chans, live), white)
    own = pick(onehot(pair_partner, block_chans, live & (pair_offset == 1)), white)
    own_hit = onehot(pair_partner, block_chans, live)
    before_row = jnp.sum(jnp.where(own_hit, own_pos_minus[None, :], 0), axis=1)
    after_row = jnp.sum(jnp.where(own_hit, own_pos_plus[None, :], 0), axis=1)
    use_before = live & (pair_offset == 0)
    use_after = live & (pair_offset == 2)
    sels = [
        onehot(before_row, fast_rows, use_before).astype(jnp.bfloat16),
        onehot(after_row, fast_rows, use_after).astype(jnp.bfloat16),
    ]
    corr_full = jnp.concatenate([
        halo_cross(c, chunk_wins, anchors, own, sels, [fast[c][0], fast[c][1]], transform)
        for c in range(chunks)
    ])

    def spill_extra(_):
        (got_before, got_after), _ = gather_rows(fast_rows, spill_rows, white, whitened=True)
        spill_sels = [
            onehot(before_row - fast_rows, spill_rows, use_before).astype(jnp.bfloat16),
            onehot(after_row - fast_rows, spill_rows, use_after).astype(jnp.bfloat16),
        ]
        zero_own = jnp.zeros_like(own)
        extra = jnp.concatenate([
            halo_cross(c, chunk_wins, anchors, zero_own, spill_sels,
                       [got_before[c * chunk_wins:(c + 1) * chunk_wins], got_after[c * chunk_wins:(c + 1) * chunk_wins]],
                       transform)
            for c in range(chunks)
        ])
        return extra

    def no_extra(_):
        return jnp.zeros((local_wins, pair_slots, lag_count), jnp.float32)

    spill_late, _ = lax.optimization_barrier((spill, fast[0]))
    corr_full = corr_full + lax.cond(spill_late, spill_extra, no_extra, 0)
    corr_all = lax.reduce_precision(corr_full, exponent_bits=8, mantissa_bits=7)
    running = jnp.sum(corr_full, axis=0)

    ref_sum = butterfly_sum(running, "win")
    norm_scale = jnp.sqrt(jnp.float32(local_wins * lax.axis_size("win")))
    ref_stack = jnp.where(live[:, None], ref_sum / norm_scale, 0.0)
    window_gain = window_gains(window_bins, bin_gain)
    numerator, denominator = window_weights_wm(corr_all, ref_sum, window_gain)
    numerator, denominator = butterfly_sum((numerator, denominator), "win")
    restack = jnp.where(live[:, None], norm_scale * numerator / denominator[:, None], 0.0)
    return (ref_stack, restack)


def solution(mesh):
    in_specs = (
        P(("days", "chan"), "win", None),
        P("chan"),
        P("chan"),
        P("chan"),
        P("chan"),
        P(("days", "win")),
        P(),
    )
    out_specs = (P(("days", "chan"), None), P(("days", "chan"), None))
    return jax.shard_map(local, mesh=mesh, in_specs=in_specs, out_specs=out_specs, check_vma=False)
```

```python
import jax
import jax.numpy as jnp
from jax import lax
from jax.experimental import pallas as pl
from jax.experimental.pallas import tpu as pltpu
from jax.sharding import PartitionSpec as P

LAG = 128


EPS_POWER = 1e-05
EPS_LAG = 1e-06


def whiten(spectra):
    spectra_f = spectra.astype(jnp.float32)
    power_mean = jnp.mean(spectra_f * spectra_f, axis=-1, keepdims=True)
    return (spectra_f * lax.rsqrt(power_mean + EPS_POWER)).astype(jnp.bfloat16)


def lag_table(freq_count, lag_count):
    freq_ids = lax.broadcasted_iota(jnp.float32, (freq_count, lag_count), 0)
    lag_ids = lax.broadcasted_iota(jnp.float32, (freq_count, lag_count), 1) - lag_count // 2
    angles = 2.0 * jnp.pi / (2 * freq_count) * freq_ids * lag_ids
    norm_scale = 1.0 / jnp.sqrt(jnp.float32(freq_count))
    return jnp.concatenate(
        [jnp.cos(angles) * norm_scale, -jnp.sin(angles) * norm_scale], axis=0
    ).astype(jnp.bfloat16)


def cross_spectra(anchors, partners):
    half_width = anchors.shape[-1] // 2
    anchor_f = anchors.astype(jnp.float32)
    partner_f = partners.astype(jnp.float32)
    anchor_re = anchor_f[..., :half_width]
    anchor_im = anchor_f[..., half_width:]
    partner_re = partner_f[..., :half_width]
    partner_im = partner_f[..., half_width:]
    cross_re = anchor_re * partner_re + anchor_im * partner_im
    cross_im = anchor_im * partner_re - anchor_re * partner_im
    return jnp.concatenate([cross_re, cross_im], axis=-1).astype(jnp.bfloat16)


def window_gains(bins, gains):
    levels = lax.broadcasted_iota(jnp.int32, (bins.shape[0], gains.shape[0]), 1)
    return jnp.sum(jnp.where(bins[:, None] == levels, gains[None, :], jnp.float32(0.0)), axis=1)


def window_weights(lag_corr, ref_sum, window_gain):
    corr_f = lag_corr.astype(jnp.float32)
    inner_prod = jnp.mean(corr_f * ref_sum[:, None, :], axis=-1)
    corr_rms = jnp.sqrt(jnp.mean(corr_f * corr_f, axis=-1) + EPS_LAG)
    ref_rms = jnp.sqrt(jnp.mean(ref_sum * ref_sum, axis=-1) + EPS_LAG)
    coherence = inner_prod / (corr_rms * ref_rms[:, None])
    weights = window_gain[None, :] * jnp.exp(2.0 * coherence)
    numerator = jnp.sum(weights[:, :, None] * corr_f, axis=1)
    denominator = jnp.sum(weights, axis=1)
    return (numerator, denominator)


def select_rows(selector, rows):
    return jnp.einsum("sc,cwf->swf", selector, rows, preferred_element_type=jnp.bfloat16)


def butterfly_sum(value, axis):
    peers = lax.axis_size(axis)
    if peers & (peers - 1):
        return lax.psum(value, axis)
    step = 1
    while step < peers:
        pairs = [(i, i ^ step) for i in range(peers)]
        value = jax.tree.map(jnp.add, value, lax.ppermute(value, axis, pairs))
        step *= 2
    return value


def ring_exchange(up_rows, down_rows, axis):
    peers = lax.axis_size(axis)
    up = [(i, (i + 1) % peers) for i in range(peers)]
    down = [(j, i) for i, j in up]
    return lax.ppermute(up_rows, axis, up), lax.ppermute(down_rows, axis, down)


def gather_blocks(row, axis):
    peers = lax.axis_size(axis)
    if peers & (peers - 1):
        return lax.all_gather(row, axis)
    me = lax.axis_index(axis)
    acc = row[None]
    step = 1
    while step < peers:
        pairs = [(i, i ^ step) for i in range(peers)]
        got = lax.ppermute(acc, axis, pairs)
        acc = jnp.where((me & step) == 0, jnp.concatenate([acc, got]), jnp.concatenate([got, acc]))
        step *= 2
    return acc


def onehot(index, size, mask):
    return (index[:, None] == lax.broadcasted_iota(jnp.int32, (index.shape[0], size), 1)) & mask[:, None]


def window_weights_wm(corr_f, ref_sum, window_gain):
    inner_prod = jnp.mean(corr_f * ref_sum[None, :, :], axis=-1)
    corr_rms = jnp.sqrt(jnp.mean(corr_f * corr_f, axis=-1) + EPS_LAG)
    ref_rms = jnp.sqrt(jnp.mean(ref_sum * ref_sum, axis=-1) + EPS_LAG)
    coherence = inner_prod / (corr_rms * ref_rms[None, :])
    weights = window_gain[:, None] * jnp.exp(2.0 * coherence)
    numerator = jnp.sum(weights[:, :, None] * corr_f, axis=0)
    denominator = jnp.sum(weights, axis=0)
    return (numerator, denominator)


def block_needs(offs, parts, count, block_chans):
    live = lax.broadcasted_iota(jnp.int32, offs.shape, 0) < count
    hit = parts[:, None] == lax.broadcasted_iota(jnp.int32, (1, block_chans), 1)
    need_minus = jnp.any(hit & (live & (offs == 0))[:, None], axis=0)
    need_plus = jnp.any(hit & (live & (offs == 2))[:, None], axis=0)
    pos_minus = jnp.cumsum(need_minus, dtype=jnp.int32) - 1
    pos_plus = jnp.cumsum(need_plus, dtype=jnp.int32) - 1
    return need_minus, need_plus, pos_minus, pos_plus


def cross_kernel(anchor_ref, own_ref, sbf_ref, saf_ref, bf_ref, af_ref, t_ref, corr_ref, sum_ref):
    wins = anchor_ref.shape[0]
    half = anchor_ref.shape[2] // 2
    t_re = t_ref[:half, :]
    t_im = t_ref[half:, :]
    sbf, saf = sbf_ref[...], saf_ref[...]
    for w in range(wins):
        part = (
            own_ref[w].astype(jnp.float32)
            + jnp.dot(sbf, bf_ref[w], preferred_element_type=jnp.float32)
            + jnp.dot(saf, af_ref[w], preferred_element_type=jnp.float32)
        )
        anc = anchor_ref[w].astype(jnp.float32)
        a_re, a_im = anc[:, :half], anc[:, half:]
        p_re, p_im = part[:, :half], part[:, half:]
        c_re = (a_re * p_re + a_im * p_im).astype(jnp.bfloat16)
        c_im = (a_im * p_re - a_re * p_im).astype(jnp.bfloat16)
        value = jnp.dot(c_re, t_re, preferred_element_type=jnp.float32) + jnp.dot(
            c_im, t_im, preferred_element_type=jnp.float32
        )
        corr_ref[w] = value
        total = value if w == 0 else total + value
    sum_ref[...] = total


def halo_cross(chunk, wins, anchors, own, sels, bufs, transform):
    _, slots, width = anchors.shape
    lag_count = transform.shape[1]
    group = min(256, slots)
    row_spec = pl.BlockSpec((wins, group, width), lambda i: (chunk, i, 0))
    sel_specs = [pl.BlockSpec((group, sel.shape[1]), lambda i: (i, 0)) for sel in sels]
    buf_specs = [pl.BlockSpec((wins,) + buf.shape[1:], lambda i: (0, 0, 0)) for buf in bufs]
    return pl.pallas_call(
        cross_kernel,
        grid=(slots // group,),
        in_specs=[row_spec, row_spec] + sel_specs + buf_specs + [pl.BlockSpec(transform.shape, lambda i: (0, 0))],
        out_specs=[
            pl.BlockSpec((wins, group, lag_count), lambda i: (0, i, 0)),
            pl.BlockSpec((group, lag_count), lambda i: (i, 0)),
        ],
        out_shape=[
            jax.ShapeDtypeStruct((wins, slots, lag_count), jnp.float32),
            jax.ShapeDtypeStruct((slots, lag_count), jnp.float32),
        ],
        compiler_params=pltpu.CompilerParams(vmem_limit_bytes=56 * 1024 * 1024),
    )(anchors, own, *sels, *bufs, transform)


def local(spectra, pair_anchor, pair_offset, pair_partner, pair_count, window_bins, bin_gain):
    block_chans, local_wins, spec_width = spectra.shape
    pair_slots = pair_anchor.shape[0]
    fast_rows = (block_chans // 2 + 15) // 16 * 16
    spill_rows = block_chans - fast_rows

    blocks = lax.axis_size("chan")
    block = lax.axis_index("chan")
    table = jnp.concatenate([pair_offset, pair_partner, pair_count])
    tables = gather_blocks(table, "chan")
    table_before = tables[(block + blocks - 1) % blocks]
    table_after = tables[(block + 1) % blocks]

    def needs_of(tab):
        return block_needs(tab[:pair_slots], tab[pair_slots:2 * pair_slots], tab[2 * pair_slots], block_chans)

    own_minus, own_plus, own_pos_minus, own_pos_plus = needs_of(table)
    up_need, _, up_pos, _ = needs_of(table_after)
    _, down_need, _, down_pos = needs_of(table_before)
    all_needs = jax.vmap(needs_of)(tables)
    need_most = jnp.maximum(
        jnp.max(jnp.sum(all_needs[0], axis=1, dtype=jnp.int32)),
        jnp.max(jnp.sum(all_needs[1], axis=1, dtype=jnp.int32)),
    )

    def send_selector(need, pos, first, rows):
        return onehot(pos - first, rows, need).T.astype(jnp.bfloat16)

    def gather_rows(first, rows, source, whitened=False):
        up_rows = jnp.einsum("jc,cwf->wjf", send_selector(up_need, up_pos, first, rows), source,
                             preferred_element_type=jnp.bfloat16)
        down_rows = jnp.einsum("jc,cwf->wjf", send_selector(down_need, down_pos, first, rows), source,
                               preferred_element_type=jnp.bfloat16)
        if not whitened:
            up_rows, down_rows = whiten(up_rows), whiten(down_rows)
        return ring_exchange(up_rows, down_rows, "chan"), (up_rows, down_rows)

    chunks = 2 if local_wins % 2 == 0 else 1
    chunk_wins = local_wins // chunks
    fast_sent = [gather_rows(0, fast_rows, spectra[:, c * chunk_wins:(c + 1) * chunk_wins]) for c in range(chunks)]
    fast = [got for got, _ in fast_sent]
    spectra_late, _ = lax.optimization_barrier((spectra, [sent for _, sent in fast_sent]))
    white = whiten(spectra_late)
    spill = need_most > fast_rows

    transform = lag_table(spec_width // 2, LAG)
    lag_count = transform.shape[1]
    live_count = pair_count[0]
    slot_ids = lax.broadcasted_iota(jnp.int32, (pair_slots,), 0)
    live = slot_ids < live_count

    def pick(selector, rows):
        return jnp.einsum("sc,cwf->wsf", selector.astype(jnp.bfloat16), rows, preferred_element_type=jnp.bfloat16)

    anchors = pick(onehot(pair_anchor, block_chans, live), white)
    own = pick(onehot(pair_partner, block_chans, live & (pair_offset == 1)), white)
    own_hit = onehot(pair_partner, block_chans, live)
    before_row = jnp.sum(jnp.where(own_hit, own_pos_minus[None, :], 0), axis=1)
    after_row = jnp.sum(jnp.where(own_hit, own_pos_plus[None, :], 0), axis=1)
    use_before = live & (pair_offset == 0)
    use_after = live & (pair_offset == 2)
    sels = [
        onehot(before_row, fast_rows, use_before).astype(jnp.bfloat16),
        onehot(after_row, fast_rows, use_after).astype(jnp.bfloat16),
    ]
    fast_out = [
        halo_cross(c, chunk_wins, anchors, own, sels, [fast[c][0], fast[c][1]], transform)
        for c in range(chunks)
    ]
    corr_full = jnp.concatenate([corr for corr, _ in fast_out])

    def spill_extra(_):
        (got_before, got_after), _ = gather_rows(fast_rows, spill_rows, white, whitened=True)
        spill_sels = [
            onehot(before_row - fast_rows, spill_rows, use_before).astype(jnp.bfloat16),
            onehot(after_row - fast_rows, spill_rows, use_after).astype(jnp.bfloat16),
        ]
        zero_own = jnp.zeros_like(own)
        outs = [
            halo_cross(c, chunk_wins, anchors, zero_own, spill_sels,
                       [got_before[c * chunk_wins:(c + 1) * chunk_wins], got_after[c * chunk_wins:(c + 1) * chunk_wins]],
                       transform)
            for c in range(chunks)
        ]
        return jnp.concatenate([corr for corr, _ in outs]), sum(part for _, part in outs)

    def no_extra(_):
        return (jnp.zeros((local_wins, pair_slots, lag_count), jnp.float32),
                jnp.zeros((pair_slots, lag_count), jnp.float32))

    spill_late, _ = lax.optimization_barrier((spill, fast[0]))
    extra, extra_sum = lax.cond(spill_late, spill_extra, no_extra, 0)
    corr_full = corr_full + extra
    corr_all = lax.reduce_precision(corr_full, exponent_bits=8, mantissa_bits=7)
    running = sum(part for _, part in fast_out) + extra_sum

    ref_sum = butterfly_sum(running, "win")
    norm_scale = jnp.sqrt(jnp.float32(local_wins * lax.axis_size("win")))
    ref_stack = jnp.where(live[:, None], ref_sum / norm_scale, 0.0)
    window_gain = window_gains(window_bins, bin_gain)
    numerator, denominator = window_weights_wm(corr_all, ref_sum, window_gain)
    numerator, denominator = butterfly_sum((numerator, denominator), "win")
    restack = jnp.where(live[:, None], norm_scale * numerator / denominator[:, None], 0.0)
    return (ref_stack, restack)


def solution(mesh):
    in_specs = (
        P(("days", "chan"), "win", None),
        P("chan"),
        P("chan"),
        P("chan"),
        P("chan"),
        P(("days", "win")),
        P(),
    )
    out_specs = (P(("days", "chan"), None), P(("days", "chan"), None))
    return jax.shard_map(local, mesh=mesh, in_specs=in_specs, out_specs=out_specs, check_vma=False)
```

```python
import jax
import jax.numpy as jnp
from jax import lax
from jax.experimental import pallas as pl
from jax.experimental.pallas import tpu as pltpu
from jax.sharding import PartitionSpec as P

LAG = 128


EPS_POWER = 1e-05
EPS_LAG = 1e-06


def whiten(spectra):
    spectra_f = spectra.astype(jnp.float32)
    power_mean = jnp.mean(spectra_f * spectra_f, axis=-1, keepdims=True)
    return (spectra_f * lax.rsqrt(power_mean + EPS_POWER)).astype(jnp.bfloat16)


def lag_table(freq_count, lag_count):
    freq_ids = lax.broadcasted_iota(jnp.float32, (freq_count, lag_count), 0)
    lag_ids = lax.broadcasted_iota(jnp.float32, (freq_count, lag_count), 1) - lag_count // 2
    angles = 2.0 * jnp.pi / (2 * freq_count) * freq_ids * lag_ids
    norm_scale = 1.0 / jnp.sqrt(jnp.float32(freq_count))
    return jnp.concatenate(
        [jnp.cos(angles) * norm_scale, -jnp.sin(angles) * norm_scale], axis=0
    ).astype(jnp.bfloat16)


def cross_spectra(anchors, partners):
    half_width = anchors.shape[-1] // 2
    anchor_f = anchors.astype(jnp.float32)
    partner_f = partners.astype(jnp.float32)
    anchor_re = anchor_f[..., :half_width]
    anchor_im = anchor_f[..., half_width:]
    partner_re = partner_f[..., :half_width]
    partner_im = partner_f[..., half_width:]
    cross_re = anchor_re * partner_re + anchor_im * partner_im
    cross_im = anchor_im * partner_re - anchor_re * partner_im
    return jnp.concatenate([cross_re, cross_im], axis=-1).astype(jnp.bfloat16)


def window_gains(bins, gains):
    levels = lax.broadcasted_iota(jnp.int32, (bins.shape[0], gains.shape[0]), 1)
    return jnp.sum(jnp.where(bins[:, None] == levels, gains[None, :], jnp.float32(0.0)), axis=1)


def window_weights(lag_corr, ref_sum, window_gain):
    corr_f = lag_corr.astype(jnp.float32)
    inner_prod = jnp.mean(corr_f * ref_sum[:, None, :], axis=-1)
    corr_rms = jnp.sqrt(jnp.mean(corr_f * corr_f, axis=-1) + EPS_LAG)
    ref_rms = jnp.sqrt(jnp.mean(ref_sum * ref_sum, axis=-1) + EPS_LAG)
    coherence = inner_prod / (corr_rms * ref_rms[:, None])
    weights = window_gain[None, :] * jnp.exp(2.0 * coherence)
    numerator = jnp.sum(weights[:, :, None] * corr_f, axis=1)
    denominator = jnp.sum(weights, axis=1)
    return (numerator, denominator)


def select_rows(selector, rows):
    return jnp.einsum("sc,cwf->swf", selector, rows, preferred_element_type=jnp.bfloat16)


def butterfly_sum(value, axis):
    peers = lax.axis_size(axis)
    if peers & (peers - 1):
        return lax.psum(value, axis)
    step = 1
    while step < peers:
        pairs = [(i, i ^ step) for i in range(peers)]
        value = jax.tree.map(jnp.add, value, lax.ppermute(value, axis, pairs))
        step *= 2
    return value


def ring_exchange(up_rows, down_rows, axis):
    peers = lax.axis_size(axis)
    up = [(i, (i + 1) % peers) for i in range(peers)]
    down = [(j, i) for i, j in up]
    return lax.ppermute(up_rows, axis, up), lax.ppermute(down_rows, axis, down)


def gather_blocks(row, axis):
    peers = lax.axis_size(axis)
    if peers & (peers - 1):
        return lax.all_gather(row, axis)
    me = lax.axis_index(axis)
    acc = row[None]
    step = 1
    while step < peers:
        pairs = [(i, i ^ step) for i in range(peers)]
        got = lax.ppermute(acc, axis, pairs)
        acc = jnp.where((me & step) == 0, jnp.concatenate([acc, got]), jnp.concatenate([got, acc]))
        step *= 2
    return acc


def onehot(index, size, mask):
    return (index[:, None] == lax.broadcasted_iota(jnp.int32, (index.shape[0], size), 1)) & mask[:, None]


def window_weights_wm(corr_f, ref_sum, window_gain):
    inner_prod = jnp.mean(corr_f * ref_sum[None, :, :], axis=-1)
    corr_rms = jnp.sqrt(jnp.mean(corr_f * corr_f, axis=-1) + EPS_LAG)
    ref_rms = jnp.sqrt(jnp.mean(ref_sum * ref_sum, axis=-1) + EPS_LAG)
    coherence = inner_prod / (corr_rms * ref_rms[None, :])
    weights = window_gain[:, None] * jnp.exp(2.0 * coherence)
    numerator = jnp.sum(weights[:, :, None] * corr_f, axis=0)
    denominator = jnp.sum(weights, axis=0)
    return (numerator, denominator)


def block_needs(offs, parts, count, block_chans):
    live = lax.broadcasted_iota(jnp.int32, offs.shape, 0) < count
    hit = parts[:, None] == lax.broadcasted_iota(jnp.int32, (1, block_chans), 1)
    need_minus = jnp.any(hit & (live & (offs == 0))[:, None], axis=0)
    need_plus = jnp.any(hit & (live & (offs == 2))[:, None], axis=0)
    pos_minus = jnp.cumsum(need_minus, dtype=jnp.int32) - 1
    pos_plus = jnp.cumsum(need_plus, dtype=jnp.int32) - 1
    return need_minus, need_plus, pos_minus, pos_plus


def cross_kernel(anchor_ref, own_ref, sbf_ref, saf_ref, bf_ref, af_ref, t_ref, corr_ref):
    wins = anchor_ref.shape[0]
    half = anchor_ref.shape[2] // 2
    t_re = t_ref[:half, :]
    t_im = t_ref[half:, :]
    sbf, saf = sbf_ref[...], saf_ref[...]
    for w in range(wins):
        part = (
            own_ref[w].astype(jnp.float32)
            + jnp.dot(sbf, bf_ref[w], preferred_element_type=jnp.float32)
            + jnp.dot(saf, af_ref[w], preferred_element_type=jnp.float32)
        )
        anc = anchor_ref[w].astype(jnp.float32)
        a_re, a_im = anc[:, :half], anc[:, half:]
        p_re, p_im = part[:, :half], part[:, half:]
        c_re = (a_re * p_re + a_im * p_im).astype(jnp.bfloat16)
        c_im = (a_im * p_re - a_re * p_im).astype(jnp.bfloat16)
        corr_ref[w] = jnp.dot(c_re, t_re, preferred_element_type=jnp.float32) + jnp.dot(
            c_im, t_im, preferred_element_type=jnp.float32
        )


def halo_cross(chunk, wins, anchors, own, sels, bufs, transform):
    _, slots, width = anchors.shape
    lag_count = transform.shape[1]
    group = min(512, slots)
    row_spec = pl.BlockSpec((wins, group, width), lambda i: (chunk, i, 0))
    sel_specs = [pl.BlockSpec((group, sel.shape[1]), lambda i: (i, 0)) for sel in sels]
    buf_specs = [pl.BlockSpec((wins,) + buf.shape[1:], lambda i: (0, 0, 0)) for buf in bufs]
    return pl.pallas_call(
        cross_kernel,
        grid=(slots // group,),
        in_specs=[row_spec, row_spec] + sel_specs + buf_specs + [pl.BlockSpec(transform.shape, lambda i: (0, 0))],
        out_specs=pl.BlockSpec((wins, group, lag_count), lambda i: (0, i, 0)),
        out_shape=jax.ShapeDtypeStruct((wins, slots, lag_count), jnp.float32),
        compiler_params=pltpu.CompilerParams(vmem_limit_bytes=56 * 1024 * 1024),
    )(anchors, own, *sels, *bufs, transform)


def local(spectra, pair_anchor, pair_offset, pair_partner, pair_count, window_bins, bin_gain):
    block_chans, local_wins, spec_width = spectra.shape
    pair_slots = pair_anchor.shape[0]
    fast_rows = (block_chans // 2 + 15) // 16 * 16
    spill_rows = block_chans - fast_rows

    blocks = lax.axis_size("chan")
    block = lax.axis_index("chan")
    table = jnp.concatenate([pair_offset, pair_partner, pair_count])
    tables = gather_blocks(table, "chan")
    table_before = tables[(block + blocks - 1) % blocks]
    table_after = tables[(block + 1) % blocks]

    def needs_of(tab):
        return block_needs(tab[:pair_slots], tab[pair_slots:2 * pair_slots], tab[2 * pair_slots], block_chans)

    own_minus, own_plus, own_pos_minus, own_pos_plus = needs_of(table)
    up_need, _, up_pos, _ = needs_of(table_after)
    _, down_need, _, down_pos = needs_of(table_before)
    all_needs = jax.vmap(needs_of)(tables)
    need_most = jnp.maximum(
        jnp.max(jnp.sum(all_needs[0], axis=1, dtype=jnp.int32)),
        jnp.max(jnp.sum(all_needs[1], axis=1, dtype=jnp.int32)),
    )

    def send_selector(need, pos, first, rows):
        return onehot(pos - first, rows, need).T.astype(jnp.bfloat16)

    def gather_rows(first, rows, source, whitened=False):
        up_rows = jnp.einsum("jc,cwf->wjf", send_selector(up_need, up_pos, first, rows), source,
                             preferred_element_type=jnp.bfloat16)
        down_rows = jnp.einsum("jc,cwf->wjf", send_selector(down_need, down_pos, first, rows), source,
                               preferred_element_type=jnp.bfloat16)
        if not whitened:
            up_rows, down_rows = whiten(up_rows), whiten(down_rows)
        return ring_exchange(up_rows, down_rows, "chan"), (up_rows, down_rows)

    chunks = 2 if local_wins % 2 == 0 else 1
    chunk_wins = local_wins // chunks
    fast_sent = [gather_rows(0, fast_rows, spectra[:, c * chunk_wins:(c + 1) * chunk_wins]) for c in range(chunks)]
    fast = [got for got, _ in fast_sent]
    spectra_late, _ = lax.optimization_barrier((spectra, [sent for _, sent in fast_sent]))
    white = whiten(spectra_late)
    spill = need_most > fast_rows

    transform = lag_table(spec_width // 2, LAG)
    lag_count = transform.shape[1]
    live_count = pair_count[0]
    slot_ids = lax.broadcasted_iota(jnp.int32, (pair_slots,), 0)
    live = slot_ids < live_count

    def pick(selector, rows):
        return jnp.einsum("sc,cwf->wsf", selector.astype(jnp.bfloat16), rows, preferred_element_type=jnp.bfloat16)

    anchors = pick(onehot(pair_anchor, block_chans, live), white)
    own = pick(onehot(pair_partner, block_chans, live & (pair_offset == 1)), white)
    own_hit = onehot(pair_partner, block_chans, live)
    before_row = jnp.sum(jnp.where(own_hit, own_pos_minus[None, :], 0), axis=1)
    after_row = jnp.sum(jnp.where(own_hit, own_pos_plus[None, :], 0), axis=1)
    use_before = live & (pair_offset == 0)
    use_after = live & (pair_offset == 2)
    sels = [
        onehot(before_row, fast_rows, use_before).astype(jnp.bfloat16),
        onehot(after_row, fast_rows, use_after).astype(jnp.bfloat16),
    ]
    corr_full = jnp.concatenate([
        halo_cross(c, chunk_wins, anchors, own, sels, [fast[c][0], fast[c][1]], transform)
        for c in range(chunks)
    ])

    def spill_extra(_):
        (got_before, got_after), _ = gather_rows(fast_rows, spill_rows, white, whitened=True)
        spill_sels = [
            onehot(before_row - fast_rows, spill_rows, use_before).astype(jnp.bfloat16),
            onehot(after_row - fast_rows, spill_rows, use_after).astype(jnp.bfloat16),
        ]
        zero_own = jnp.zeros_like(own)
        extra = jnp.concatenate([
            halo_cross(c, chunk_wins, anchors, zero_own, spill_sels,
                       [got_before[c * chunk_wins:(c + 1) * chunk_wins], got_after[c * chunk_wins:(c + 1) * chunk_wins]],
                       transform)
            for c in range(chunks)
        ])
        return extra

    def no_extra(_):
        return jnp.zeros((local_wins, pair_slots, lag_count), jnp.float32)

    spill_late, _ = lax.optimization_barrier((spill, fast[0]))
    corr_full = corr_full + lax.cond(spill_late, spill_extra, no_extra, 0)
    corr_all = lax.reduce_precision(corr_full, exponent_bits=8, mantissa_bits=7)
    running = jnp.sum(corr_full, axis=0)

    ref_sum = butterfly_sum(running, "win")
    norm_scale = jnp.sqrt(jnp.float32(local_wins * lax.axis_size("win")))
    ref_stack = jnp.where(live[:, None], ref_sum / norm_scale, 0.0)
    window_gain = window_gains(window_bins, bin_gain)
    numerator, denominator = window_weights_wm(corr_all, ref_sum, window_gain)
    numerator, denominator = butterfly_sum((numerator, denominator), "win")
    restack = jnp.where(live[:, None], norm_scale * numerator / denominator[:, None], 0.0)
    return (ref_stack, restack)


def solution(mesh):
    in_specs = (
        P(("days", "chan"), "win", None),
        P("chan"),
        P("chan"),
        P("chan"),
        P("chan"),
        P(("days", "win")),
        P(),
    )
    out_specs = (P(("days", "chan"), None), P(("days", "chan"), None))
    return jax.shard_map(local, mesh=mesh, in_specs=in_specs, out_specs=out_specs, check_vma=False)
```

```python
import jax
import jax.numpy as jnp
from jax import lax
from jax.experimental import pallas as pl
from jax.experimental.pallas import tpu as pltpu
from jax.sharding import PartitionSpec as P

LAG = 128


EPS_POWER = 1e-05
EPS_LAG = 1e-06


def whiten(spectra):
    spectra_f = spectra.astype(jnp.float32)
    power_mean = jnp.mean(spectra_f * spectra_f, axis=-1, keepdims=True)
    return (spectra_f * lax.rsqrt(power_mean + EPS_POWER)).astype(jnp.bfloat16)


def lag_table(freq_count, lag_count):
    freq_ids = lax.broadcasted_iota(jnp.float32, (freq_count, lag_count), 0)
    lag_ids = lax.broadcasted_iota(jnp.float32, (freq_count, lag_count), 1) - lag_count // 2
    angles = 2.0 * jnp.pi / (2 * freq_count) * freq_ids * lag_ids
    norm_scale = 1.0 / jnp.sqrt(jnp.float32(freq_count))
    return jnp.concatenate(
        [jnp.cos(angles) * norm_scale, -jnp.sin(angles) * norm_scale], axis=0
    ).astype(jnp.bfloat16)


def cross_spectra(anchors, partners):
    half_width = anchors.shape[-1] // 2
    anchor_f = anchors.astype(jnp.float32)
    partner_f = partners.astype(jnp.float32)
    anchor_re = anchor_f[..., :half_width]
    anchor_im = anchor_f[..., half_width:]
    partner_re = partner_f[..., :half_width]
    partner_im = partner_f[..., half_width:]
    cross_re = anchor_re * partner_re + anchor_im * partner_im
    cross_im = anchor_im * partner_re - anchor_re * partner_im
    return jnp.concatenate([cross_re, cross_im], axis=-1).astype(jnp.bfloat16)


def window_gains(bins, gains):
    levels = lax.broadcasted_iota(jnp.int32, (bins.shape[0], gains.shape[0]), 1)
    return jnp.sum(jnp.where(bins[:, None] == levels, gains[None, :], jnp.float32(0.0)), axis=1)


def window_weights(lag_corr, ref_sum, window_gain):
    corr_f = lag_corr.astype(jnp.float32)
    inner_prod = jnp.mean(corr_f * ref_sum[:, None, :], axis=-1)
    corr_rms = jnp.sqrt(jnp.mean(corr_f * corr_f, axis=-1) + EPS_LAG)
    ref_rms = jnp.sqrt(jnp.mean(ref_sum * ref_sum, axis=-1) + EPS_LAG)
    coherence = inner_prod / (corr_rms * ref_rms[:, None])
    weights = window_gain[None, :] * jnp.exp(2.0 * coherence)
    numerator = jnp.sum(weights[:, :, None] * corr_f, axis=1)
    denominator = jnp.sum(weights, axis=1)
    return (numerator, denominator)


def select_rows(selector, rows):
    return jnp.einsum("sc,cwf->swf", selector, rows, preferred_element_type=jnp.bfloat16)


def butterfly_sum(value, axis):
    peers = lax.axis_size(axis)
    if peers & (peers - 1):
        return lax.psum(value, axis)
    step = 1
    while step < peers:
        pairs = [(i, i ^ step) for i in range(peers)]
        value = jax.tree.map(jnp.add, value, lax.ppermute(value, axis, pairs))
        step *= 2
    return value


def ring_exchange(up_rows, down_rows, axis):
    peers = lax.axis_size(axis)
    up = [(i, (i + 1) % peers) for i in range(peers)]
    down = [(j, i) for i, j in up]
    return lax.ppermute(up_rows, axis, up), lax.ppermute(down_rows, axis, down)


def gather_blocks(row, axis):
    peers = lax.axis_size(axis)
    if peers & (peers - 1):
        return lax.all_gather(row, axis)
    me = lax.axis_index(axis)
    acc = row[None]
    step = 1
    while step < peers:
        pairs = [(i, i ^ step) for i in range(peers)]
        got = lax.ppermute(acc, axis, pairs)
        acc = jnp.where((me & step) == 0, jnp.concatenate([acc, got]), jnp.concatenate([got, acc]))
        step *= 2
    return acc


def onehot(index, size, mask):
    return (index[:, None] == lax.broadcasted_iota(jnp.int32, (index.shape[0], size), 1)) & mask[:, None]


def window_weights_wm(corr_f, ref_sum, window_gain):
    inner_prod = jnp.mean(corr_f * ref_sum[None, :, :], axis=-1)
    corr_rms = jnp.sqrt(jnp.mean(corr_f * corr_f, axis=-1) + EPS_LAG)
    ref_rms = jnp.sqrt(jnp.mean(ref_sum * ref_sum, axis=-1) + EPS_LAG)
    coherence = inner_prod / (corr_rms * ref_rms[None, :])
    weights = window_gain[:, None] * jnp.exp(2.0 * coherence)
    numerator = jnp.sum(weights[:, :, None] * corr_f, axis=0)
    denominator = jnp.sum(weights, axis=0)
    return (numerator, denominator)


def block_needs(offs, parts, count, block_chans):
    live = lax.broadcasted_iota(jnp.int32, offs.shape, 0) < count
    hit = parts[:, None] == lax.broadcasted_iota(jnp.int32, (1, block_chans), 1)
    need_minus = jnp.any(hit & (live & (offs == 0))[:, None], axis=0)
    need_plus = jnp.any(hit & (live & (offs == 2))[:, None], axis=0)
    pos_minus = jnp.cumsum(need_minus, dtype=jnp.int32) - 1
    pos_plus = jnp.cumsum(need_plus, dtype=jnp.int32) - 1
    return need_minus, need_plus, pos_minus, pos_plus


def cross_kernel(anchor_ref, own_ref, sbf_ref, saf_ref, bf_ref, af_ref, t_ref, corr_ref):
    wins = anchor_ref.shape[0]
    half = anchor_ref.shape[2] // 2
    t_re = t_ref[:half, :]
    t_im = t_ref[half:, :]
    sbf, saf = sbf_ref[...], saf_ref[...]
    for w in range(wins):
        part = (
            own_ref[w].astype(jnp.float32)
            + jnp.dot(sbf, bf_ref[w], preferred_element_type=jnp.float32)
            + jnp.dot(saf, af_ref[w], preferred_element_type=jnp.float32)
        )
        anc = anchor_ref[w].astype(jnp.float32)
        a_re, a_im = anc[:, :half], anc[:, half:]
        p_re, p_im = part[:, :half], part[:, half:]
        c_re = (a_re * p_re + a_im * p_im).astype(jnp.bfloat16)
        c_im = (a_im * p_re - a_re * p_im).astype(jnp.bfloat16)
        corr_ref[w] = jnp.dot(c_re, t_re, preferred_element_type=jnp.float32) + jnp.dot(
            c_im, t_im, preferred_element_type=jnp.float32
        )


def halo_cross(chunk, wins, anchors, own, sels, bufs, transform):
    _, slots, width = anchors.shape
    lag_count = transform.shape[1]
    group = min(256, slots)
    row_spec = pl.BlockSpec((wins, group, width), lambda i: (chunk, i, 0))
    sel_specs = [pl.BlockSpec((group, sel.shape[1]), lambda i: (i, 0)) for sel in sels]
    buf_specs = [pl.BlockSpec((wins,) + buf.shape[1:], lambda i: (0, 0, 0)) for buf in bufs]
    return pl.pallas_call(
        cross_kernel,
        grid=(slots // group,),
        in_specs=[row_spec, row_spec] + sel_specs + buf_specs + [pl.BlockSpec(transform.shape, lambda i: (0, 0))],
        out_specs=pl.BlockSpec((wins, group, lag_count), lambda i: (0, i, 0)),
        out_shape=jax.ShapeDtypeStruct((wins, slots, lag_count), jnp.float32),
        compiler_params=pltpu.CompilerParams(vmem_limit_bytes=56 * 1024 * 1024),
    )(anchors, own, *sels, *bufs, transform)


def local(spectra, pair_anchor, pair_offset, pair_partner, pair_count, window_bins, bin_gain):
    block_chans, local_wins, spec_width = spectra.shape
    pair_slots = pair_anchor.shape[0]
    fast_rows = (block_chans // 2 + 15) // 16 * 16
    spill_rows = block_chans - fast_rows

    blocks = lax.axis_size("chan")
    block = lax.axis_index("chan")
    table = jnp.concatenate([pair_offset, pair_partner, pair_count])
    tables = gather_blocks(table, "chan")
    table_before = tables[(block + blocks - 1) % blocks]
    table_after = tables[(block + 1) % blocks]

    def needs_of(tab):
        return block_needs(tab[:pair_slots], tab[pair_slots:2 * pair_slots], tab[2 * pair_slots], block_chans)

    own_minus, own_plus, own_pos_minus, own_pos_plus = needs_of(table)
    up_need, _, up_pos, _ = needs_of(table_after)
    _, down_need, _, down_pos = needs_of(table_before)
    all_needs = jax.vmap(needs_of)(tables)
    need_most = jnp.maximum(
        jnp.max(jnp.sum(all_needs[0], axis=1, dtype=jnp.int32)),
        jnp.max(jnp.sum(all_needs[1], axis=1, dtype=jnp.int32)),
    )

    def send_selector(need, pos, first, rows):
        return onehot(pos - first, rows, need).T.astype(jnp.bfloat16)

    def gather_rows(first, rows, source, whitened=False):
        up_rows = jnp.einsum("jc,cwf->wjf", send_selector(up_need, up_pos, first, rows), source,
                             preferred_element_type=jnp.bfloat16)
        down_rows = jnp.einsum("jc,cwf->wjf", send_selector(down_need, down_pos, first, rows), source,
                               preferred_element_type=jnp.bfloat16)
        if not whitened:
            up_rows, down_rows = whiten(up_rows), whiten(down_rows)
        return ring_exchange(up_rows, down_rows, "chan"), (up_rows, down_rows)

    chunks = 4 if local_wins % 4 == 0 else 1
    chunk_wins = local_wins // chunks
    fast_sent = [gather_rows(0, fast_rows, spectra[:, c * chunk_wins:(c + 1) * chunk_wins]) for c in range(chunks)]
    fast = [got for got, _ in fast_sent]
    spectra_late, _ = lax.optimization_barrier((spectra, [sent for _, sent in fast_sent]))
    white = whiten(spectra_late)
    spill = need_most > fast_rows

    transform = lag_table(spec_width // 2, LAG)
    lag_count = transform.shape[1]
    live_count = pair_count[0]
    slot_ids = lax.broadcasted_iota(jnp.int32, (pair_slots,), 0)
    live = slot_ids < live_count

    def pick(selector, rows):
        return jnp.einsum("sc,cwf->wsf", selector.astype(jnp.bfloat16), rows, preferred_element_type=jnp.bfloat16)

    anchors = pick(onehot(pair_anchor, block_chans, live), white)
    own = pick(onehot(pair_partner, block_chans, live & (pair_offset == 1)), white)
    own_hit = onehot(pair_partner, block_chans, live)
    before_row = jnp.sum(jnp.where(own_hit, own_pos_minus[None, :], 0), axis=1)
    after_row = jnp.sum(jnp.where(own_hit, own_pos_plus[None, :], 0), axis=1)
    use_before = live & (pair_offset == 0)
    use_after = live & (pair_offset == 2)
    sels = [
        onehot(before_row, fast_rows, use_before).astype(jnp.bfloat16),
        onehot(after_row, fast_rows, use_after).astype(jnp.bfloat16),
    ]
    corr_full = jnp.concatenate([
        halo_cross(c, chunk_wins, anchors, own, sels, [fast[c][0], fast[c][1]], transform)
        for c in range(chunks)
    ])

    def spill_extra(_):
        (got_before, got_after), _ = gather_rows(fast_rows, spill_rows, white, whitened=True)
        spill_sels = [
            onehot(before_row - fast_rows, spill_rows, use_before).astype(jnp.bfloat16),
            onehot(after_row - fast_rows, spill_rows, use_after).astype(jnp.bfloat16),
        ]
        zero_own = jnp.zeros_like(own)
        extra = jnp.concatenate([
            halo_cross(c, chunk_wins, anchors, zero_own, spill_sels,
                       [got_before[c * chunk_wins:(c + 1) * chunk_wins], got_after[c * chunk_wins:(c + 1) * chunk_wins]],
                       transform)
            for c in range(chunks)
        ])
        return extra

    def no_extra(_):
        return jnp.zeros((local_wins, pair_slots, lag_count), jnp.float32)

    spill_late, _ = lax.optimization_barrier((spill, fast[0]))
    corr_full = corr_full + lax.cond(spill_late, spill_extra, no_extra, 0)
    corr_all = lax.reduce_precision(corr_full, exponent_bits=8, mantissa_bits=7)
    running = jnp.sum(corr_full, axis=0)

    ref_sum = butterfly_sum(running, "win")
    norm_scale = jnp.sqrt(jnp.float32(local_wins * lax.axis_size("win")))
    ref_stack = jnp.where(live[:, None], ref_sum / norm_scale, 0.0)
    window_gain = window_gains(window_bins, bin_gain)
    numerator, denominator = window_weights_wm(corr_all, ref_sum, window_gain)
    numerator, denominator = butterfly_sum((numerator, denominator), "win")
    restack = jnp.where(live[:, None], norm_scale * numerator / denominator[:, None], 0.0)
    return (ref_stack, restack)


def solution(mesh):
    in_specs = (
        P(("days", "chan"), "win", None),
        P("chan"),
        P("chan"),
        P("chan"),
        P("chan"),
        P(("days", "win")),
        P(),
    )
    out_specs = (P(("days", "chan"), None), P(("days", "chan"), None))
    return jax.shard_map(local, mesh=mesh, in_specs=in_specs, out_specs=out_specs, check_vma=False)
```

```python
import jax
import jax.numpy as jnp
from jax import lax
from jax.experimental import pallas as pl
from jax.experimental.pallas import tpu as pltpu
from jax.sharding import PartitionSpec as P

LAG = 128


EPS_POWER = 1e-05
EPS_LAG = 1e-06


def whiten(spectra):
    spectra_f = spectra.astype(jnp.float32)
    power_mean = jnp.mean(spectra_f * spectra_f, axis=-1, keepdims=True)
    return (spectra_f * lax.rsqrt(power_mean + EPS_POWER)).astype(jnp.bfloat16)


def lag_table(freq_count, lag_count):
    freq_ids = lax.broadcasted_iota(jnp.float32, (freq_count, lag_count), 0)
    lag_ids = lax.broadcasted_iota(jnp.float32, (freq_count, lag_count), 1) - lag_count // 2
    angles = 2.0 * jnp.pi / (2 * freq_count) * freq_ids * lag_ids
    norm_scale = 1.0 / jnp.sqrt(jnp.float32(freq_count))
    return jnp.concatenate(
        [jnp.cos(angles) * norm_scale, -jnp.sin(angles) * norm_scale], axis=0
    ).astype(jnp.bfloat16)


def cross_spectra(anchors, partners):
    half_width = anchors.shape[-1] // 2
    anchor_f = anchors.astype(jnp.float32)
    partner_f = partners.astype(jnp.float32)
    anchor_re = anchor_f[..., :half_width]
    anchor_im = anchor_f[..., half_width:]
    partner_re = partner_f[..., :half_width]
    partner_im = partner_f[..., half_width:]
    cross_re = anchor_re * partner_re + anchor_im * partner_im
    cross_im = anchor_im * partner_re - anchor_re * partner_im
    return jnp.concatenate([cross_re, cross_im], axis=-1).astype(jnp.bfloat16)


def window_gains(bins, gains):
    levels = lax.broadcasted_iota(jnp.int32, (bins.shape[0], gains.shape[0]), 1)
    return jnp.sum(jnp.where(bins[:, None] == levels, gains[None, :], jnp.float32(0.0)), axis=1)


def window_weights(lag_corr, ref_sum, window_gain):
    corr_f = lag_corr.astype(jnp.float32)
    inner_prod = jnp.mean(corr_f * ref_sum[:, None, :], axis=-1)
    corr_rms = jnp.sqrt(jnp.mean(corr_f * corr_f, axis=-1) + EPS_LAG)
    ref_rms = jnp.sqrt(jnp.mean(ref_sum * ref_sum, axis=-1) + EPS_LAG)
    coherence = inner_prod / (corr_rms * ref_rms[:, None])
    weights = window_gain[None, :] * jnp.exp(2.0 * coherence)
    numerator = jnp.sum(weights[:, :, None] * corr_f, axis=1)
    denominator = jnp.sum(weights, axis=1)
    return (numerator, denominator)


def select_rows(selector, rows):
    return jnp.einsum("sc,cwf->swf", selector, rows, preferred_element_type=jnp.bfloat16)


def butterfly_sum(value, axis):
    peers = lax.axis_size(axis)
    if peers & (peers - 1):
        return lax.psum(value, axis)
    step = 1
    while step < peers:
        pairs = [(i, i ^ step) for i in range(peers)]
        value = jax.tree.map(jnp.add, value, lax.ppermute(value, axis, pairs))
        step *= 2
    return value


def ring_exchange(up_rows, down_rows, axis):
    peers = lax.axis_size(axis)
    up = [(i, (i + 1) % peers) for i in range(peers)]
    down = [(j, i) for i, j in up]
    return lax.ppermute(up_rows, axis, up), lax.ppermute(down_rows, axis, down)


def gather_blocks(row, axis):
    peers = lax.axis_size(axis)
    if peers & (peers - 1):
        return lax.all_gather(row, axis)
    me = lax.axis_index(axis)
    acc = row[None]
    step = 1
    while step < peers:
        pairs = [(i, i ^ step) for i in range(peers)]
        got = lax.ppermute(acc, axis, pairs)
        acc = jnp.where((me & step) == 0, jnp.concatenate([acc, got]), jnp.concatenate([got, acc]))
        step *= 2
    return acc


def onehot(index, size, mask):
    return (index[:, None] == lax.broadcasted_iota(jnp.int32, (index.shape[0], size), 1)) & mask[:, None]


def window_weights_wm(corr_f, ref_sum, window_gain):
    inner_prod = jnp.mean(corr_f * ref_sum[None, :, :], axis=-1)
    corr_rms = jnp.sqrt(jnp.mean(corr_f * corr_f, axis=-1) + EPS_LAG)
    ref_rms = jnp.sqrt(jnp.mean(ref_sum * ref_sum, axis=-1) + EPS_LAG)
    coherence = inner_prod / (corr_rms * ref_rms[None, :])
    weights = window_gain[:, None] * jnp.exp(2.0 * coherence)
    numerator = jnp.sum(weights[:, :, None] * corr_f, axis=0)
    denominator = jnp.sum(weights, axis=0)
    return (numerator, denominator)


def block_needs(offs, parts, count, block_chans):
    live = lax.broadcasted_iota(jnp.int32, offs.shape, 0) < count
    hit = parts[:, None] == lax.broadcasted_iota(jnp.int32, (1, block_chans), 1)
    need_minus = jnp.any(hit & (live & (offs == 0))[:, None], axis=0)
    need_plus = jnp.any(hit & (live & (offs == 2))[:, None], axis=0)
    pos_minus = jnp.cumsum(need_minus, dtype=jnp.int32) - 1
    pos_plus = jnp.cumsum(need_plus, dtype=jnp.int32) - 1
    return need_minus, need_plus, pos_minus, pos_plus


def cross_kernel(anchor_ref, own_ref, sbf_ref, saf_ref, bf_ref, af_ref, t_ref, corr_ref):
    wins = anchor_ref.shape[0]
    half = anchor_ref.shape[2] // 2
    t_re = t_ref[:half, :]
    t_im = t_ref[half:, :]
    sbf, saf = sbf_ref[...], saf_ref[...]
    for w in range(wins):
        part = (
            own_ref[w].astype(jnp.float32)
            + jnp.dot(sbf, bf_ref[w], preferred_element_type=jnp.float32)
            + jnp.dot(saf, af_ref[w], preferred_element_type=jnp.float32)
        )
        anc = anchor_ref[w].astype(jnp.float32)
        a_re, a_im = anc[:, :half], anc[:, half:]
        p_re, p_im = part[:, :half], part[:, half:]
        c_re = (a_re * p_re + a_im * p_im).astype(jnp.bfloat16)
        c_im = (a_im * p_re - a_re * p_im).astype(jnp.bfloat16)
        corr_ref[w] = jnp.dot(c_re, t_re, preferred_element_type=jnp.float32) + jnp.dot(
            c_im, t_im, preferred_element_type=jnp.float32
        )


def halo_cross(chunk, wins, anchors, own, sels, bufs, transform):
    _, slots, width = anchors.shape
    lag_count = transform.shape[1]
    group = min(256, slots)
    row_spec = pl.BlockSpec((wins, group, width), lambda i: (chunk, i, 0))
    sel_specs = [pl.BlockSpec((group, sel.shape[1]), lambda i: (i, 0)) for sel in sels]
    buf_specs = [pl.BlockSpec((wins,) + buf.shape[1:], lambda i: (0, 0, 0)) for buf in bufs]
    return pl.pallas_call(
        cross_kernel,
        grid=(slots // group,),
        in_specs=[row_spec, row_spec] + sel_specs + buf_specs + [pl.BlockSpec(transform.shape, lambda i: (0, 0))],
        out_specs=pl.BlockSpec((wins, group, lag_count), lambda i: (0, i, 0)),
        out_shape=jax.ShapeDtypeStruct((wins, slots, lag_count), jnp.float32),
        compiler_params=pltpu.CompilerParams(vmem_limit_bytes=56 * 1024 * 1024),
    )(anchors, own, *sels, *bufs, transform)


def local(spectra, pair_anchor, pair_offset, pair_partner, pair_count, window_bins, bin_gain):
    block_chans, local_wins, spec_width = spectra.shape
    pair_slots = pair_anchor.shape[0]
    fast_rows = (block_chans // 2 + 15) // 16 * 16
    spill_rows = block_chans - fast_rows

    blocks = lax.axis_size("chan")
    block = lax.axis_index("chan")
    table = jnp.concatenate([pair_offset, pair_partner, pair_count])
    tables = gather_blocks(table, "chan")
    table_before = tables[(block + blocks - 1) % blocks]
    table_after = tables[(block + 1) % blocks]

    def needs_of(tab):
        return block_needs(tab[:pair_slots], tab[pair_slots:2 * pair_slots], tab[2 * pair_slots], block_chans)

    own_minus, own_plus, own_pos_minus, own_pos_plus = needs_of(table)
    up_need, _, up_pos, _ = needs_of(table_after)
    _, down_need, _, down_pos = needs_of(table_before)
    all_needs = jax.vmap(needs_of)(tables)
    need_most = jnp.maximum(
        jnp.max(jnp.sum(all_needs[0], axis=1, dtype=jnp.int32)),
        jnp.max(jnp.sum(all_needs[1], axis=1, dtype=jnp.int32)),
    )

    def send_selector(need, pos, first, rows):
        return onehot(pos - first, rows, need).T.astype(jnp.bfloat16)

    def gather_rows(first, rows, source, whitened=False):
        up_rows = jnp.einsum("jc,cwf->wjf", send_selector(up_need, up_pos, first, rows), source,
                             preferred_element_type=jnp.bfloat16)
        down_rows = jnp.einsum("jc,cwf->wjf", send_selector(down_need, down_pos, first, rows), source,
                               preferred_element_type=jnp.bfloat16)
        if not whitened:
            up_rows, down_rows = whiten(up_rows), whiten(down_rows)
        return ring_exchange(up_rows, down_rows, "chan"), (up_rows, down_rows)

    chunks = 2 if local_wins % 2 == 0 else 1
    chunk_wins = local_wins // chunks
    fast_sent = [gather_rows(0, fast_rows, spectra[:, c * chunk_wins:(c + 1) * chunk_wins]) for c in range(chunks)]
    fast = [got for got, _ in fast_sent]
    spectra_late, _ = lax.optimization_barrier((spectra, [sent for _, sent in fast_sent]))
    white = whiten(spectra_late)
    spill = need_most > fast_rows

    transform = lag_table(spec_width // 2, LAG)
    lag_count = transform.shape[1]
    live_count = pair_count[0]
    slot_ids = lax.broadcasted_iota(jnp.int32, (pair_slots,), 0)
    live = slot_ids < live_count

    def pick(selector, rows):
        return jnp.einsum("sc,cwf->wsf", selector.astype(jnp.bfloat16), rows, preferred_element_type=jnp.bfloat16)

    anchors = pick(onehot(pair_anchor, block_chans, live), white)
    own = pick(onehot(pair_partner, block_chans, live & (pair_offset == 1)), white)
    own_hit = onehot(pair_partner, block_chans, live)
    before_row = jnp.sum(jnp.where(own_hit, own_pos_minus[None, :], 0), axis=1)
    after_row = jnp.sum(jnp.where(own_hit, own_pos_plus[None, :], 0), axis=1)
    use_before = live & (pair_offset == 0)
    use_after = live & (pair_offset == 2)
    sels = [
        onehot(before_row, fast_rows, use_before).astype(jnp.bfloat16),
        onehot(after_row, fast_rows, use_after).astype(jnp.bfloat16),
    ]
    corr_full = jnp.concatenate([
        halo_cross(c, chunk_wins, anchors, own, sels, [fast[c][0], fast[c][1]], transform)
        for c in range(chunks)
    ])

    def spill_extra(_):
        (got_before, got_after), _ = gather_rows(fast_rows, spill_rows, white, whitened=True)
        spill_sels = [
            onehot(before_row - fast_rows, spill_rows, use_before).astype(jnp.bfloat16),
            onehot(after_row - fast_rows, spill_rows, use_after).astype(jnp.bfloat16),
        ]
        zero_own = jnp.zeros_like(own)
        extra = jnp.concatenate([
            halo_cross(c, chunk_wins, anchors, zero_own, spill_sels,
                       [got_before[c * chunk_wins:(c + 1) * chunk_wins], got_after[c * chunk_wins:(c + 1) * chunk_wins]],
                       transform)
            for c in range(chunks)
        ])
        return extra

    def no_extra(_):
        return jnp.zeros((local_wins, pair_slots, lag_count), jnp.float32)

    spill_late, _ = lax.optimization_barrier((spill, fast[0]))
    corr_full = corr_full + lax.cond(spill_late, spill_extra, no_extra, 0)
    corr_all = lax.reduce_precision(corr_full, exponent_bits=8, mantissa_bits=7)
    running = jnp.sum(corr_full, axis=0)

    ref_sum = butterfly_sum(running, "win")
    norm_scale = jnp.sqrt(jnp.float32(local_wins * lax.axis_size("win")))
    ref_stack = jnp.where(live[:, None], ref_sum / norm_scale, 0.0)
    window_gain = window_gains(window_bins, bin_gain)
    numerator, denominator = window_weights_wm(corr_all, ref_sum, window_gain)
    if pair_slots % lag_count == 0:
        packed = jnp.concatenate([numerator, denominator.reshape(-1, lag_count)])
        packed = butterfly_sum(packed, "win")
        numerator, denominator = packed[:pair_slots], packed[pair_slots:].reshape(-1)
    else:
        numerator, denominator = butterfly_sum((numerator, denominator), "win")
    restack = jnp.where(live[:, None], norm_scale * numerator / denominator[:, None], 0.0)
    return (ref_stack, restack)


def solution(mesh):
    in_specs = (
        P(("days", "chan"), "win", None),
        P("chan"),
        P("chan"),
        P("chan"),
        P("chan"),
        P(("days", "win")),
        P(),
    )
    out_specs = (P(("days", "chan"), None), P(("days", "chan"), None))
    return jax.shard_map(local, mesh=mesh, in_specs=in_specs, out_specs=out_specs, check_vma=False)
```
